128 devices in a mesh: mgrp: 8 (over x, core), band: 16 (over y, z).
Axes of the slice: x: 4, y: 4, z: 4, core: 2. Of those that a mesh axis runs over, the one named last changes fastest.
Arguments:
- solution: float32 [2, 64, 8, 8192], P(None, None, 'mgrp', 'band'), may hold values from -6 to 6
- residual: float32 [2, 64, 8, 8192], P(None, None, 'mgrp', 'band'), may hold values from -16 to 16
- direction: float32 [2, 64, 8, 8192], P(None, None, 'mgrp', 'band'), may hold values from -16 to 16
- legendre: bfloat16 [8, 1024, 8192], P('mgrp', None, 'band'), may hold values from -0.0625 to 0.0625
- prior_inv: float32 [8192], P('band'), may hold values from 0.1 to 20, as said below
- noise_mats: bfloat16 [8, 64, 64], replicated, may hold values from -1 to 4, as said below
- noise_index: int32 [1024, 256], P(('band', 'mgrp')), may hold values from 0 to 7
- cycle_lengths: int32 [1024], P(('band', 'mgrp')), may hold values from 4096 to 16384, as said below
- m_values: int32 [8], replicated, may hold values from 0 to 8191, as said below
- cut_pattern: int32 [8, 16], P('mgrp'), may hold values from 0 to 1, as said below
Outputs:
- solution_new: float32 [2, 64, 8, 8192], P(None, None, 'mgrp', 'band')
- residual_new: float32 [2, 64, 8, 8192], P(None, None, 'mgrp', 'band')
- direction_new: float32 [2, 64, 8, 8192], P(None, None, 'mgrp', 'band')
The draws below stay inside these ranges and needn't reach their ends.
Inputs may be any that keep to these rules, and one draw needn't show every extreme that they name: `noise_mats`: symmetric; in every row the diagonal entry exceeds the sum of the magnitudes of the other entries. `prior_inv`: positive. `cycle_lengths`: every length is a multiple of 4; cycle 0 has exactly 16384 pixels. `m_values`: distinct values; 0 and 8191 are among them. `cut_pattern`: row m is 1 on cycle blocks c_m to 15 - c_m and 0 elsewhere, for some c_m from 0 to 5.
All inputs are finite; a program needn't handle non-finite values.
Results may differ from the reference program's by a relative error of at most 0.00095.
The reference program's roundings to bfloat16 on the way count: a program that leaves them out, or rounds other values in their place, can miss the bound.
Values may be sent and summed in bfloat16 or wider, within the bound.
No kernel may reach another device: no remote copies, remote signals or barrier semaphores. Data moves between devices by JAX's collectives and lax.ppermute only.
A program may use at most 192 MiB of HBM per device.

```python
import math
import jax
import jax.numpy as jnp
from jax import lax

L = 8192
RLEN = 16384
BLK = 64
RB = 64
NTYPES = 8
NMAPS = 64
M = 8
CYCLES = 1024


def ramped_field(key):
    field_shape = (2, NMAPS, M, L)
    base_draw = jax.random.truncated_normal(key, -4.0, 4.0, field_shape, jnp.float32)
    degree = jnp.arange(L, dtype=jnp.float32) / L
    position = jnp.arange(M, dtype=jnp.float32) / M
    return base_draw * (1.0 + degree)[None, None, None, :] * (1.0 + position)[None, None, :, None]


def draw_residual(key, part):
    return ramped_field(jax.random.fold_in(key, 1))


def draw_direction(key, part):
    return ramped_field(jax.random.fold_in(key, 2))


def draw_prior_inv(key, part):
    degree = jnp.arange(L, dtype=jnp.float32) / L
    own_key = jax.random.fold_in(key, 3)
    jitter = jax.random.uniform(own_key, (L,), jnp.float32, -0.5, 0.5)
    return 0.3 * (1.0 + 9.0 * degree) * jnp.exp(jitter)


def draw_noise_mats(key, part):
    first_key, second_key = jax.random.split(jax.random.fold_in(key, 4))
    raw_draw = jax.random.uniform(first_key, (NTYPES, BLK, BLK), jnp.float32, -1.0, 1.0)
    symmetric = 0.5 * (raw_draw + jnp.swapaxes(raw_draw, 1, 2))
    identity = jnp.eye(BLK, dtype=jnp.float32)
    off_scale = 1.0
    diagonal = jax.random.uniform(second_key, (NTYPES, BLK), jnp.float32, 1.2, 2.0)
    return (symmetric * (1.0 - identity)[None] * (off_scale / BLK) + identity[None] * diagonal[:, :, None]).astype(jnp.bfloat16)


def draw_cycle_lengths(key, part):
    lengths = 4 * jax.random.randint(jax.random.fold_in(key, 5), (CYCLES,), RLEN // 16, RLEN // 4 + 1)
    return jnp.where(jnp.arange(CYCLES) == 0, RLEN, lengths).astype(jnp.int32)


def draw_m_values(key, part):
    first_key, second_key = jax.random.split(jax.random.fold_in(key, 6))
    middle_values = 1 + jax.random.permutation(first_key, L - 2)[:M - 2]
    values = jnp.concatenate([jnp.array([0, L - 1], dtype=jnp.int32), middle_values.astype(jnp.int32)])
    return values[jax.random.permutation(second_key, M)].astype(jnp.int32)


def draw_cut_pattern(key, part):
    blocks = CYCLES // RB
    cut_counts = jax.random.randint(jax.random.fold_in(key, 8), (M, 1), 0, blocks // 3 + 1)
    position = jnp.arange(blocks, dtype=jnp.int32)[None, :]
    return ((position >= cut_counts) & (position < blocks - cut_counts)).astype(jnp.int32)


def with_ends(values, key, low, top_value):
    shape = values.shape
    index_at = [jax.random.randint(jax.random.fold_in(key, axis), (), 0, shape[axis]) for axis in range(len(shape))]
    values = values.at[tuple(index_at)].set(low)
    longest = shape.index(max(shape))
    index_at[longest] = (index_at[longest] + 1) % shape[longest]
    return values.at[tuple(index_at)].set(top_value)


def level_of(key, extent, pieces, least, top_value):
    gain = 1.0
    for dim, parts in pieces:
        steps = jax.random.uniform(jax.random.fold_in(jax.random.fold_in(key, 6), dim), (parts,), jnp.float32, least / len(pieces), top_value / len(pieces))
        gain = gain * jnp.repeat(jnp.exp(steps), extent[dim] // parts).reshape((-1,) + (1,) * (len(extent) - 1 - dim))
    return gain


def normal_values(key, shape, spread, reach, cuts=(), kind=jnp.bfloat16):
    level = level_of(key, shape, cuts, -0.22, 0.18) if cuts else 1.0
    values = jax.random.normal(key, shape, jnp.float32) * spread * level
    return jnp.minimum(jnp.maximum(values, -reach), reach).astype(kind)


def setup_inputs(seed: int = 0) -> dict:
    arg_keys = jax.random.split(jax.random.key(seed), 11)
    solution = normal_values(arg_keys[0], (2, NMAPS, M, L), 1.0, 6.0, ((2, 8), (3, 16)), jnp.float32)
    residual = draw_residual(jax.random.fold_in(arg_keys[10], 71), 0)
    direction = draw_direction(jax.random.fold_in(arg_keys[10], 71), 0)
    legendre = normal_values(arg_keys[3], (M, CYCLES, L), L ** -0.5, 0.0625, ((0, 8), (2, 16)))
    prior_inv = draw_prior_inv(jax.random.fold_in(arg_keys[10], 71), 0)
    noise_mats = draw_noise_mats(jax.random.fold_in(arg_keys[10], 71), 0)
    noise_index = with_ends(jax.random.randint(arg_keys[6], (CYCLES, RLEN // BLK), 0, NTYPES), jax.random.fold_in(arg_keys[6], 1), 0, NTYPES - 1).astype(jnp.int32)
    cycle_lengths = draw_cycle_lengths(jax.random.fold_in(arg_keys[10], 71), 0)
    m_values = draw_m_values(jax.random.fold_in(arg_keys[10], 71), 0)
    cut_pattern = draw_cut_pattern(jax.random.fold_in(arg_keys[10], 71), 0)
    return {"solution": solution, "residual": residual, "direction": direction, "legendre": legendre, "prior_inv": prior_inv, "noise_mats": noise_mats, "noise_index": noise_index, "cycle_lengths": cycle_lengths, "m_values": m_values, "cut_pattern": cut_pattern}


def cycle_tables(m_values, lengths, pixels):
    high_count = pixels // 128
    coarse = jnp.arange(high_count, dtype=jnp.int32) * 128
    fine = jnp.arange(128, dtype=jnp.int32)
    cycle_size = lengths[:, None, None].astype(jnp.float32)
    phase_high = (m_values[None, :, None] * coarse[None, None, :]) % lengths[:, None, None]
    phase_low = (m_values[None, :, None] * fine[None, None, :]) % lengths[:, None, None]
    angle_high = (2.0 * math.pi) * phase_high.astype(jnp.float32) / cycle_size
    angle_low = (2.0 * math.pi) * phase_low.astype(jnp.float32) / cycle_size
    cos_high = jnp.cos(angle_high)[:, :, :, None]
    sin_high = jnp.sin(angle_high)[:, :, :, None]
    cos_low = jnp.cos(angle_low)[:, :, None, :]
    sin_low = jnp.sin(angle_low)[:, :, None, :]
    cycle_count = lengths.shape[0]
    mode_count = m_values.shape[0]
    cos_full = (cos_high * cos_low - sin_high * sin_low).reshape(cycle_count, mode_count, pixels)
    sin_full = (sin_high * cos_low + cos_high * sin_low).reshape(cycle_count, mode_count, pixels)
    column = jnp.arange(pixels, dtype=jnp.int32)
    factor = jnp.where(m_values == 0, 1.0, 2.0).astype(jnp.float32)[None, :, None]
    inside = (column[None, None, :] < lengths[:, None, None]).astype(jnp.float32)
    cosine = factor * cos_full * inside
    sine_part = -factor * sin_full * inside
    return jnp.concatenate([cosine, sine_part], axis=1).astype(jnp.bfloat16)


def cycle_segment(coeffs, lengths, indices, m_values, noise_mats, weight):
    cycle_count, mode_count, columns = coeffs.shape
    map_count = columns // 2
    tables = cycle_tables(m_values, lengths, RLEN).astype(jnp.float32)
    stacked = coeffs.reshape(cycle_count, mode_count, 2, map_count).transpose(0, 2, 1, 3)
    stacked = stacked.reshape(cycle_count, 2 * mode_count, map_count).astype(jnp.float32)
    sky_map = jnp.einsum("rjb,rjk->rbk", stacked, tables).astype(jnp.bfloat16)
    block_count = RLEN // BLK
    matrices = noise_mats.reshape(NTYPES, BLK * BLK)[indices].reshape(cycle_count, block_count, BLK, BLK)
    blocked = sky_map.reshape(cycle_count, map_count, block_count, BLK).astype(jnp.float32)
    noisy_map = weight * jnp.einsum("rqij,rbqj->rbqi", matrices.astype(jnp.float32), blocked)
    noisy_map = noisy_map.reshape(cycle_count, map_count, RLEN).astype(jnp.bfloat16)
    backward = jnp.einsum("rbk,rjk->rjb", noisy_map.astype(jnp.float32), tables)
    backward = backward.reshape(cycle_count, 2, mode_count, map_count).transpose(0, 2, 1, 3)
    return backward.reshape(cycle_count, mode_count, columns).astype(jnp.bfloat16)


def reference(solution, residual, direction, legendre, prior_inv, noise_mats, noise_index, cycle_lengths, m_values, cut_pattern):
    columns = 2 * NMAPS
    weight = L / (CYCLES * RLEN)
    rounded = direction.astype(jnp.bfloat16).reshape(columns, M, L).transpose(1, 0, 2)
    keep_mask = jnp.repeat(cut_pattern, RB, axis=1)

    def synthesize(operands):
        return jnp.dot(operands[0], operands[1].T, preferred_element_type=jnp.float32)

    partials = lax.map(synthesize, (legendre, rounded))
    coeffs = (partials * keep_mask.astype(jnp.float32)[:, :, None]).astype(jnp.bfloat16)
    grouped = coeffs.transpose(1, 0, 2).reshape(CYCLES // 8, 8, M, columns)
    backward = lax.map(
        lambda operands: cycle_segment(operands[0], operands[1], operands[2], m_values, noise_mats, weight),
        (grouped, cycle_lengths.reshape(CYCLES // 8, 8), noise_index.reshape(CYCLES // 8, 8, RLEN // BLK)))
    returned = backward.reshape(CYCLES, M, columns).transpose(1, 0, 2)
    returned = returned * keep_mask.astype(jnp.bfloat16)[:, :, None]

    def analyze(operands):
        return jnp.dot(operands[0].T, operands[1], preferred_element_type=jnp.float32)

    image_data = lax.map(analyze, (returned, legendre))
    image_data = image_data.transpose(1, 0, 2).reshape(2, NMAPS, M, L)
    image_field = prior_inv[None, None, None, :] * direction + image_data
    norm_now = jnp.sum(residual * residual, axis=(0, 2, 3))
    curvature = jnp.sum(direction * image_field, axis=(0, 2, 3))
    step_size = (norm_now / curvature)[None, :, None, None]
    solution_new = solution + step_size * direction
    residual_new = residual - step_size * image_field
    norm_next = jnp.sum(residual_new * residual_new, axis=(0, 2, 3))
    direction_new = residual_new + (norm_next / norm_now)[None, :, None, None] * direction
    return (solution_new, residual_new, direction_new)
```

```python
import math

import jax
import jax.numpy as jnp
from jax import lax
from jax.sharding import PartitionSpec as P

L = 8192
RLEN = 16384
BLK = 64
RB = 64


MESH_AXES = ("mgrp", "band")


def total_over_mesh(values):
    count = lax.axis_size(MESH_AXES)
    copies = jnp.broadcast_to(values[None], (count,) + values.shape)
    return jnp.sum(lax.all_to_all(copies, MESH_AXES, 0, 0, tiled=True), axis=0)


def gather_cycles(partials, band_count):
    cycle_total, columns = partials.shape
    group_count = lax.axis_size("mgrp")
    own = cycle_total // (band_count * group_count)
    pieces = partials.reshape(band_count, group_count, own, columns).transpose(1, 0, 2, 3)
    pieces = pieces.reshape(group_count * band_count, own, columns)
    received = lax.all_to_all(pieces, MESH_AXES, 0, 0, tiled=True)
    received = received.reshape(group_count, band_count, own, columns)
    return jnp.sum(received, axis=1).transpose(1, 0, 2)


def spread_cycles(backward, band_count):
    own, group_count, columns = backward.shape
    pieces = jnp.broadcast_to(
        backward.transpose(1, 0, 2)[:, None], (group_count, band_count, own, columns)
    ).reshape(group_count * band_count, own, columns)
    received = lax.all_to_all(pieces, MESH_AXES, 0, 0, tiled=True)
    received = received.reshape(group_count, band_count, own, columns).transpose(1, 0, 2, 3)
    return received.reshape(band_count * group_count * own, columns)


def cycle_tables(m_values, lengths, pixels):
    high_count = pixels // 128
    coarse = jnp.arange(high_count, dtype=jnp.int32) * 128
    fine = jnp.arange(128, dtype=jnp.int32)
    cycle_size = lengths[:, None, None].astype(jnp.float32)
    phase_high = m_values[None, :, None] * coarse[None, None, :] % lengths[:, None, None]
    phase_low = m_values[None, :, None] * fine[None, None, :] % lengths[:, None, None]
    angle_high = 2.0 * math.pi * phase_high.astype(jnp.float32) / cycle_size
    angle_low = 2.0 * math.pi * phase_low.astype(jnp.float32) / cycle_size
    cos_high = jnp.cos(angle_high)[:, :, :, None]
    sin_high = jnp.sin(angle_high)[:, :, :, None]
    cos_low = jnp.cos(angle_low)[:, :, None, :]
    sin_low = jnp.sin(angle_low)[:, :, None, :]
    cycle_count = lengths.shape[0]
    mode_count = m_values.shape[0]
    cos_full = (cos_high * cos_low - sin_high * sin_low).reshape(cycle_count, mode_count, pixels)
    sin_full = (sin_high * cos_low + cos_high * sin_low).reshape(cycle_count, mode_count, pixels)
    column = jnp.arange(pixels, dtype=jnp.int32)
    factor = jnp.where(m_values == 0, 1.0, 2.0).astype(jnp.float32)[None, :, None]
    inside = (column[None, None, :] < lengths[:, None, None]).astype(jnp.float32)
    cosine = factor * cos_full * inside
    sine_part = -factor * sin_full * inside
    return jnp.stack([cosine, sine_part], axis=1).astype(jnp.bfloat16)


def pair_table(noise_mats):
    kinds = noise_mats.shape[0]
    first = jnp.broadcast_to(noise_mats[:, None], (kinds, kinds, BLK, BLK))
    second = jnp.broadcast_to(noise_mats[None, :], (kinds, kinds, BLK, BLK))
    empty = jnp.zeros((kinds, kinds, BLK, BLK), noise_mats.dtype)
    upper = jnp.concatenate([first, empty], axis=3)
    lower = jnp.concatenate([empty, second], axis=3)
    return jnp.concatenate([upper, lower], axis=2).reshape(kinds * kinds, 2 * BLK, 2 * BLK)


def cycle_segment(coeffs, lengths, indices, m_values, pairs, kinds, weight):
    cycle_count, mode_count, columns = coeffs.shape
    map_count = columns // 2
    tables = cycle_tables(m_values, lengths, RLEN)
    split_coeffs = coeffs.reshape(cycle_count, mode_count, 2, map_count)
    sky_map = jnp.einsum(
        "rmcb,rcmk->rbk", split_coeffs, tables, preferred_element_type=jnp.float32
    ).astype(jnp.bfloat16)
    pair_count = RLEN // (2 * BLK)
    kind_pairs = indices.reshape(cycle_count, pair_count, 2)
    pair_index = kind_pairs[:, :, 0] * kinds + kind_pairs[:, :, 1]
    matrices = pairs.reshape(kinds * kinds, 4 * BLK * BLK)[pair_index].reshape(
        cycle_count, pair_count, 2 * BLK, 2 * BLK
    )
    blocked = sky_map.reshape(cycle_count, map_count, pair_count, 2 * BLK)
    noisy_map = weight * jnp.einsum(
        "rbqj,rqij->rbqi", blocked, matrices, preferred_element_type=jnp.float32
    )
    noisy_map = noisy_map.reshape(cycle_count, map_count, RLEN).astype(jnp.bfloat16)
    backward = jnp.einsum("rbk,rcmk->rmcb", noisy_map, tables, preferred_element_type=jnp.float32)
    return backward.reshape(cycle_count, mode_count, columns).astype(jnp.bfloat16)


def shards(
    solution,
    residual,
    direction,
    legendre,
    prior_inv,
    noise_mats,
    noise_index,
    cycle_lengths,
    m_values,
    cut_pattern,
):
    band_count = lax.axis_size("band")
    mode_local, cycle_total, l_local = legendre.shape
    map_count = direction.shape[1]
    columns = 2 * map_count
    band_rows = cycle_total // band_count
    weight = L / (cycle_total * RLEN)
    rounded = direction.astype(jnp.bfloat16).reshape(columns, mode_local, l_local)

    def row_mask(first_row, row_count):
        block_flags = lax.dynamic_slice_in_dim(cut_pattern, first_row // RB, row_count // RB, 1)
        return jnp.repeat(block_flags, RB, axis=1).T

    section = legendre
    products = jnp.einsum("mrl,nml->rmn", section, rounded, preferred_element_type=jnp.float32)
    masked_products = products * row_mask(jnp.int32(0), cycle_total).astype(jnp.float32)[:, :, None]
    coeffs = gather_cycles(masked_products.reshape(cycle_total, columns), band_count).astype(jnp.bfloat16)
    cycle_local = coeffs.shape[0]
    mode_total = coeffs.shape[1]
    kinds = noise_mats.shape[0]
    pairs = pair_table(noise_mats)
    outputs = lax.map(
        lambda operands: cycle_segment(
            operands[0], operands[1], operands[2], m_values, pairs, kinds, weight
        ),
        (
            coeffs.reshape(cycle_local // 8, 8, mode_total, columns),
            cycle_lengths.reshape(cycle_local // 8, 8),
            noise_index.reshape(cycle_local // 8, 8, RLEN // BLK),
        ),
    )
    backward = outputs.reshape(cycle_local, mode_total, columns)
    returned = spread_cycles(backward, band_count)
    masked = returned * row_mask(jnp.int32(0), cycle_total).astype(jnp.bfloat16)
    image_data = jnp.einsum(
        "mrl,rn->nml", legendre, masked, preferred_element_type=jnp.float32
    )
    image_data = image_data.reshape(2, map_count, mode_local, l_local)
    image_field = prior_inv[None, None, None, :] * direction + image_data
    norm_now, curvature = total_over_mesh(
        jnp.stack(
            [
                jnp.sum(residual * residual, axis=(0, 2, 3)),
                jnp.sum(direction * image_field, axis=(0, 2, 3)),
            ]
        )
    )
    step_size = norm_now / curvature
    new_residual = residual - step_size[None, :, None, None] * image_field
    norm_next = total_over_mesh(jnp.sum(new_residual * new_residual, axis=(0, 2, 3)))
    growth = norm_next / norm_now
    new_solution = solution + step_size[None, :, None, None] * direction
    new_direction = new_residual + growth[None, :, None, None] * direction
    return (new_solution, new_residual, new_direction)


def solution(mesh):
    in_specs = (
        P(None, None, "mgrp", "band"),
        P(None, None, "mgrp", "band"),
        P(None, None, "mgrp", "band"),
        P("mgrp", None, "band"),
        P("band"),
        P(),
        P(("band", "mgrp"), None),
        P(("band", "mgrp")),
        P(),
        P("mgrp", None),
    )
    out_specs = (
        P(None, None, "mgrp", "band"),
        P(None, None, "mgrp", "band"),
        P(None, None, "mgrp", "band"),
    )
    return jax.shard_map(shards, mesh=mesh, in_specs=in_specs, out_specs=out_specs, check_vma=False)
```

```python
import functools
import math

import jax
import jax.numpy as jnp
from jax import lax
from jax.experimental import pallas as pl
from jax.experimental.pallas import tpu as pltpu
from jax.sharding import PartitionSpec as P

L = 8192
RLEN = 16384
BLK = 64
RB = 64


MESH_AXES = ("mgrp", "band")


def total_over_mesh(values):
    count = lax.axis_size(MESH_AXES)
    copies = jnp.broadcast_to(values[None], (count,) + values.shape)
    return jnp.sum(lax.all_to_all(copies, MESH_AXES, 0, 0, tiled=True), axis=0)


def gather_cycles(partials, band_count):
    cycle_total, columns = partials.shape
    group_count = lax.axis_size("mgrp")
    own = cycle_total // (band_count * group_count)
    pieces = partials.reshape(band_count, group_count, own, columns).transpose(1, 0, 2, 3)
    pieces = pieces.reshape(group_count * band_count, own, columns)
    received = lax.all_to_all(pieces, MESH_AXES, 0, 0, tiled=True)
    received = received.reshape(group_count, band_count, own, columns)
    return jnp.sum(received, axis=1).transpose(1, 0, 2)


def spread_cycles(backward, band_count):
    own, group_count, columns = backward.shape
    pieces = jnp.broadcast_to(
        backward.transpose(1, 0, 2)[:, None], (group_count, band_count, own, columns)
    ).reshape(group_count * band_count, own, columns)
    received = lax.all_to_all(pieces, MESH_AXES, 0, 0, tiled=True)
    received = received.reshape(group_count, band_count, own, columns).transpose(1, 0, 2, 3)
    return received.reshape(band_count * group_count * own, columns)


def cycle_tables(m_values, lengths, pixels):
    high_count = pixels // 128
    coarse = jnp.arange(high_count, dtype=jnp.int32) * 128
    fine = jnp.arange(128, dtype=jnp.int32)
    cycle_size = lengths[:, None, None].astype(jnp.float32)
    phase_high = m_values[None, :, None] * coarse[None, None, :] % lengths[:, None, None]
    phase_low = m_values[None, :, None] * fine[None, None, :] % lengths[:, None, None]
    angle_high = 2.0 * math.pi * phase_high.astype(jnp.float32) / cycle_size
    angle_low = 2.0 * math.pi * phase_low.astype(jnp.float32) / cycle_size
    cos_high = jnp.cos(angle_high)[:, :, :, None]
    sin_high = jnp.sin(angle_high)[:, :, :, None]
    cos_low = jnp.cos(angle_low)[:, :, None, :]
    sin_low = jnp.sin(angle_low)[:, :, None, :]
    cycle_count = lengths.shape[0]
    mode_count = m_values.shape[0]
    cos_full = (cos_high * cos_low - sin_high * sin_low).reshape(cycle_count, mode_count, pixels)
    sin_full = (sin_high * cos_low + cos_high * sin_low).reshape(cycle_count, mode_count, pixels)
    column = jnp.arange(pixels, dtype=jnp.int32)
    factor = jnp.where(m_values == 0, 1.0, 2.0).astype(jnp.float32)[None, :, None]
    inside = (column[None, None, :] < lengths[:, None, None]).astype(jnp.float32)
    cosine = factor * cos_full * inside
    sine_part = -factor * sin_full * inside
    return jnp.stack([cosine, sine_part], axis=1).astype(jnp.bfloat16)


def pair_table(noise_mats):
    kinds = noise_mats.shape[0]
    first = jnp.broadcast_to(noise_mats[:, None], (kinds, kinds, BLK, BLK))
    second = jnp.broadcast_to(noise_mats[None, :], (kinds, kinds, BLK, BLK))
    empty = jnp.zeros((kinds, kinds, BLK, BLK), noise_mats.dtype)
    upper = jnp.concatenate([first, empty], axis=3)
    lower = jnp.concatenate([empty, second], axis=3)
    return jnp.concatenate([upper, lower], axis=2).reshape(kinds * kinds, 2 * BLK, 2 * BLK)


def cycle_segment(coeffs, lengths, indices, m_values, pairs, kinds, weight):
    cycle_count, mode_count, columns = coeffs.shape
    map_count = columns // 2
    tables = cycle_tables(m_values, lengths, RLEN)
    split_coeffs = coeffs.reshape(cycle_count, mode_count, 2, map_count)
    sky_map = jnp.einsum(
        "rmcb,rcmk->rbk", split_coeffs, tables, preferred_element_type=jnp.float32
    ).astype(jnp.bfloat16)
    pair_count = RLEN // (2 * BLK)
    kind_pairs = indices.reshape(cycle_count, pair_count, 2)
    pair_index = kind_pairs[:, :, 0] * kinds + kind_pairs[:, :, 1]
    matrices = pairs.reshape(kinds * kinds, 4 * BLK * BLK)[pair_index].reshape(
        cycle_count, pair_count, 2 * BLK, 2 * BLK
    )
    blocked = sky_map.reshape(cycle_count, map_count, pair_count, 2 * BLK)
    noisy_map = weight * jnp.einsum(
        "rbqj,rqij->rbqi", blocked, matrices, preferred_element_type=jnp.float32
    )
    noisy_map = noisy_map.reshape(cycle_count, map_count, RLEN).astype(jnp.bfloat16)
    backward = jnp.einsum("rbk,rcmk->rmcb", noisy_map, tables, preferred_element_type=jnp.float32)
    return backward.reshape(cycle_count, mode_count, columns).astype(jnp.bfloat16)


def noise_kernel(index_ref, coeff_ref, table_ref, pair_ref, back_ref, noisy_ref, *, weight):
    cycle = pl.program_id(0)
    span = 1024
    pair_width = 2 * BLK
    coeff = coeff_ref[0]

    def chunk(step, carry):
        start = pl.multiple_of(step * span, span)
        sky = jnp.dot(
            coeff, table_ref[0, :, pl.ds(start, span)], preferred_element_type=jnp.float32
        ).astype(jnp.bfloat16)
        for inner in range(span // pair_width):
            block = (start + inner * pair_width) // BLK
            kinds = pair_ref.shape[0]
            side = int(round(kinds ** 0.5))
            pick = index_ref[cycle, block] * side + index_ref[cycle, block + 1]
            noisy = jnp.dot(
                sky[:, inner * pair_width:(inner + 1) * pair_width],
                pair_ref[pick],
                preferred_element_type=jnp.float32,
            )
            noisy_ref[:, pl.ds(start + inner * pair_width, pair_width)] = (
                weight * noisy
            ).astype(jnp.bfloat16)
        return carry

    lax.fori_loop(0, table_ref.shape[2] // span, chunk, 0)
    back_ref[0] = lax.dot_general(
        noisy_ref[...],
        table_ref[0],
        (((1,), (1,)), ((), ())),
        preferred_element_type=jnp.float32,
    ).astype(back_ref.dtype)


def cycle_transform(coeffs, lengths, indices, m_values, noise_mats, weight):
    cycle_count, mode_count, columns = coeffs.shape
    map_count = columns // 2
    kinds = noise_mats.shape[0]
    tables = cycle_tables(m_values, lengths, RLEN).reshape(cycle_count, 2 * mode_count, RLEN)
    coeff_t = (
        coeffs.reshape(cycle_count, mode_count, 2, map_count)
        .transpose(0, 3, 2, 1)
        .reshape(cycle_count, map_count, 2 * mode_count)
    )
    pairs_t = jnp.swapaxes(pair_table(noise_mats), 1, 2)
    grid_spec = pltpu.PrefetchScalarGridSpec(
        num_scalar_prefetch=1,
        grid=(cycle_count,),
        in_specs=[
            pl.BlockSpec((1, map_count, 2 * mode_count), lambda r, idx: (r, 0, 0)),
            pl.BlockSpec((1, 2 * mode_count, RLEN), lambda r, idx: (r, 0, 0)),
            pl.BlockSpec(pairs_t.shape, lambda r, idx: (0, 0, 0)),
        ],
        out_specs=pl.BlockSpec((1, map_count, 2 * mode_count), lambda r, idx: (r, 0, 0)),
        scratch_shapes=[pltpu.VMEM((map_count, RLEN), jnp.bfloat16)],
    )
    back = pl.pallas_call(
        functools.partial(noise_kernel, weight=weight),
        grid_spec=grid_spec,
        out_shape=jax.ShapeDtypeStruct((cycle_count, map_count, 2 * mode_count), jnp.bfloat16),
    )(indices, coeff_t, tables, pairs_t)
    return (
        back.reshape(cycle_count, map_count, 2, mode_count)
        .transpose(0, 3, 2, 1)
        .reshape(cycle_count, mode_count, columns)
    )


def shards(
    solution,
    residual,
    direction,
    legendre,
    prior_inv,
    noise_mats,
    noise_index,
    cycle_lengths,
    m_values,
    cut_pattern,
):
    band_count = lax.axis_size("band")
    mode_local, cycle_total, l_local = legendre.shape
    map_count = direction.shape[1]
    columns = 2 * map_count
    band_rows = cycle_total // band_count
    weight = L / (cycle_total * RLEN)
    rounded = direction.astype(jnp.bfloat16).reshape(columns, mode_local, l_local)

    def row_mask(first_row, row_count):
        block_flags = lax.dynamic_slice_in_dim(cut_pattern, first_row // RB, row_count // RB, 1)
        return jnp.repeat(block_flags, RB, axis=1).T

    section = legendre
    products = jnp.einsum("mrl,nml->rmn", section, rounded, preferred_element_type=jnp.float32)
    masked_products = products * row_mask(jnp.int32(0), cycle_total).astype(jnp.float32)[:, :, None]
    coeffs = gather_cycles(masked_products.reshape(cycle_total, columns), band_count).astype(jnp.bfloat16)
    cycle_local = coeffs.shape[0]
    mode_total = coeffs.shape[1]
    outputs = cycle_transform(coeffs, cycle_lengths, noise_index, m_values, noise_mats, weight)
    backward = outputs.reshape(cycle_local, mode_total, columns)
    returned = spread_cycles(backward, band_count)
    masked = returned * row_mask(jnp.int32(0), cycle_total).astype(jnp.bfloat16)
    image_data = jnp.einsum(
        "mrl,rn->nml", legendre, masked, preferred_element_type=jnp.float32
    )
    image_data = image_data.reshape(2, map_count, mode_local, l_local)
    image_field = prior_inv[None, None, None, :] * direction + image_data
    norm_now, curvature = total_over_mesh(
        jnp.stack(
            [
                jnp.sum(residual * residual, axis=(0, 2, 3)),
                jnp.sum(direction * image_field, axis=(0, 2, 3)),
            ]
        )
    )
    step_size = norm_now / curvature
    new_residual = residual - step_size[None, :, None, None] * image_field
    norm_next = total_over_mesh(jnp.sum(new_residual * new_residual, axis=(0, 2, 3)))
    growth = norm_next / norm_now
    new_solution = solution + step_size[None, :, None, None] * direction
    new_direction = new_residual + growth[None, :, None, None] * direction
    return (new_solution, new_residual, new_direction)


def solution(mesh):
    in_specs = (
        P(None, None, "mgrp", "band"),
        P(None, None, "mgrp", "band"),
        P(None, None, "mgrp", "band"),
        P("mgrp", None, "band"),
        P("band"),
        P(),
        P(("band", "mgrp"), None),
        P(("band", "mgrp")),
        P(),
        P("mgrp", None),
    )
    out_specs = (
        P(None, None, "mgrp", "band"),
        P(None, None, "mgrp", "band"),
        P(None, None, "mgrp", "band"),
    )
    return jax.shard_map(shards, mesh=mesh, in_specs=in_specs, out_specs=out_specs, check_vma=False)
```

```python
import functools
import math

import jax
import jax.numpy as jnp
from jax import lax
from jax.experimental import pallas as pl
from jax.experimental.pallas import tpu as pltpu
from jax.sharding import PartitionSpec as P

L = 8192
RLEN = 16384
BLK = 64
RB = 64


MESH_AXES = ("mgrp", "band")


def total_over_mesh(values):
    count = lax.axis_size(MESH_AXES)
    copies = jnp.broadcast_to(values[None], (count,) + values.shape)
    return jnp.sum(lax.all_to_all(copies, MESH_AXES, 0, 0, tiled=True), axis=0)


def gather_cycles(partials, band_count):
    cycle_total, columns = partials.shape
    group_count = lax.axis_size("mgrp")
    own = cycle_total // (band_count * group_count)
    pieces = partials.reshape(band_count, group_count, own, columns).transpose(1, 0, 2, 3)
    pieces = pieces.reshape(group_count * band_count, own, columns)
    received = lax.all_to_all(pieces, MESH_AXES, 0, 0, tiled=True)
    received = received.reshape(group_count, band_count, own, columns)
    return jnp.sum(received, axis=1).transpose(1, 0, 2)


def spread_cycles(backward, band_count):
    own, group_count, columns = backward.shape
    pieces = jnp.broadcast_to(
        backward.transpose(1, 0, 2)[:, None], (group_count, band_count, own, columns)
    ).reshape(group_count * band_count, own, columns)
    received = lax.all_to_all(pieces, MESH_AXES, 0, 0, tiled=True)
    received = received.reshape(group_count, band_count, own, columns).transpose(1, 0, 2, 3)
    return received.reshape(band_count * group_count * own, columns)


def cycle_tables(m_values, lengths, pixels):
    high_count = pixels // 128
    coarse = jnp.arange(high_count, dtype=jnp.int32) * 128
    fine = jnp.arange(128, dtype=jnp.int32)
    cycle_size = lengths[:, None, None].astype(jnp.float32)
    phase_high = m_values[None, :, None] * coarse[None, None, :] % lengths[:, None, None]
    phase_low = m_values[None, :, None] * fine[None, None, :] % lengths[:, None, None]
    angle_high = 2.0 * math.pi * phase_high.astype(jnp.float32) / cycle_size
    angle_low = 2.0 * math.pi * phase_low.astype(jnp.float32) / cycle_size
    cos_high = jnp.cos(angle_high)[:, :, :, None]
    sin_high = jnp.sin(angle_high)[:, :, :, None]
    cos_low = jnp.cos(angle_low)[:, :, None, :]
    sin_low = jnp.sin(angle_low)[:, :, None, :]
    cycle_count = lengths.shape[0]
    mode_count = m_values.shape[0]
    cos_full = (cos_high * cos_low - sin_high * sin_low).reshape(cycle_count, mode_count, pixels)
    sin_full = (sin_high * cos_low + cos_high * sin_low).reshape(cycle_count, mode_count, pixels)
    column = jnp.arange(pixels, dtype=jnp.int32)
    factor = jnp.where(m_values == 0, 1.0, 2.0).astype(jnp.float32)[None, :, None]
    inside = (column[None, None, :] < lengths[:, None, None]).astype(jnp.float32)
    cosine = factor * cos_full * inside
    sine_part = -factor * sin_full * inside
    return jnp.stack([cosine, sine_part], axis=1).astype(jnp.bfloat16)


def pair_table(noise_mats):
    kinds = noise_mats.shape[0]
    first = jnp.broadcast_to(noise_mats[:, None], (kinds, kinds, BLK, BLK))
    second = jnp.broadcast_to(noise_mats[None, :], (kinds, kinds, BLK, BLK))
    empty = jnp.zeros((kinds, kinds, BLK, BLK), noise_mats.dtype)
    upper = jnp.concatenate([first, empty], axis=3)
    lower = jnp.concatenate([empty, second], axis=3)
    return jnp.concatenate([upper, lower], axis=2).reshape(kinds * kinds, 2 * BLK, 2 * BLK)


def cycle_segment(coeffs, lengths, indices, m_values, pairs, kinds, weight):
    cycle_count, mode_count, columns = coeffs.shape
    map_count = columns // 2
    tables = cycle_tables(m_values, lengths, RLEN)
    split_coeffs = coeffs.reshape(cycle_count, mode_count, 2, map_count)
    sky_map = jnp.einsum(
        "rmcb,rcmk->rbk", split_coeffs, tables, preferred_element_type=jnp.float32
    ).astype(jnp.bfloat16)
    pair_count = RLEN // (2 * BLK)
    kind_pairs = indices.reshape(cycle_count, pair_count, 2)
    pair_index = kind_pairs[:, :, 0] * kinds + kind_pairs[:, :, 1]
    matrices = pairs.reshape(kinds * kinds, 4 * BLK * BLK)[pair_index].reshape(
        cycle_count, pair_count, 2 * BLK, 2 * BLK
    )
    blocked = sky_map.reshape(cycle_count, map_count, pair_count, 2 * BLK)
    noisy_map = weight * jnp.einsum(
        "rbqj,rqij->rbqi", blocked, matrices, preferred_element_type=jnp.float32
    )
    noisy_map = noisy_map.reshape(cycle_count, map_count, RLEN).astype(jnp.bfloat16)
    backward = jnp.einsum("rbk,rcmk->rmcb", noisy_map, tables, preferred_element_type=jnp.float32)
    return backward.reshape(cycle_count, mode_count, columns).astype(jnp.bfloat16)


def noise_kernel(index_ref, coeff_ref, table_ref, pair_ref, back_ref, noisy_ref):
    cycle = pl.program_id(0)
    span = 1024
    pair_width = 2 * BLK
    coeff = coeff_ref[0]

    def chunk(step, carry):
        start = pl.multiple_of(step * span, span)
        sky = jnp.dot(
            coeff, table_ref[0, :, pl.ds(start, span)], preferred_element_type=jnp.float32
        ).astype(jnp.bfloat16)
        for inner in range(span // pair_width):
            block = (start + inner * pair_width) // BLK
            kinds = pair_ref.shape[0]
            side = int(round(kinds ** 0.5))
            pick = index_ref[cycle, block] * side + index_ref[cycle, block + 1]
            noisy = jnp.dot(
                sky[:, inner * pair_width:(inner + 1) * pair_width],
                pair_ref[pick],
                preferred_element_type=jnp.float32,
            )
            noisy_ref[:, pl.ds(start + inner * pair_width, pair_width)] = noisy.astype(
                jnp.bfloat16
            )
        return carry

    lax.fori_loop(0, table_ref.shape[2] // span, chunk, 0)
    back_ref[0] = lax.dot_general(
        noisy_ref[...],
        table_ref[0],
        (((1,), (1,)), ((), ())),
        preferred_element_type=jnp.float32,
    ).astype(back_ref.dtype)


def cycle_transform(coeffs, lengths, indices, m_values, noise_mats, weight):
    cycle_count, mode_count, columns = coeffs.shape
    map_count = columns // 2
    kinds = noise_mats.shape[0]
    tables = cycle_tables(m_values, lengths, RLEN).reshape(cycle_count, 2 * mode_count, RLEN)
    coeff_t = (
        coeffs.reshape(cycle_count, mode_count, 2, map_count)
        .transpose(0, 3, 2, 1)
        .reshape(cycle_count, map_count, 2 * mode_count)
    )
    pairs_t = jnp.swapaxes(pair_table(noise_mats), 1, 2) * jnp.asarray(weight, jnp.bfloat16)
    grid_spec = pltpu.PrefetchScalarGridSpec(
        num_scalar_prefetch=1,
        grid=(cycle_count,),
        in_specs=[
            pl.BlockSpec((1, map_count, 2 * mode_count), lambda r, idx: (r, 0, 0)),
            pl.BlockSpec((1, 2 * mode_count, RLEN), lambda r, idx: (r, 0, 0)),
            pl.BlockSpec(pairs_t.shape, lambda r, idx: (0, 0, 0)),
        ],
        out_specs=pl.BlockSpec((1, map_count, 2 * mode_count), lambda r, idx: (r, 0, 0)),
        scratch_shapes=[pltpu.VMEM((map_count, RLEN), jnp.bfloat16)],
    )
    back = pl.pallas_call(
        noise_kernel,
        grid_spec=grid_spec,
        out_shape=jax.ShapeDtypeStruct((cycle_count, map_count, 2 * mode_count), jnp.bfloat16),
    )(indices, coeff_t, tables, pairs_t)
    return (
        back.reshape(cycle_count, map_count, 2, mode_count)
        .transpose(0, 3, 2, 1)
        .reshape(cycle_count, mode_count, columns)
    )


def shards(
    solution,
    residual,
    direction,
    legendre,
    prior_inv,
    noise_mats,
    noise_index,
    cycle_lengths,
    m_values,
    cut_pattern,
):
    band_count = lax.axis_size("band")
    mode_local, cycle_total, l_local = legendre.shape
    map_count = direction.shape[1]
    columns = 2 * map_count
    band_rows = cycle_total // band_count
    weight = L / (cycle_total * RLEN)
    rounded = direction.astype(jnp.bfloat16).reshape(columns, mode_local, l_local)

    def row_mask(first_row, row_count):
        block_flags = lax.dynamic_slice_in_dim(cut_pattern, first_row // RB, row_count // RB, 1)
        return jnp.repeat(block_flags, RB, axis=1).T

    section = legendre
    products = jnp.einsum("mrl,nml->rmn", section, rounded, preferred_element_type=jnp.float32)
    masked_products = products * row_mask(jnp.int32(0), cycle_total).astype(jnp.float32)[:, :, None]
    coeffs = gather_cycles(masked_products.reshape(cycle_total, columns), band_count).astype(jnp.bfloat16)
    cycle_local = coeffs.shape[0]
    mode_total = coeffs.shape[1]
    outputs = cycle_transform(coeffs, cycle_lengths, noise_index, m_values, noise_mats, weight)
    backward = outputs.reshape(cycle_local, mode_total, columns)
    returned = spread_cycles(backward, band_count)
    masked = returned * row_mask(jnp.int32(0), cycle_total).astype(jnp.bfloat16)
    image_data = jnp.einsum(
        "mrl,rn->nml", legendre, masked, preferred_element_type=jnp.float32
    )
    image_data = image_data.reshape(2, map_count, mode_local, l_local)
    image_field = prior_inv[None, None, None, :] * direction + image_data
    norm_now, curvature, cross, image_norm = total_over_mesh(
        jnp.stack(
            [
                jnp.sum(residual * residual, axis=(0, 2, 3)),
                jnp.sum(direction * image_field, axis=(0, 2, 3)),
                jnp.sum(residual * image_field, axis=(0, 2, 3)),
                jnp.sum(image_field * image_field, axis=(0, 2, 3)),
            ]
        )
    )
    step_size = norm_now / curvature
    new_residual = residual - step_size[None, :, None, None] * image_field
    norm_next = norm_now - 2.0 * step_size * cross + step_size * step_size * image_norm
    growth = norm_next / norm_now
    new_solution = solution + step_size[None, :, None, None] * direction
    new_direction = new_residual + growth[None, :, None, None] * direction
    return (new_solution, new_residual, new_direction)


def solution(mesh):
    in_specs = (
        P(None, None, "mgrp", "band"),
        P(None, None, "mgrp", "band"),
        P(None, None, "mgrp", "band"),
        P("mgrp", None, "band"),
        P("band"),
        P(),
        P(("band", "mgrp"), None),
        P(("band", "mgrp")),
        P(),
        P("mgrp", None),
    )
    out_specs = (
        P(None, None, "mgrp", "band"),
        P(None, None, "mgrp", "band"),
        P(None, None, "mgrp", "band"),
    )
    return jax.shard_map(shards, mesh=mesh, in_specs=in_specs, out_specs=out_specs, check_vma=False)
```

```python
import functools
import math

import jax
import jax.numpy as jnp
from jax import lax
from jax.experimental import pallas as pl
from jax.experimental.pallas import tpu as pltpu
from jax.sharding import PartitionSpec as P

L = 8192
RLEN = 16384
BLK = 64
RB = 64


MESH_AXES = ("mgrp", "band")


def total_over_mesh(values):
    count = lax.axis_size(MESH_AXES)
    copies = jnp.broadcast_to(values[None], (count,) + values.shape)
    return jnp.sum(lax.all_to_all(copies, MESH_AXES, 0, 0, tiled=True), axis=0)


def gather_cycles(partials, band_count):
    cycle_total, columns = partials.shape
    group_count = lax.axis_size("mgrp")
    own = cycle_total // (band_count * group_count)
    pieces = partials.reshape(band_count, group_count, own, columns).transpose(1, 0, 2, 3)
    pieces = pieces.reshape(group_count * band_count, own, columns)
    received = lax.all_to_all(pieces, MESH_AXES, 0, 0, tiled=True)
    received = received.reshape(group_count, band_count, own, columns)
    return jnp.sum(received, axis=1).transpose(1, 0, 2)


def spread_cycles(backward, band_count):
    own, group_count, columns = backward.shape
    pieces = jnp.broadcast_to(
        backward.transpose(1, 0, 2)[:, None], (group_count, band_count, own, columns)
    ).reshape(group_count * band_count, own, columns)
    received = lax.all_to_all(pieces, MESH_AXES, 0, 0, tiled=True)
    received = received.reshape(group_count, band_count, own, columns).transpose(1, 0, 2, 3)
    return received.reshape(band_count * group_count * own, columns)


def cycle_tables(m_values, lengths, pixels):
    high_count = pixels // 128
    coarse = jnp.arange(high_count, dtype=jnp.int32) * 128
    fine = jnp.arange(128, dtype=jnp.int32)
    cycle_size = lengths[:, None, None].astype(jnp.float32)
    phase_high = m_values[None, :, None] * coarse[None, None, :] % lengths[:, None, None]
    phase_low = m_values[None, :, None] * fine[None, None, :] % lengths[:, None, None]
    angle_high = 2.0 * math.pi * phase_high.astype(jnp.float32) / cycle_size
    angle_low = 2.0 * math.pi * phase_low.astype(jnp.float32) / cycle_size
    cos_high = jnp.cos(angle_high)[:, :, :, None]
    sin_high = jnp.sin(angle_high)[:, :, :, None]
    cos_low = jnp.cos(angle_low)[:, :, None, :]
    sin_low = jnp.sin(angle_low)[:, :, None, :]
    cycle_count = lengths.shape[0]
    mode_count = m_values.shape[0]
    cos_full = (cos_high * cos_low - sin_high * sin_low).reshape(cycle_count, mode_count, pixels)
    sin_full = (sin_high * cos_low + cos_high * sin_low).reshape(cycle_count, mode_count, pixels)
    column = jnp.arange(pixels, dtype=jnp.int32)
    factor = jnp.where(m_values == 0, 1.0, 2.0).astype(jnp.float32)[None, :, None]
    inside = (column[None, None, :] < lengths[:, None, None]).astype(jnp.float32)
    cosine = factor * cos_full * inside
    sine_part = -factor * sin_full * inside
    return jnp.stack([cosine, sine_part], axis=1).astype(jnp.bfloat16)


def pair_table(noise_mats):
    kinds = noise_mats.shape[0]
    first = jnp.broadcast_to(noise_mats[:, None], (kinds, kinds, BLK, BLK))
    second = jnp.broadcast_to(noise_mats[None, :], (kinds, kinds, BLK, BLK))
    empty = jnp.zeros((kinds, kinds, BLK, BLK), noise_mats.dtype)
    upper = jnp.concatenate([first, empty], axis=3)
    lower = jnp.concatenate([empty, second], axis=3)
    return jnp.concatenate([upper, lower], axis=2).reshape(kinds * kinds, 2 * BLK, 2 * BLK)


def cycle_segment(coeffs, lengths, indices, m_values, pairs, kinds, weight):
    cycle_count, mode_count, columns = coeffs.shape
    map_count = columns // 2
    tables = cycle_tables(m_values, lengths, RLEN)
    split_coeffs = coeffs.reshape(cycle_count, mode_count, 2, map_count)
    sky_map = jnp.einsum(
        "rmcb,rcmk->rbk", split_coeffs, tables, preferred_element_type=jnp.float32
    ).astype(jnp.bfloat16)
    pair_count = RLEN // (2 * BLK)
    kind_pairs = indices.reshape(cycle_count, pair_count, 2)
    pair_index = kind_pairs[:, :, 0] * kinds + kind_pairs[:, :, 1]
    matrices = pairs.reshape(kinds * kinds, 4 * BLK * BLK)[pair_index].reshape(
        cycle_count, pair_count, 2 * BLK, 2 * BLK
    )
    blocked = sky_map.reshape(cycle_count, map_count, pair_count, 2 * BLK)
    noisy_map = weight * jnp.einsum(
        "rbqj,rqij->rbqi", blocked, matrices, preferred_element_type=jnp.float32
    )
    noisy_map = noisy_map.reshape(cycle_count, map_count, RLEN).astype(jnp.bfloat16)
    backward = jnp.einsum("rbk,rcmk->rmcb", noisy_map, tables, preferred_element_type=jnp.float32)
    return backward.reshape(cycle_count, mode_count, columns).astype(jnp.bfloat16)


def noise_kernel(index_ref, coeff_ref, table_ref, pair_ref, back_ref, noisy_ref):
    cycle = pl.program_id(0)
    span = 4096
    pair_width = 2 * BLK
    coeff = coeff_ref[0]

    def chunk(step, carry):
        start = pl.multiple_of(step * span, span)
        sky = jnp.dot(
            coeff, table_ref[0, :, pl.ds(start, span)], preferred_element_type=jnp.float32
        ).astype(jnp.bfloat16)
        for inner in range(span // pair_width):
            block = (start + inner * pair_width) // BLK
            kinds = pair_ref.shape[0]
            side = int(round(kinds ** 0.5))
            pick = index_ref[cycle, block] * side + index_ref[cycle, block + 1]
            noisy = jnp.dot(
                sky[:, inner * pair_width:(inner + 1) * pair_width],
                pair_ref[pick],
                preferred_element_type=jnp.float32,
            )
            noisy_ref[:, pl.ds(start + inner * pair_width, pair_width)] = noisy.astype(
                jnp.bfloat16
            )
        return carry

    lax.fori_loop(0, table_ref.shape[2] // span, chunk, 0)
    back_ref[0] = lax.dot_general(
        noisy_ref[...],
        table_ref[0],
        (((1,), (1,)), ((), ())),
        preferred_element_type=jnp.float32,
    ).astype(back_ref.dtype)


def cycle_transform(coeffs, lengths, indices, m_values, noise_mats, weight):
    cycle_count, mode_count, columns = coeffs.shape
    map_count = columns // 2
    kinds = noise_mats.shape[0]
    tables = cycle_tables(m_values, lengths, RLEN).reshape(cycle_count, 2 * mode_count, RLEN)
    coeff_t = (
        coeffs.reshape(cycle_count, mode_count, 2, map_count)
        .transpose(0, 3, 2, 1)
        .reshape(cycle_count, map_count, 2 * mode_count)
    )
    pairs_t = jnp.swapaxes(pair_table(noise_mats), 1, 2) * jnp.asarray(weight, jnp.bfloat16)
    grid_spec = pltpu.PrefetchScalarGridSpec(
        num_scalar_prefetch=1,
        grid=(cycle_count,),
        in_specs=[
            pl.BlockSpec((1, map_count, 2 * mode_count), lambda r, idx: (r, 0, 0)),
            pl.BlockSpec((1, 2 * mode_count, RLEN), lambda r, idx: (r, 0, 0)),
            pl.BlockSpec(pairs_t.shape, lambda r, idx: (0, 0, 0)),
        ],
        out_specs=pl.BlockSpec((1, map_count, 2 * mode_count), lambda r, idx: (r, 0, 0)),
        scratch_shapes=[pltpu.VMEM((map_count, RLEN), jnp.bfloat16)],
    )
    back = pl.pallas_call(
        noise_kernel,
        grid_spec=grid_spec,
        out_shape=jax.ShapeDtypeStruct((cycle_count, map_count, 2 * mode_count), jnp.bfloat16),
    )(indices, coeff_t, tables, pairs_t)
    return (
        back.reshape(cycle_count, map_count, 2, mode_count)
        .transpose(0, 3, 2, 1)
        .reshape(cycle_count, mode_count, columns)
    )


def shards(
    solution,
    residual,
    direction,
    legendre,
    prior_inv,
    noise_mats,
    noise_index,
    cycle_lengths,
    m_values,
    cut_pattern,
):
    band_count = lax.axis_size("band")
    mode_local, cycle_total, l_local = legendre.shape
    map_count = direction.shape[1]
    columns = 2 * map_count
    band_rows = cycle_total // band_count
    weight = L / (cycle_total * RLEN)
    rounded = direction.astype(jnp.bfloat16).reshape(columns, mode_local, l_local)

    def row_mask(first_row, row_count):
        block_flags = lax.dynamic_slice_in_dim(cut_pattern, first_row // RB, row_count // RB, 1)
        return jnp.repeat(block_flags, RB, axis=1).T

    section = legendre
    products = jnp.einsum("mrl,nml->rmn", section, rounded, preferred_element_type=jnp.float32)
    masked_products = products * row_mask(jnp.int32(0), cycle_total).astype(jnp.float32)[:, :, None]
    coeffs = gather_cycles(masked_products.reshape(cycle_total, columns), band_count).astype(jnp.bfloat16)
    cycle_local = coeffs.shape[0]
    mode_total = coeffs.shape[1]
    outputs = cycle_transform(coeffs, cycle_lengths, noise_index, m_values, noise_mats, weight)
    backward = outputs.reshape(cycle_local, mode_total, columns)
    returned = spread_cycles(backward, band_count)
    masked = returned * row_mask(jnp.int32(0), cycle_total).astype(jnp.bfloat16)
    image_data = jnp.einsum(
        "mrl,rn->nml", legendre, masked, preferred_element_type=jnp.float32
    )
    image_data = image_data.reshape(2, map_count, mode_local, l_local)
    image_field = prior_inv[None, None, None, :] * direction + image_data
    norm_now, curvature, cross, image_norm = total_over_mesh(
        jnp.stack(
            [
                jnp.sum(residual * residual, axis=(0, 2, 3)),
                jnp.sum(direction * image_field, axis=(0, 2, 3)),
                jnp.sum(residual * image_field, axis=(0, 2, 3)),
                jnp.sum(image_field * image_field, axis=(0, 2, 3)),
            ]
        )
    )
    step_size = norm_now / curvature
    new_residual = residual - step_size[None, :, None, None] * image_field
    norm_next = norm_now - 2.0 * step_size * cross + step_size * step_size * image_norm
    growth = norm_next / norm_now
    new_solution = solution + step_size[None, :, None, None] * direction
    new_direction = new_residual + growth[None, :, None, None] * direction
    return (new_solution, new_residual, new_direction)


def solution(mesh):
    in_specs = (
        P(None, None, "mgrp", "band"),
        P(None, None, "mgrp", "band"),
        P(None, None, "mgrp", "band"),
        P("mgrp", None, "band"),
        P("band"),
        P(),
        P(("band", "mgrp"), None),
        P(("band", "mgrp")),
        P(),
        P("mgrp", None),
    )
    out_specs = (
        P(None, None, "mgrp", "band"),
        P(None, None, "mgrp", "band"),
        P(None, None, "mgrp", "band"),
    )
    return jax.shard_map(shards, mesh=mesh, in_specs=in_specs, out_specs=out_specs, check_vma=False)
```

```python
import functools
import math

import jax
import jax.numpy as jnp
from jax import lax
from jax.experimental import pallas as pl
from jax.experimental.pallas import tpu as pltpu
from jax.sharding import PartitionSpec as P

L = 8192
RLEN = 16384
BLK = 64
RB = 64


MESH_AXES = ("mgrp", "band")


def total_over_mesh(values):
    count = lax.axis_size(MESH_AXES)
    copies = jnp.broadcast_to(values[None], (count,) + values.shape)
    return jnp.sum(lax.all_to_all(copies, MESH_AXES, 0, 0, tiled=True), axis=0)


def gather_cycles(partials, band_count):
    cycle_total, columns = partials.shape
    group_count = lax.axis_size("mgrp")
    own = cycle_total // (band_count * group_count)
    pieces = partials.reshape(band_count, group_count, own, columns).transpose(1, 0, 2, 3)
    pieces = pieces.reshape(group_count * band_count, own, columns)
    received = lax.all_to_all(pieces, MESH_AXES, 0, 0, tiled=True)
    received = received.reshape(group_count, band_count, own, columns)
    return jnp.sum(received, axis=1).transpose(1, 0, 2)


def spread_cycles(backward, band_count):
    own, group_count, columns = backward.shape
    pieces = jnp.broadcast_to(
        backward.transpose(1, 0, 2)[:, None], (group_count, band_count, own, columns)
    ).reshape(group_count * band_count, own, columns)
    received = lax.all_to_all(pieces, MESH_AXES, 0, 0, tiled=True)
    received = received.reshape(group_count, band_count, own, columns).transpose(1, 0, 2, 3)
    return received.reshape(band_count * group_count * own, columns)


def cycle_tables(m_values, lengths, pixels):
    high_count = pixels // 128
    coarse = jnp.arange(high_count, dtype=jnp.int32) * 128
    fine = jnp.arange(128, dtype=jnp.int32)
    cycle_size = lengths[:, None, None].astype(jnp.float32)
    phase_high = m_values[None, :, None] * coarse[None, None, :] % lengths[:, None, None]
    phase_low = m_values[None, :, None] * fine[None, None, :] % lengths[:, None, None]
    angle_high = 2.0 * math.pi * phase_high.astype(jnp.float32) / cycle_size
    angle_low = 2.0 * math.pi * phase_low.astype(jnp.float32) / cycle_size
    cos_high = jnp.cos(angle_high)[:, :, :, None]
    sin_high = jnp.sin(angle_high)[:, :, :, None]
    cos_low = jnp.cos(angle_low)[:, :, None, :]
    sin_low = jnp.sin(angle_low)[:, :, None, :]
    cycle_count = lengths.shape[0]
    mode_count = m_values.shape[0]
    cos_full = (cos_high * cos_low - sin_high * sin_low).reshape(cycle_count, mode_count, pixels)
    sin_full = (sin_high * cos_low + cos_high * sin_low).reshape(cycle_count, mode_count, pixels)
    column = jnp.arange(pixels, dtype=jnp.int32)
    factor = jnp.where(m_values == 0, 1.0, 2.0).astype(jnp.float32)[None, :, None]
    inside = (column[None, None, :] < lengths[:, None, None]).astype(jnp.float32)
    cosine = factor * cos_full * inside
    sine_part = -factor * sin_full * inside
    return jnp.stack([cosine, sine_part], axis=1).astype(jnp.bfloat16)


def pair_table(noise_mats):
    kinds = noise_mats.shape[0]
    first = jnp.broadcast_to(noise_mats[:, None], (kinds, kinds, BLK, BLK))
    second = jnp.broadcast_to(noise_mats[None, :], (kinds, kinds, BLK, BLK))
    empty = jnp.zeros((kinds, kinds, BLK, BLK), noise_mats.dtype)
    upper = jnp.concatenate([first, empty], axis=3)
    lower = jnp.concatenate([empty, second], axis=3)
    return jnp.concatenate([upper, lower], axis=2).reshape(kinds * kinds, 2 * BLK, 2 * BLK)


def cycle_segment(coeffs, lengths, indices, m_values, pairs, kinds, weight):
    cycle_count, mode_count, columns = coeffs.shape
    map_count = columns // 2
    tables = cycle_tables(m_values, lengths, RLEN)
    split_coeffs = coeffs.reshape(cycle_count, mode_count, 2, map_count)
    sky_map = jnp.einsum(
        "rmcb,rcmk->rbk", split_coeffs, tables, preferred_element_type=jnp.float32
    ).astype(jnp.bfloat16)
    pair_count = RLEN // (2 * BLK)
    kind_pairs = indices.reshape(cycle_count, pair_count, 2)
    pair_index = kind_pairs[:, :, 0] * kinds + kind_pairs[:, :, 1]
    matrices = pairs.reshape(kinds * kinds, 4 * BLK * BLK)[pair_index].reshape(
        cycle_count, pair_count, 2 * BLK, 2 * BLK
    )
    blocked = sky_map.reshape(cycle_count, map_count, pair_count, 2 * BLK)
    noisy_map = weight * jnp.einsum(
        "rbqj,rqij->rbqi", blocked, matrices, preferred_element_type=jnp.float32
    )
    noisy_map = noisy_map.reshape(cycle_count, map_count, RLEN).astype(jnp.bfloat16)
    backward = jnp.einsum("rbk,rcmk->rmcb", noisy_map, tables, preferred_element_type=jnp.float32)
    return backward.reshape(cycle_count, mode_count, columns).astype(jnp.bfloat16)


def noise_kernel(index_ref, length_ref, coeff_ref, table_ref, pair_ref, back_ref, noisy_ref):
    cycle = pl.program_id(0)
    span = noisy_ref.shape[1]
    pair_width = 2 * BLK
    coeff = coeff_ref[0]
    side = int(round(pair_ref.shape[0] ** 0.5))

    def chunk(step, total):
        start = pl.multiple_of(step * span, span)
        table = table_ref[0, :, pl.ds(start, span)]
        sky = jnp.dot(coeff, table, preferred_element_type=jnp.float32).astype(jnp.bfloat16)
        for inner in range(span // pair_width):
            block = (start + inner * pair_width) // BLK
            pick = index_ref[cycle, block] * side + index_ref[cycle, block + 1]
            noisy = jnp.dot(
                sky[:, inner * pair_width:(inner + 1) * pair_width],
                pair_ref[pick],
                preferred_element_type=jnp.float32,
            )
            noisy_ref[:, inner * pair_width:(inner + 1) * pair_width] = noisy.astype(jnp.bfloat16)
        return total + lax.dot_general(
            noisy_ref[...], table, (((1,), (1,)), ((), ())), preferred_element_type=jnp.float32
        )

    used = (length_ref[cycle] + span - 1) // span
    total = lax.fori_loop(0, used, chunk, jnp.zeros(back_ref.shape[1:], jnp.float32))
    back_ref[0] = total.astype(back_ref.dtype)


def cycle_transform(coeffs, lengths, indices, m_values, noise_mats, weight):
    cycle_count, mode_count, columns = coeffs.shape
    map_count = columns // 2
    kinds = noise_mats.shape[0]
    tables = cycle_tables(m_values, lengths, RLEN).reshape(cycle_count, 2 * mode_count, RLEN)
    coeff_t = (
        coeffs.reshape(cycle_count, mode_count, 2, map_count)
        .transpose(0, 3, 2, 1)
        .reshape(cycle_count, map_count, 2 * mode_count)
    )
    pairs_t = jnp.swapaxes(pair_table(noise_mats), 1, 2) * jnp.asarray(weight, jnp.bfloat16)
    grid_spec = pltpu.PrefetchScalarGridSpec(
        num_scalar_prefetch=2,
        grid=(cycle_count,),
        in_specs=[
            pl.BlockSpec((1, map_count, 2 * mode_count), lambda r, idx, n: (r, 0, 0)),
            pl.BlockSpec((1, 2 * mode_count, RLEN), lambda r, idx, n: (r, 0, 0)),
            pl.BlockSpec(pairs_t.shape, lambda r, idx, n: (0, 0, 0)),
        ],
        out_specs=pl.BlockSpec((1, map_count, 2 * mode_count), lambda r, idx, n: (r, 0, 0)),
        scratch_shapes=[pltpu.VMEM((map_count, 4096), jnp.bfloat16)],
    )
    back = pl.pallas_call(
        noise_kernel,
        grid_spec=grid_spec,
        out_shape=jax.ShapeDtypeStruct((cycle_count, map_count, 2 * mode_count), jnp.bfloat16),
    )(indices, lengths, coeff_t, tables, pairs_t)
    return (
        back.reshape(cycle_count, map_count, 2, mode_count)
        .transpose(0, 3, 2, 1)
        .reshape(cycle_count, mode_count, columns)
    )


def shards(
    solution,
    residual,
    direction,
    legendre,
    prior_inv,
    noise_mats,
    noise_index,
    cycle_lengths,
    m_values,
    cut_pattern,
):
    band_count = lax.axis_size("band")
    mode_local, cycle_total, l_local = legendre.shape
    map_count = direction.shape[1]
    columns = 2 * map_count
    band_rows = cycle_total // band_count
    weight = L / (cycle_total * RLEN)
    rounded = direction.astype(jnp.bfloat16).reshape(columns, mode_local, l_local)

    def row_mask(first_row, row_count):
        block_flags = lax.dynamic_slice_in_dim(cut_pattern, first_row // RB, row_count // RB, 1)
        return jnp.repeat(block_flags, RB, axis=1).T

    section = legendre
    products = jnp.einsum("mrl,nml->rmn", section, rounded, preferred_element_type=jnp.float32)
    masked_products = products * row_mask(jnp.int32(0), cycle_total).astype(jnp.float32)[:, :, None]
    coeffs = gather_cycles(masked_products.reshape(cycle_total, columns), band_count).astype(jnp.bfloat16)
    cycle_local = coeffs.shape[0]
    mode_total = coeffs.shape[1]
    outputs = cycle_transform(coeffs, cycle_lengths, noise_index, m_values, noise_mats, weight)
    backward = outputs.reshape(cycle_local, mode_total, columns)
    returned = spread_cycles(backward, band_count)
    masked = returned * row_mask(jnp.int32(0), cycle_total).astype(jnp.bfloat16)
    image_data = jnp.einsum(
        "mrl,rn->nml", legendre, masked, preferred_element_type=jnp.float32
    )
    image_data = image_data.reshape(2, map_count, mode_local, l_local)
    image_field = prior_inv[None, None, None, :] * direction + image_data
    norm_now, curvature, cross, image_norm = total_over_mesh(
        jnp.stack(
            [
                jnp.sum(residual * residual, axis=(0, 2, 3)),
                jnp.sum(direction * image_field, axis=(0, 2, 3)),
                jnp.sum(residual * image_field, axis=(0, 2, 3)),
                jnp.sum(image_field * image_field, axis=(0, 2, 3)),
            ]
        )
    )
    step_size = norm_now / curvature
    new_residual = residual - step_size[None, :, None, None] * image_field
    norm_next = norm_now - 2.0 * step_size * cross + step_size * step_size * image_norm
    growth = norm_next / norm_now
    new_solution = solution + step_size[None, :, None, None] * direction
    new_direction = new_residual + growth[None, :, None, None] * direction
    return (new_solution, new_residual, new_direction)


def solution(mesh):
    in_specs = (
        P(None, None, "mgrp", "band"),
        P(None, None, "mgrp", "band"),
        P(None, None, "mgrp", "band"),
        P("mgrp", None, "band"),
        P("band"),
        P(),
        P(("band", "mgrp"), None),
        P(("band", "mgrp")),
        P(),
        P("mgrp", None),
    )
    out_specs = (
        P(None, None, "mgrp", "band"),
        P(None, None, "mgrp", "band"),
        P(None, None, "mgrp", "band"),
    )
    return jax.shard_map(shards, mesh=mesh, in_specs=in_specs, out_specs=out_specs, check_vma=False)
```

```python
import functools
import math

import jax
import jax.numpy as jnp
from jax import lax
from jax.experimental import pallas as pl
from jax.experimental.pallas import tpu as pltpu
from jax.sharding import PartitionSpec as P

L = 8192
RLEN = 16384
BLK = 64
RB = 64


MESH_AXES = ("mgrp", "band")


def total_over_mesh(values):
    count = lax.axis_size(MESH_AXES)
    copies = jnp.broadcast_to(values[None], (count,) + values.shape)
    return jnp.sum(lax.all_to_all(copies, MESH_AXES, 0, 0, tiled=True), axis=0)


def gather_cycles(partials):
    group_count, band_count, own, columns = partials.shape
    pieces = partials.reshape(group_count * band_count, own, columns)
    received = lax.all_to_all(pieces, MESH_AXES, 0, 0, tiled=True)
    received = received.reshape(group_count, band_count, own, columns)
    return jnp.sum(received, axis=1).transpose(1, 0, 2)


def spread_cycles(backward, band_count):
    own, group_count, columns = backward.shape
    pieces = jnp.broadcast_to(
        backward.transpose(1, 0, 2)[:, None], (group_count, band_count, own, columns)
    ).reshape(group_count * band_count, own, columns)
    received = lax.all_to_all(pieces, MESH_AXES, 0, 0, tiled=True)
    received = received.reshape(group_count, band_count, own, columns).transpose(1, 0, 2, 3)
    return received.reshape(band_count * group_count * own, columns)


def cycle_tables(m_values, lengths, pixels):
    high_count = pixels // 128
    coarse = jnp.arange(high_count, dtype=jnp.int32) * 128
    fine = jnp.arange(128, dtype=jnp.int32)
    cycle_size = lengths[:, None, None].astype(jnp.float32)
    phase_high = m_values[None, :, None] * coarse[None, None, :] % lengths[:, None, None]
    phase_low = m_values[None, :, None] * fine[None, None, :] % lengths[:, None, None]
    angle_high = 2.0 * math.pi * phase_high.astype(jnp.float32) / cycle_size
    angle_low = 2.0 * math.pi * phase_low.astype(jnp.float32) / cycle_size
    cos_high = jnp.cos(angle_high)[:, :, :, None]
    sin_high = jnp.sin(angle_high)[:, :, :, None]
    cos_low = jnp.cos(angle_low)[:, :, None, :]
    sin_low = jnp.sin(angle_low)[:, :, None, :]
    cycle_count = lengths.shape[0]
    mode_count = m_values.shape[0]
    cos_full = (cos_high * cos_low - sin_high * sin_low).reshape(cycle_count, mode_count, pixels)
    sin_full = (sin_high * cos_low + cos_high * sin_low).reshape(cycle_count, mode_count, pixels)
    column = jnp.arange(pixels, dtype=jnp.int32)
    factor = jnp.where(m_values == 0, 1.0, 2.0).astype(jnp.float32)[None, :, None]
    inside = (column[None, None, :] < lengths[:, None, None]).astype(jnp.float32)
    cosine = factor * cos_full * inside
    sine_part = -factor * sin_full * inside
    return jnp.stack([cosine, sine_part], axis=2).astype(jnp.bfloat16)


def pair_table(noise_mats):
    kinds = noise_mats.shape[0]
    first = jnp.broadcast_to(noise_mats[:, None], (kinds, kinds, BLK, BLK))
    second = jnp.broadcast_to(noise_mats[None, :], (kinds, kinds, BLK, BLK))
    empty = jnp.zeros((kinds, kinds, BLK, BLK), noise_mats.dtype)
    upper = jnp.concatenate([first, empty], axis=3)
    lower = jnp.concatenate([empty, second], axis=3)
    return jnp.concatenate([upper, lower], axis=2).reshape(kinds * kinds, 2 * BLK, 2 * BLK)


def cycle_segment(coeffs, lengths, indices, m_values, pairs, kinds, weight):
    cycle_count, mode_count, columns = coeffs.shape
    map_count = columns // 2
    tables = cycle_tables(m_values, lengths, RLEN)
    split_coeffs = coeffs.reshape(cycle_count, mode_count, 2, map_count)
    sky_map = jnp.einsum(
        "rmcb,rcmk->rbk", split_coeffs, tables, preferred_element_type=jnp.float32
    ).astype(jnp.bfloat16)
    pair_count = RLEN // (2 * BLK)
    kind_pairs = indices.reshape(cycle_count, pair_count, 2)
    pair_index = kind_pairs[:, :, 0] * kinds + kind_pairs[:, :, 1]
    matrices = pairs.reshape(kinds * kinds, 4 * BLK * BLK)[pair_index].reshape(
        cycle_count, pair_count, 2 * BLK, 2 * BLK
    )
    blocked = sky_map.reshape(cycle_count, map_count, pair_count, 2 * BLK)
    noisy_map = weight * jnp.einsum(
        "rbqj,rqij->rbqi", blocked, matrices, preferred_element_type=jnp.float32
    )
    noisy_map = noisy_map.reshape(cycle_count, map_count, RLEN).astype(jnp.bfloat16)
    backward = jnp.einsum("rbk,rcmk->rmcb", noisy_map, tables, preferred_element_type=jnp.float32)
    return backward.reshape(cycle_count, mode_count, columns).astype(jnp.bfloat16)


def noise_kernel(index_ref, length_ref, coeff_ref, table_ref, pair_ref, back_ref, noisy_ref):
    cycle = pl.program_id(0)
    span = noisy_ref.shape[1]
    pair_width = 2 * BLK
    coeff = coeff_ref[0]
    side = int(round(pair_ref.shape[0] ** 0.5))

    def chunk(step, total):
        start = pl.multiple_of(step * span, span)
        table = table_ref[0, :, pl.ds(start, span)]
        sky = lax.dot_general(
            coeff, table, (((0,), (0,)), ((), ())), preferred_element_type=jnp.float32
        ).astype(jnp.bfloat16)
        for inner in range(span // pair_width):
            block = (start + inner * pair_width) // BLK
            pick = index_ref[cycle, block] * side + index_ref[cycle, block + 1]
            noisy = jnp.dot(
                sky[:, inner * pair_width:(inner + 1) * pair_width],
                pair_ref[pick],
                preferred_element_type=jnp.float32,
            )
            noisy_ref[:, inner * pair_width:(inner + 1) * pair_width] = noisy.astype(jnp.bfloat16)
        return total + lax.dot_general(
            table, noisy_ref[...], (((1,), (1,)), ((), ())), preferred_element_type=jnp.float32
        )

    used = (length_ref[cycle] + span - 1) // span
    total = lax.fori_loop(0, used, chunk, jnp.zeros(back_ref.shape[1:], jnp.float32))
    back_ref[0] = total.astype(back_ref.dtype)


def cycle_transform(coeffs, lengths, indices, m_values, noise_mats, weight):
    cycle_count, mode_count, columns = coeffs.shape
    map_count = columns // 2
    kinds = noise_mats.shape[0]
    tables = cycle_tables(m_values, lengths, RLEN).reshape(cycle_count, 2 * mode_count, RLEN)
    coeff_t = coeffs.reshape(cycle_count, 2 * mode_count, map_count)
    pairs_t = jnp.swapaxes(pair_table(noise_mats), 1, 2) * jnp.asarray(weight, jnp.bfloat16)
    grid_spec = pltpu.PrefetchScalarGridSpec(
        num_scalar_prefetch=2,
        grid=(cycle_count,),
        in_specs=[
            pl.BlockSpec((1, 2 * mode_count, map_count), lambda r, idx, n: (r, 0, 0)),
            pl.BlockSpec((1, 2 * mode_count, RLEN), lambda r, idx, n: (r, 0, 0)),
            pl.BlockSpec(pairs_t.shape, lambda r, idx, n: (0, 0, 0)),
        ],
        out_specs=pl.BlockSpec((1, 2 * mode_count, map_count), lambda r, idx, n: (r, 0, 0)),
        scratch_shapes=[pltpu.VMEM((map_count, 4096), jnp.bfloat16)],
    )
    back = pl.pallas_call(
        noise_kernel,
        grid_spec=grid_spec,
        out_shape=jax.ShapeDtypeStruct((cycle_count, 2 * mode_count, map_count), jnp.bfloat16),
    )(indices, lengths, coeff_t, tables, pairs_t)
    return back.reshape(cycle_count, mode_count, columns)


def shards(
    solution,
    residual,
    direction,
    legendre,
    prior_inv,
    noise_mats,
    noise_index,
    cycle_lengths,
    m_values,
    cut_pattern,
):
    band_count = lax.axis_size("band")
    mode_local, cycle_total, l_local = legendre.shape
    map_count = direction.shape[1]
    columns = 2 * map_count
    band_rows = cycle_total // band_count
    weight = L / (cycle_total * RLEN)
    rounded = direction.astype(jnp.bfloat16).reshape(columns, mode_local, l_local)

    def row_mask(first_row, row_count):
        block_flags = lax.dynamic_slice_in_dim(cut_pattern, first_row // RB, row_count // RB, 1)
        return jnp.repeat(block_flags, RB, axis=1).T

    group_count = lax.axis_size("mgrp")
    own = cycle_total // (band_count * group_count)
    section = legendre[0].reshape(band_count, group_count, own, l_local)
    products = jnp.einsum(
        "jgcl,nl->gjcn", section, rounded[:, 0, :], preferred_element_type=jnp.float32
    )
    keep = row_mask(jnp.int32(0), cycle_total).reshape(band_count, group_count, own)
    keep = keep.transpose(1, 0, 2).astype(jnp.float32)[:, :, :, None]
    coeffs = gather_cycles(products * keep).astype(jnp.bfloat16)
    cycle_local = coeffs.shape[0]
    mode_total = coeffs.shape[1]
    outputs = cycle_transform(coeffs, cycle_lengths, noise_index, m_values, noise_mats, weight)
    backward = outputs.reshape(cycle_local, mode_total, columns)
    returned = spread_cycles(backward, band_count)
    masked = returned * row_mask(jnp.int32(0), cycle_total).astype(jnp.bfloat16)
    image_data = jnp.einsum(
        "mrl,rn->nml", legendre, masked, preferred_element_type=jnp.float32
    )
    image_data = image_data.reshape(2, map_count, mode_local, l_local)
    image_field = prior_inv[None, None, None, :] * direction + image_data
    norm_now, curvature, cross, image_norm = total_over_mesh(
        jnp.stack(
            [
                jnp.sum(residual * residual, axis=(0, 2, 3)),
                jnp.sum(direction * image_field, axis=(0, 2, 3)),
                jnp.sum(residual * image_field, axis=(0, 2, 3)),
                jnp.sum(image_field * image_field, axis=(0, 2, 3)),
            ]
        )
    )
    step_size = norm_now / curvature
    new_residual = residual - step_size[None, :, None, None] * image_field
    norm_next = norm_now - 2.0 * step_size * cross + step_size * step_size * image_norm
    growth = norm_next / norm_now
    new_solution = solution + step_size[None, :, None, None] * direction
    new_direction = new_residual + growth[None, :, None, None] * direction
    return (new_solution, new_residual, new_direction)


def solution(mesh):
    in_specs = (
        P(None, None, "mgrp", "band"),
        P(None, None, "mgrp", "band"),
        P(None, None, "mgrp", "band"),
        P("mgrp", None, "band"),
        P("band"),
        P(),
        P(("band", "mgrp"), None),
        P(("band", "mgrp")),
        P(),
        P("mgrp", None),
    )
    out_specs = (
        P(None, None, "mgrp", "band"),
        P(None, None, "mgrp", "band"),
        P(None, None, "mgrp", "band"),
    )
    return jax.shard_map(shards, mesh=mesh, in_specs=in_specs, out_specs=out_specs, check_vma=False)
```

```python
import functools
import math

import jax
import jax.numpy as jnp
from jax import lax
from jax.experimental import pallas as pl
from jax.experimental.pallas import tpu as pltpu
from jax.sharding import PartitionSpec as P

L = 8192
RLEN = 16384
BLK = 64
RB = 64


MESH_AXES = ("mgrp", "band")


def total_over_mesh(values):
    count = lax.axis_size(MESH_AXES)
    copies = jnp.broadcast_to(values[None], (count,) + values.shape)
    return jnp.sum(lax.all_to_all(copies, MESH_AXES, 0, 0, tiled=True), axis=0)


def gather_cycles(partials, band_count):
    cycle_total, columns = partials.shape
    group_count = lax.axis_size("mgrp")
    own = cycle_total // (band_count * group_count)
    pieces = partials.reshape(band_count, group_count, own, columns).transpose(1, 0, 2, 3)
    pieces = pieces.reshape(group_count * band_count, own, columns)
    received = lax.all_to_all(pieces, MESH_AXES, 0, 0, tiled=True)
    received = received.reshape(group_count, band_count, own, columns)
    return jnp.sum(received, axis=1).transpose(1, 0, 2)


def spread_cycles(backward, band_count):
    own, group_count, columns = backward.shape
    pieces = jnp.broadcast_to(
        backward.transpose(1, 0, 2)[:, None], (group_count, band_count, own, columns)
    ).reshape(group_count * band_count, own, columns)
    received = lax.all_to_all(pieces, MESH_AXES, 0, 0, tiled=True)
    received = received.reshape(group_count, band_count, own, columns).transpose(1, 0, 2, 3)
    return received.reshape(band_count * group_count * own, columns)


def cycle_tables(m_values, lengths, pixels):
    high_count = pixels // 128
    coarse = jnp.arange(high_count, dtype=jnp.int32) * 128
    fine = jnp.arange(128, dtype=jnp.int32)
    cycle_size = lengths[:, None, None].astype(jnp.float32)
    phase_high = m_values[None, :, None] * coarse[None, None, :] % lengths[:, None, None]
    phase_low = m_values[None, :, None] * fine[None, None, :] % lengths[:, None, None]
    angle_high = 2.0 * math.pi * phase_high.astype(jnp.float32) / cycle_size
    angle_low = 2.0 * math.pi * phase_low.astype(jnp.float32) / cycle_size
    cos_high = jnp.cos(angle_high)[:, :, :, None]
    sin_high = jnp.sin(angle_high)[:, :, :, None]
    cos_low = jnp.cos(angle_low)[:, :, None, :]
    sin_low = jnp.sin(angle_low)[:, :, None, :]
    cycle_count = lengths.shape[0]
    mode_count = m_values.shape[0]
    cos_full = (cos_high * cos_low - sin_high * sin_low).reshape(cycle_count, mode_count, pixels)
    sin_full = (sin_high * cos_low + cos_high * sin_low).reshape(cycle_count, mode_count, pixels)
    column = jnp.arange(pixels, dtype=jnp.int32)
    factor = jnp.where(m_values == 0, 1.0, 2.0).astype(jnp.float32)[None, :, None]
    inside = (column[None, None, :] < lengths[:, None, None]).astype(jnp.float32)
    cosine = factor * cos_full * inside
    sine_part = -factor * sin_full * inside
    return jnp.stack([cosine, sine_part], axis=1).astype(jnp.bfloat16)


def pair_table(noise_mats):
    kinds = noise_mats.shape[0]
    first = jnp.broadcast_to(noise_mats[:, None], (kinds, kinds, BLK, BLK))
    second = jnp.broadcast_to(noise_mats[None, :], (kinds, kinds, BLK, BLK))
    empty = jnp.zeros((kinds, kinds, BLK, BLK), noise_mats.dtype)
    upper = jnp.concatenate([first, empty], axis=3)
    lower = jnp.concatenate([empty, second], axis=3)
    return jnp.concatenate([upper, lower], axis=2).reshape(kinds * kinds, 2 * BLK, 2 * BLK)


def cycle_segment(coeffs, lengths, indices, m_values, pairs, kinds, weight):
    cycle_count, mode_count, columns = coeffs.shape
    map_count = columns // 2
    tables = cycle_tables(m_values, lengths, RLEN)
    split_coeffs = coeffs.reshape(cycle_count, mode_count, 2, map_count)
    sky_map = jnp.einsum(
        "rmcb,rcmk->rbk", split_coeffs, tables, preferred_element_type=jnp.float32
    ).astype(jnp.bfloat16)
    pair_count = RLEN // (2 * BLK)
    kind_pairs = indices.reshape(cycle_count, pair_count, 2)
    pair_index = kind_pairs[:, :, 0] * kinds + kind_pairs[:, :, 1]
    matrices = pairs.reshape(kinds * kinds, 4 * BLK * BLK)[pair_index].reshape(
        cycle_count, pair_count, 2 * BLK, 2 * BLK
    )
    blocked = sky_map.reshape(cycle_count, map_count, pair_count, 2 * BLK)
    noisy_map = weight * jnp.einsum(
        "rbqj,rqij->rbqi", blocked, matrices, preferred_element_type=jnp.float32
    )
    noisy_map = noisy_map.reshape(cycle_count, map_count, RLEN).astype(jnp.bfloat16)
    backward = jnp.einsum("rbk,rcmk->rmcb", noisy_map, tables, preferred_element_type=jnp.float32)
    return backward.reshape(cycle_count, mode_count, columns).astype(jnp.bfloat16)


def noise_kernel(index_ref, length_ref, coeff_ref, table_ref, pair_ref, back_ref, noisy_ref):
    cycle = pl.program_id(0)
    span = noisy_ref.shape[1]
    pair_width = 2 * BLK
    coeff = coeff_ref[0]
    side = int(round(pair_ref.shape[0] ** 0.5))

    def chunk(step, total):
        start = pl.multiple_of(step * span, span)
        table = table_ref[0, :, pl.ds(start, span)]
        sky = jnp.dot(coeff, table, preferred_element_type=jnp.float32).astype(jnp.bfloat16)
        for inner in range(span // pair_width):
            block = (start + inner * pair_width) // BLK
            pick = index_ref[cycle, block] * side + index_ref[cycle, block + 1]
            noisy = jnp.dot(
                sky[:, inner * pair_width:(inner + 1) * pair_width],
                pair_ref[pick],
                preferred_element_type=jnp.float32,
            )
            noisy_ref[:, inner * pair_width:(inner + 1) * pair_width] = noisy.astype(jnp.bfloat16)
        return total + lax.dot_general(
            noisy_ref[...], table, (((1,), (1,)), ((), ())), preferred_element_type=jnp.float32
        )

    used = (length_ref[cycle] + span - 1) // span
    total = lax.fori_loop(0, used, chunk, jnp.zeros(back_ref.shape[1:], jnp.float32))
    back_ref[0] = total.astype(back_ref.dtype)


def cycle_transform(coeffs, lengths, indices, m_values, noise_mats, weight):
    cycle_count, mode_count, columns = coeffs.shape
    map_count = columns // 2
    kinds = noise_mats.shape[0]
    tables = cycle_tables(m_values, lengths, RLEN).reshape(cycle_count, 2 * mode_count, RLEN)
    coeff_t = (
        coeffs.reshape(cycle_count, mode_count, 2, map_count)
        .transpose(0, 3, 2, 1)
        .reshape(cycle_count, map_count, 2 * mode_count)
    )
    pairs_t = jnp.swapaxes(pair_table(noise_mats), 1, 2) * jnp.asarray(weight, jnp.bfloat16)
    grid_spec = pltpu.PrefetchScalarGridSpec(
        num_scalar_prefetch=2,
        grid=(cycle_count,),
        in_specs=[
            pl.BlockSpec((1, map_count, 2 * mode_count), lambda r, idx, n: (r, 0, 0)),
            pl.BlockSpec((1, 2 * mode_count, RLEN), lambda r, idx, n: (r, 0, 0)),
            pl.BlockSpec(pairs_t.shape, lambda r, idx, n: (0, 0, 0)),
        ],
        out_specs=pl.BlockSpec((1, map_count, 2 * mode_count), lambda r, idx, n: (r, 0, 0)),
        scratch_shapes=[pltpu.VMEM((map_count, 4096), jnp.bfloat16)],
    )
    back = pl.pallas_call(
        noise_kernel,
        grid_spec=grid_spec,
        out_shape=jax.ShapeDtypeStruct((cycle_count, map_count, 2 * mode_count), jnp.bfloat16),
    )(indices, lengths, coeff_t, tables, pairs_t)
    return (
        back.reshape(cycle_count, map_count, 2, mode_count)
        .transpose(0, 3, 2, 1)
        .reshape(cycle_count, mode_count, columns)
    )


def shards(
    solution,
    residual,
    direction,
    legendre,
    prior_inv,
    noise_mats,
    noise_index,
    cycle_lengths,
    m_values,
    cut_pattern,
):
    band_count = lax.axis_size("band")
    mode_local, cycle_total, l_local = legendre.shape
    map_count = direction.shape[1]
    columns = 2 * map_count
    band_rows = cycle_total // band_count
    weight = L / (cycle_total * RLEN)
    rounded = direction.astype(jnp.bfloat16).reshape(columns, mode_local, l_local)

    def row_mask(first_row, row_count):
        block_flags = lax.dynamic_slice_in_dim(cut_pattern, first_row // RB, row_count // RB, 1)
        return jnp.repeat(block_flags, RB, axis=1).T

    section = legendre
    products = jnp.einsum("mrl,nml->rmn", section, rounded, preferred_element_type=jnp.float32)
    masked_products = products * row_mask(jnp.int32(0), cycle_total).astype(jnp.float32)[:, :, None]
    coeffs = gather_cycles(masked_products.reshape(cycle_total, columns), band_count).astype(jnp.bfloat16)
    cycle_local = coeffs.shape[0]
    mode_total = coeffs.shape[1]
    group_count = lax.axis_size("mgrp")
    half = cycle_local // 2
    keep_rows = row_mask(jnp.int32(0), cycle_total).astype(jnp.bfloat16)
    keep_rows = keep_rows.reshape(band_count, group_count, cycle_local, 1)
    rows = legendre[0].reshape(band_count, group_count, cycle_local, l_local)
    image_data = None
    for part in range(2):
        chosen = slice(part * half, (part + 1) * half)
        outputs = cycle_transform(
            coeffs[chosen], cycle_lengths[chosen], noise_index[chosen], m_values, noise_mats, weight
        )
        returned = spread_cycles(outputs.reshape(half, mode_total, columns), band_count)
        masked = returned * keep_rows[:, :, chosen].reshape(-1, 1)
        partial = jnp.einsum(
            "rl,rn->nl", rows[:, :, chosen].reshape(-1, l_local), masked,
            preferred_element_type=jnp.float32,
        )
        image_data = partial if image_data is None else image_data + partial
    image_data = image_data.reshape(2, map_count, mode_local, l_local)
    image_field = prior_inv[None, None, None, :] * direction + image_data
    norm_now, curvature, cross, image_norm = total_over_mesh(
        jnp.stack(
            [
                jnp.sum(residual * residual, axis=(0, 2, 3)),
                jnp.sum(direction * image_field, axis=(0, 2, 3)),
                jnp.sum(residual * image_field, axis=(0, 2, 3)),
                jnp.sum(image_field * image_field, axis=(0, 2, 3)),
            ]
        )
    )
    step_size = norm_now / curvature
    new_residual = residual - step_size[None, :, None, None] * image_field
    norm_next = norm_now - 2.0 * step_size * cross + step_size * step_size * image_norm
    growth = norm_next / norm_now
    new_solution = solution + step_size[None, :, None, None] * direction
    new_direction = new_residual + growth[None, :, None, None] * direction
    return (new_solution, new_residual, new_direction)


def solution(mesh):
    in_specs = (
        P(None, None, "mgrp", "band"),
        P(None, None, "mgrp", "band"),
        P(None, None, "mgrp", "band"),
        P("mgrp", None, "band"),
        P("band"),
        P(),
        P(("band", "mgrp"), None),
        P(("band", "mgrp")),
        P(),
        P("mgrp", None),
    )
    out_specs = (
        P(None, None, "mgrp", "band"),
        P(None, None, "mgrp", "band"),
        P(None, None, "mgrp", "band"),
    )
    return jax.shard_map(shards, mesh=mesh, in_specs=in_specs, out_specs=out_specs, check_vma=False)
```

```python
import functools
import math

import jax
import jax.numpy as jnp
from jax import lax
from jax.experimental import pallas as pl
from jax.experimental.pallas import tpu as pltpu
from jax.sharding import PartitionSpec as P

L = 8192
RLEN = 16384
BLK = 64
RB = 64


MESH_AXES = ("mgrp", "band")


def total_over_mesh(values):
    count = lax.axis_size(MESH_AXES)
    copies = jnp.broadcast_to(values[None], (count,) + values.shape)
    return jnp.sum(lax.all_to_all(copies, MESH_AXES, 0, 0, tiled=True), axis=0)


def gather_cycles(partials, band_count):
    cycle_total, columns = partials.shape
    group_count = lax.axis_size("mgrp")
    own = cycle_total // (band_count * group_count)
    pieces = partials.reshape(band_count, group_count, own, columns).transpose(1, 0, 2, 3)
    pieces = pieces.reshape(group_count * band_count, own, columns)
    received = lax.all_to_all(pieces, MESH_AXES, 0, 0, tiled=True)
    received = received.reshape(group_count, band_count, own, columns)
    return jnp.sum(received, axis=1).transpose(1, 0, 2)


def spread_cycles(backward, band_count):
    own, group_count, columns = backward.shape
    pieces = jnp.broadcast_to(
        backward.transpose(1, 0, 2)[:, None], (group_count, band_count, own, columns)
    ).reshape(group_count * band_count, own, columns)
    received = lax.all_to_all(pieces, MESH_AXES, 0, 0, tiled=True)
    received = received.reshape(group_count, band_count, own, columns).transpose(1, 0, 2, 3)
    return received.reshape(band_count * group_count * own, columns)


def cycle_tables(m_values, lengths, pixels):
    high_count = pixels // 128
    coarse = jnp.arange(high_count, dtype=jnp.int32) * 128
    fine = jnp.arange(128, dtype=jnp.int32)
    cycle_size = lengths[:, None, None].astype(jnp.float32)
    phase_high = m_values[None, :, None] * coarse[None, None, :] % lengths[:, None, None]
    phase_low = m_values[None, :, None] * fine[None, None, :] % lengths[:, None, None]
    angle_high = 2.0 * math.pi * phase_high.astype(jnp.float32) / cycle_size
    angle_low = 2.0 * math.pi * phase_low.astype(jnp.float32) / cycle_size
    cos_high = jnp.cos(angle_high)[:, :, :, None]
    sin_high = jnp.sin(angle_high)[:, :, :, None]
    cos_low = jnp.cos(angle_low)[:, :, None, :]
    sin_low = jnp.sin(angle_low)[:, :, None, :]
    cycle_count = lengths.shape[0]
    mode_count = m_values.shape[0]
    cos_full = (cos_high * cos_low - sin_high * sin_low).reshape(cycle_count, mode_count, pixels)
    sin_full = (sin_high * cos_low + cos_high * sin_low).reshape(cycle_count, mode_count, pixels)
    column = jnp.arange(pixels, dtype=jnp.int32)
    factor = jnp.where(m_values == 0, 1.0, 2.0).astype(jnp.float32)[None, :, None]
    inside = (column[None, None, :] < lengths[:, None, None]).astype(jnp.float32)
    cosine = factor * cos_full * inside
    sine_part = -factor * sin_full * inside
    return jnp.stack([cosine, sine_part], axis=1).astype(jnp.bfloat16)


def pair_table(noise_mats):
    kinds = noise_mats.shape[0]
    first = jnp.broadcast_to(noise_mats[:, None], (kinds, kinds, BLK, BLK))
    second = jnp.broadcast_to(noise_mats[None, :], (kinds, kinds, BLK, BLK))
    empty = jnp.zeros((kinds, kinds, BLK, BLK), noise_mats.dtype)
    upper = jnp.concatenate([first, empty], axis=3)
    lower = jnp.concatenate([empty, second], axis=3)
    return jnp.concatenate([upper, lower], axis=2).reshape(kinds * kinds, 2 * BLK, 2 * BLK)


def cycle_segment(coeffs, lengths, indices, m_values, pairs, kinds, weight):
    cycle_count, mode_count, columns = coeffs.shape
    map_count = columns // 2
    tables = cycle_tables(m_values, lengths, RLEN)
    split_coeffs = coeffs.reshape(cycle_count, mode_count, 2, map_count)
    sky_map = jnp.einsum(
        "rmcb,rcmk->rbk", split_coeffs, tables, preferred_element_type=jnp.float32
    ).astype(jnp.bfloat16)
    pair_count = RLEN // (2 * BLK)
    kind_pairs = indices.reshape(cycle_count, pair_count, 2)
    pair_index = kind_pairs[:, :, 0] * kinds + kind_pairs[:, :, 1]
    matrices = pairs.reshape(kinds * kinds, 4 * BLK * BLK)[pair_index].reshape(
        cycle_count, pair_count, 2 * BLK, 2 * BLK
    )
    blocked = sky_map.reshape(cycle_count, map_count, pair_count, 2 * BLK)
    noisy_map = weight * jnp.einsum(
        "rbqj,rqij->rbqi", blocked, matrices, preferred_element_type=jnp.float32
    )
    noisy_map = noisy_map.reshape(cycle_count, map_count, RLEN).astype(jnp.bfloat16)
    backward = jnp.einsum("rbk,rcmk->rmcb", noisy_map, tables, preferred_element_type=jnp.float32)
    return backward.reshape(cycle_count, mode_count, columns).astype(jnp.bfloat16)


def noise_kernel(index_ref, length_ref, coeff_ref, table_ref, pair_ref, back_ref, noisy_ref):
    cycle = pl.program_id(0)
    wide = noisy_ref.shape[1]
    pair_width = 2 * BLK
    coeff = coeff_ref[0]
    side = int(round(pair_ref.shape[0] ** 0.5))

    def chunk(start, span, total):
        table = table_ref[0, :, pl.ds(start, span)]
        sky = jnp.dot(coeff, table, preferred_element_type=jnp.float32).astype(jnp.bfloat16)
        for inner in range(span // pair_width):
            block = (start + inner * pair_width) // BLK
            pick = index_ref[cycle, block] * side + index_ref[cycle, block + 1]
            noisy = jnp.dot(
                sky[:, inner * pair_width:(inner + 1) * pair_width],
                pair_ref[pick],
                preferred_element_type=jnp.float32,
            )
            noisy_ref[:, inner * pair_width:(inner + 1) * pair_width] = noisy.astype(jnp.bfloat16)
        return total + lax.dot_general(
            noisy_ref[:, :span], table, (((1,), (1,)), ((), ())), preferred_element_type=jnp.float32
        )

    length = length_ref[cycle]
    full = length // wide
    rest = length - full * wide
    narrow = wide // 2
    wide_count = full + (rest > narrow).astype(jnp.int32)
    narrow_count = ((rest > 0) & (rest <= narrow)).astype(jnp.int32)
    total = lax.fori_loop(
        0,
        wide_count,
        lambda step, acc: chunk(pl.multiple_of(step * wide, wide), wide, acc),
        jnp.zeros(back_ref.shape[1:], jnp.float32),
    )
    total = lax.fori_loop(
        0,
        narrow_count,
        lambda step, acc: chunk(pl.multiple_of(full * wide, wide), narrow, acc),
        total,
    )
    back_ref[0] = total.astype(back_ref.dtype)


def cycle_transform(coeffs, lengths, indices, m_values, noise_mats, weight):
    cycle_count, mode_count, columns = coeffs.shape
    map_count = columns // 2
    kinds = noise_mats.shape[0]
    tables = cycle_tables(m_values, lengths, RLEN).reshape(cycle_count, 2 * mode_count, RLEN)
    coeff_t = (
        coeffs.reshape(cycle_count, mode_count, 2, map_count)
        .transpose(0, 3, 2, 1)
        .reshape(cycle_count, map_count, 2 * mode_count)
    )
    pairs_t = jnp.swapaxes(pair_table(noise_mats), 1, 2) * jnp.asarray(weight, jnp.bfloat16)
    grid_spec = pltpu.PrefetchScalarGridSpec(
        num_scalar_prefetch=2,
        grid=(cycle_count,),
        in_specs=[
            pl.BlockSpec((1, map_count, 2 * mode_count), lambda r, idx, n: (r, 0, 0)),
            pl.BlockSpec((1, 2 * mode_count, RLEN), lambda r, idx, n: (r, 0, 0)),
            pl.BlockSpec(pairs_t.shape, lambda r, idx, n: (0, 0, 0)),
        ],
        out_specs=pl.BlockSpec((1, map_count, 2 * mode_count), lambda r, idx, n: (r, 0, 0)),
        scratch_shapes=[pltpu.VMEM((map_count, 4096), jnp.bfloat16)],
    )
    back = pl.pallas_call(
        noise_kernel,
        grid_spec=grid_spec,
        out_shape=jax.ShapeDtypeStruct((cycle_count, map_count, 2 * mode_count), jnp.bfloat16),
    )(indices, lengths, coeff_t, tables, pairs_t)
    return (
        back.reshape(cycle_count, map_count, 2, mode_count)
        .transpose(0, 3, 2, 1)
        .reshape(cycle_count, mode_count, columns)
    )


def shards(
    solution,
    residual,
    direction,
    legendre,
    prior_inv,
    noise_mats,
    noise_index,
    cycle_lengths,
    m_values,
    cut_pattern,
):
    band_count = lax.axis_size("band")
    mode_local, cycle_total, l_local = legendre.shape
    map_count = direction.shape[1]
    columns = 2 * map_count
    band_rows = cycle_total // band_count
    weight = L / (cycle_total * RLEN)
    rounded = direction.astype(jnp.bfloat16).reshape(columns, mode_local, l_local)

    def row_mask(first_row, row_count):
        block_flags = lax.dynamic_slice_in_dim(cut_pattern, first_row // RB, row_count // RB, 1)
        return jnp.repeat(block_flags, RB, axis=1).T

    section = legendre
    products = jnp.einsum("mrl,nml->rmn", section, rounded, preferred_element_type=jnp.float32)
    masked_products = products * row_mask(jnp.int32(0), cycle_total).astype(jnp.float32)[:, :, None]
    coeffs = gather_cycles(masked_products.reshape(cycle_total, columns), band_count).astype(jnp.bfloat16)
    cycle_local = coeffs.shape[0]
    mode_total = coeffs.shape[1]
    outputs = cycle_transform(coeffs, cycle_lengths, noise_index, m_values, noise_mats, weight)
    backward = outputs.reshape(cycle_local, mode_total, columns)
    returned = spread_cycles(backward, band_count)
    masked = returned * row_mask(jnp.int32(0), cycle_total).astype(jnp.bfloat16)
    image_data = lax.optimization_barrier(
        jnp.einsum("rl,rn->nl", legendre[0], masked, preferred_element_type=jnp.float32)
    )
    image_data = image_data.reshape(2, map_count, mode_local, l_local)
    image_field = prior_inv[None, None, None, :] * direction + image_data
    norm_now, curvature, cross, image_norm = total_over_mesh(
        jnp.stack(
            [
                jnp.sum(residual * residual, axis=(0, 2, 3)),
                jnp.sum(direction * image_field, axis=(0, 2, 3)),
                jnp.sum(residual * image_field, axis=(0, 2, 3)),
                jnp.sum(image_field * image_field, axis=(0, 2, 3)),
            ]
        )
    )
    step_size = norm_now / curvature
    new_residual = residual - step_size[None, :, None, None] * image_field
    norm_next = norm_now - 2.0 * step_size * cross + step_size * step_size * image_norm
    growth = norm_next / norm_now
    new_solution = solution + step_size[None, :, None, None] * direction
    new_direction = new_residual + growth[None, :, None, None] * direction
    return (new_solution, new_residual, new_direction)


def solution(mesh):
    in_specs = (
        P(None, None, "mgrp", "band"),
        P(None, None, "mgrp", "band"),
        P(None, None, "mgrp", "band"),
        P("mgrp", None, "band"),
        P("band"),
        P(),
        P(("band", "mgrp"), None),
        P(("band", "mgrp")),
        P(),
        P("mgrp", None),
    )
    out_specs = (
        P(None, None, "mgrp", "band"),
        P(None, None, "mgrp", "band"),
        P(None, None, "mgrp", "band"),
    )
    return jax.shard_map(shards, mesh=mesh, in_specs=in_specs, out_specs=out_specs, check_vma=False)
```

```python
import functools
import math

import jax
import jax.numpy as jnp
from jax import lax
from jax.experimental import pallas as pl
from jax.experimental.pallas import tpu as pltpu
from jax.sharding import PartitionSpec as P

L = 8192
RLEN = 16384
BLK = 64
RB = 64


MESH_AXES = ("mgrp", "band")


def total_over_mesh(values):
    count = lax.axis_size(MESH_AXES)
    copies = jnp.broadcast_to(values[None], (count,) + values.shape)
    return jnp.sum(lax.all_to_all(copies, MESH_AXES, 0, 0, tiled=True), axis=0)


def gather_cycles(partials, band_count):
    cycle_total, columns = partials.shape
    group_count = lax.axis_size("mgrp")
    own = cycle_total // (band_count * group_count)
    pieces = partials.reshape(band_count, group_count, own, columns).transpose(1, 0, 2, 3)
    pieces = pieces.reshape(group_count * band_count, own, columns)
    received = lax.all_to_all(pieces, MESH_AXES, 0, 0, tiled=True)
    received = received.reshape(group_count, band_count, own, columns)
    return jnp.sum(received, axis=1).transpose(1, 0, 2)


def spread_cycles(backward, band_count):
    own, group_count, columns = backward.shape
    pieces = jnp.broadcast_to(
        backward.transpose(1, 0, 2)[:, None], (group_count, band_count, own, columns)
    ).reshape(group_count * band_count, own, columns)
    received = lax.all_to_all(pieces, MESH_AXES, 0, 0, tiled=True)
    received = received.reshape(group_count, band_count, own, columns).transpose(1, 0, 2, 3)
    return received.reshape(band_count * group_count * own, columns)


def cycle_tables(m_values, lengths, pixels):
    high_count = pixels // 128
    coarse = jnp.arange(high_count, dtype=jnp.int32) * 128
    fine = jnp.arange(128, dtype=jnp.int32)
    cycle_size = lengths[:, None, None].astype(jnp.float32)
    phase_high = m_values[None, :, None] * coarse[None, None, :] % lengths[:, None, None]
    phase_low = m_values[None, :, None] * fine[None, None, :] % lengths[:, None, None]
    angle_high = 2.0 * math.pi * phase_high.astype(jnp.float32) / cycle_size
    angle_low = 2.0 * math.pi * phase_low.astype(jnp.float32) / cycle_size
    cos_high = jnp.cos(angle_high)[:, :, :, None]
    sin_high = jnp.sin(angle_high)[:, :, :, None]
    cos_low = jnp.cos(angle_low)[:, :, None, :]
    sin_low = jnp.sin(angle_low)[:, :, None, :]
    cycle_count = lengths.shape[0]
    mode_count = m_values.shape[0]
    cos_full = (cos_high * cos_low - sin_high * sin_low).reshape(cycle_count, mode_count, pixels)
    sin_full = (sin_high * cos_low + cos_high * sin_low).reshape(cycle_count, mode_count, pixels)
    column = jnp.arange(pixels, dtype=jnp.int32)
    factor = jnp.where(m_values == 0, 1.0, 2.0).astype(jnp.float32)[None, :, None]
    inside = (column[None, None, :] < lengths[:, None, None]).astype(jnp.float32)
    cosine = factor * cos_full * inside
    sine_part = -factor * sin_full * inside
    return jnp.stack([cosine, sine_part], axis=1).astype(jnp.bfloat16)


def pair_table(noise_mats):
    kinds = noise_mats.shape[0]
    first = jnp.broadcast_to(noise_mats[:, None], (kinds, kinds, BLK, BLK))
    second = jnp.broadcast_to(noise_mats[None, :], (kinds, kinds, BLK, BLK))
    empty = jnp.zeros((kinds, kinds, BLK, BLK), noise_mats.dtype)
    upper = jnp.concatenate([first, empty], axis=3)
    lower = jnp.concatenate([empty, second], axis=3)
    return jnp.concatenate([upper, lower], axis=2).reshape(kinds * kinds, 2 * BLK, 2 * BLK)


def cycle_segment(coeffs, lengths, indices, m_values, pairs, kinds, weight):
    cycle_count, mode_count, columns = coeffs.shape
    map_count = columns // 2
    tables = cycle_tables(m_values, lengths, RLEN)
    split_coeffs = coeffs.reshape(cycle_count, mode_count, 2, map_count)
    sky_map = jnp.einsum(
        "rmcb,rcmk->rbk", split_coeffs, tables, preferred_element_type=jnp.float32
    ).astype(jnp.bfloat16)
    pair_count = RLEN // (2 * BLK)
    kind_pairs = indices.reshape(cycle_count, pair_count, 2)
    pair_index = kind_pairs[:, :, 0] * kinds + kind_pairs[:, :, 1]
    matrices = pairs.reshape(kinds * kinds, 4 * BLK * BLK)[pair_index].reshape(
        cycle_count, pair_count, 2 * BLK, 2 * BLK
    )
    blocked = sky_map.reshape(cycle_count, map_count, pair_count, 2 * BLK)
    noisy_map = weight * jnp.einsum(
        "rbqj,rqij->rbqi", blocked, matrices, preferred_element_type=jnp.float32
    )
    noisy_map = noisy_map.reshape(cycle_count, map_count, RLEN).astype(jnp.bfloat16)
    backward = jnp.einsum("rbk,rcmk->rmcb", noisy_map, tables, preferred_element_type=jnp.float32)
    return backward.reshape(cycle_count, mode_count, columns).astype(jnp.bfloat16)


def noise_kernel(index_ref, length_ref, coeff_ref, table_ref, pair_ref, back_ref, noisy_ref):
    cycle = pl.program_id(0)
    wide = noisy_ref.shape[1]
    pair_width = 2 * BLK
    coeff = coeff_ref[0]
    side = int(round(pair_ref.shape[0] ** 0.5))

    def chunk(start, span, total):
        table = table_ref[0, :, pl.ds(start, span)]
        sky = jnp.dot(coeff, table, preferred_element_type=jnp.float32).astype(jnp.bfloat16)
        for inner in range(span // pair_width):
            block = (start + inner * pair_width) // BLK
            pick = index_ref[cycle, block] * side + index_ref[cycle, block + 1]
            noisy = jnp.dot(
                sky[:, inner * pair_width:(inner + 1) * pair_width],
                pair_ref[pick],
                preferred_element_type=jnp.float32,
            )
            noisy_ref[:, inner * pair_width:(inner + 1) * pair_width] = noisy.astype(jnp.bfloat16)
        return total + lax.dot_general(
            noisy_ref[:, :span], table, (((1,), (1,)), ((), ())), preferred_element_type=jnp.float32
        )

    length = length_ref[cycle]
    mid = wide // 2
    narrow = wide // 4
    full = length // wide
    rest = length - full * wide
    wide_count = full + (rest > mid + narrow).astype(jnp.int32)
    mid_count = ((rest > narrow) & (rest <= mid + narrow)).astype(jnp.int32)
    narrow_count = (((rest > 0) & (rest <= narrow)) | ((rest > mid) & (rest <= mid + narrow))).astype(jnp.int32)
    total = lax.fori_loop(
        0,
        wide_count,
        lambda step, acc: chunk(pl.multiple_of(step * wide, wide), wide, acc),
        jnp.zeros(back_ref.shape[1:], jnp.float32),
    )
    total = lax.fori_loop(
        0,
        mid_count,
        lambda step, acc: chunk(pl.multiple_of(full * wide, wide), mid, acc),
        total,
    )
    total = lax.fori_loop(
        0,
        narrow_count,
        lambda step, acc: chunk(pl.multiple_of(full * wide + mid_count * mid, mid), narrow, acc),
        total,
    )
    back_ref[0] = total.astype(back_ref.dtype)


def cycle_transform(coeffs, lengths, indices, m_values, noise_mats, weight):
    cycle_count, mode_count, columns = coeffs.shape
    map_count = columns // 2
    kinds = noise_mats.shape[0]
    tables = cycle_tables(m_values, lengths, RLEN).reshape(cycle_count, 2 * mode_count, RLEN)
    coeff_t = (
        coeffs.reshape(cycle_count, mode_count, 2, map_count)
        .transpose(0, 3, 2, 1)
        .reshape(cycle_count, map_count, 2 * mode_count)
    )
    pairs_t = jnp.swapaxes(pair_table(noise_mats), 1, 2) * jnp.asarray(weight, jnp.bfloat16)
    grid_spec = pltpu.PrefetchScalarGridSpec(
        num_scalar_prefetch=2,
        grid=(cycle_count,),
        in_specs=[
            pl.BlockSpec((1, map_count, 2 * mode_count), lambda r, idx, n: (r, 0, 0)),
            pl.BlockSpec((1, 2 * mode_count, RLEN), lambda r, idx, n: (r, 0, 0)),
            pl.BlockSpec(pairs_t.shape, lambda r, idx, n: (0, 0, 0)),
        ],
        out_specs=pl.BlockSpec((1, map_count, 2 * mode_count), lambda r, idx, n: (r, 0, 0)),
        scratch_shapes=[pltpu.VMEM((map_count, 8192), jnp.bfloat16)],
    )
    back = pl.pallas_call(
        noise_kernel,
        grid_spec=grid_spec,
        out_shape=jax.ShapeDtypeStruct((cycle_count, map_count, 2 * mode_count), jnp.bfloat16),
    )(indices, lengths, coeff_t, tables, pairs_t)
    return (
        back.reshape(cycle_count, map_count, 2, mode_count)
        .transpose(0, 3, 2, 1)
        .reshape(cycle_count, mode_count, columns)
    )


def shards(
    solution,
    residual,
    direction,
    legendre,
    prior_inv,
    noise_mats,
    noise_index,
    cycle_lengths,
    m_values,
    cut_pattern,
):
    band_count = lax.axis_size("band")
    mode_local, cycle_total, l_local = legendre.shape
    map_count = direction.shape[1]
    columns = 2 * map_count
    band_rows = cycle_total // band_count
    weight = L / (cycle_total * RLEN)
    rounded = direction.astype(jnp.bfloat16).reshape(columns, mode_local, l_local)

    def row_mask(first_row, row_count):
        block_flags = lax.dynamic_slice_in_dim(cut_pattern, first_row // RB, row_count // RB, 1)
        return jnp.repeat(block_flags, RB, axis=1).T

    section = legendre
    products = jnp.einsum("mrl,nml->rmn", section, rounded, preferred_element_type=jnp.float32)
    masked_products = products * row_mask(jnp.int32(0), cycle_total).astype(jnp.float32)[:, :, None]
    coeffs = gather_cycles(masked_products.reshape(cycle_total, columns), band_count).astype(jnp.bfloat16)
    cycle_local = coeffs.shape[0]
    mode_total = coeffs.shape[1]
    outputs = cycle_transform(coeffs, cycle_lengths, noise_index, m_values, noise_mats, weight)
    backward = outputs.reshape(cycle_local, mode_total, columns)
    returned = spread_cycles(backward, band_count)
    masked = returned * row_mask(jnp.int32(0), cycle_total).astype(jnp.bfloat16)
    image_data = lax.optimization_barrier(
        jnp.einsum("rl,rn->nl", legendre[0], masked, preferred_element_type=jnp.float32)
    )
    image_data = image_data.reshape(2, map_count, mode_local, l_local)
    image_field = prior_inv[None, None, None, :] * direction + image_data
    norm_now, curvature, cross, image_norm = total_over_mesh(
        jnp.stack(
            [
                jnp.sum(residual * residual, axis=(0, 2, 3)),
                jnp.sum(direction * image_field, axis=(0, 2, 3)),
                jnp.sum(residual * image_field, axis=(0, 2, 3)),
                jnp.sum(image_field * image_field, axis=(0, 2, 3)),
            ]
        )
    )
    step_size = norm_now / curvature
    new_residual = residual - step_size[None, :, None, None] * image_field
    norm_next = norm_now - 2.0 * step_size * cross + step_size * step_size * image_norm
    growth = norm_next / norm_now
    new_solution = solution + step_size[None, :, None, None] * direction
    new_direction = new_residual + growth[None, :, None, None] * direction
    return (new_solution, new_residual, new_direction)


def solution(mesh):
    in_specs = (
        P(None, None, "mgrp", "band"),
        P(None, None, "mgrp", "band"),
        P(None, None, "mgrp", "band"),
        P("mgrp", None, "band"),
        P("band"),
        P(),
        P(("band", "mgrp"), None),
        P(("band", "mgrp")),
        P(),
        P("mgrp", None),
    )
    out_specs = (
        P(None, None, "mgrp", "band"),
        P(None, None, "mgrp", "band"),
        P(None, None, "mgrp", "band"),
    )
    return jax.shard_map(shards, mesh=mesh, in_specs=in_specs, out_specs=out_specs, check_vma=False)
```

```python
import functools
import math

import jax
import jax.numpy as jnp
from jax import lax
from jax.experimental import pallas as pl
from jax.experimental.pallas import tpu as pltpu
from jax.sharding import PartitionSpec as P

L = 8192
RLEN = 16384
BLK = 64
RB = 64


MESH_AXES = ("mgrp", "band")


def total_over_mesh(values):
    count = lax.axis_size(MESH_AXES)
    copies = jnp.broadcast_to(values[None], (count,) + values.shape)
    return jnp.sum(lax.all_to_all(copies, MESH_AXES, 0, 0, tiled=True), axis=0)


def gather_cycles(partials, band_count):
    cycle_total, columns = partials.shape
    group_count = lax.axis_size("mgrp")
    own = cycle_total // (band_count * group_count)
    pieces = partials.reshape(band_count, group_count, own, columns).transpose(1, 0, 2, 3)
    pieces = pieces.reshape(group_count * band_count, own, columns)
    received = lax.all_to_all(pieces, MESH_AXES, 0, 0, tiled=True)
    received = received.reshape(group_count, band_count, own, columns)
    return jnp.sum(received, axis=1).transpose(1, 0, 2)


def spread_cycles(backward, band_count):
    own, group_count, columns = backward.shape
    pieces = jnp.broadcast_to(
        backward.transpose(1, 0, 2)[:, None], (group_count, band_count, own, columns)
    ).reshape(group_count * band_count, own, columns)
    received = lax.all_to_all(pieces, MESH_AXES, 0, 0, tiled=True)
    received = received.reshape(group_count, band_count, own, columns).transpose(1, 0, 2, 3)
    return received.reshape(band_count * group_count * own, columns)


def cycle_tables(m_values, lengths, pixels):
    high_count = pixels // 128
    coarse = jnp.arange(high_count, dtype=jnp.int32) * 128
    fine = jnp.arange(128, dtype=jnp.int32)
    cycle_size = lengths[:, None, None].astype(jnp.float32)
    phase_high = m_values[None, :, None] * coarse[None, None, :] % lengths[:, None, None]
    phase_low = m_values[None, :, None] * fine[None, None, :] % lengths[:, None, None]
    angle_high = 2.0 * math.pi * phase_high.astype(jnp.float32) / cycle_size
    angle_low = 2.0 * math.pi * phase_low.astype(jnp.float32) / cycle_size
    cos_high = jnp.cos(angle_high)[:, :, :, None]
    sin_high = jnp.sin(angle_high)[:, :, :, None]
    cos_low = jnp.cos(angle_low)[:, :, None, :]
    sin_low = jnp.sin(angle_low)[:, :, None, :]
    cycle_count = lengths.shape[0]
    mode_count = m_values.shape[0]
    cos_full = (cos_high * cos_low - sin_high * sin_low).reshape(cycle_count, mode_count, pixels)
    sin_full = (sin_high * cos_low + cos_high * sin_low).reshape(cycle_count, mode_count, pixels)
    column = jnp.arange(pixels, dtype=jnp.int32)
    factor = jnp.where(m_values == 0, 1.0, 2.0).astype(jnp.float32)[None, :, None]
    inside = (column[None, None, :] < lengths[:, None, None]).astype(jnp.float32)
    cosine = factor * cos_full * inside
    sine_part = -factor * sin_full * inside
    return jnp.stack([cosine, sine_part], axis=1).astype(jnp.bfloat16)


def pair_table(noise_mats):
    kinds = noise_mats.shape[0]
    first = jnp.broadcast_to(noise_mats[:, None], (kinds, kinds, BLK, BLK))
    second = jnp.broadcast_to(noise_mats[None, :], (kinds, kinds, BLK, BLK))
    empty = jnp.zeros((kinds, kinds, BLK, BLK), noise_mats.dtype)
    upper = jnp.concatenate([first, empty], axis=3)
    lower = jnp.concatenate([empty, second], axis=3)
    return jnp.concatenate([upper, lower], axis=2).reshape(kinds * kinds, 2 * BLK, 2 * BLK)


def cycle_segment(coeffs, lengths, indices, m_values, pairs, kinds, weight):
    cycle_count, mode_count, columns = coeffs.shape
    map_count = columns // 2
    tables = cycle_tables(m_values, lengths, RLEN)
    split_coeffs = coeffs.reshape(cycle_count, mode_count, 2, map_count)
    sky_map = jnp.einsum(
        "rmcb,rcmk->rbk", split_coeffs, tables, preferred_element_type=jnp.float32
    ).astype(jnp.bfloat16)
    pair_count = RLEN // (2 * BLK)
    kind_pairs = indices.reshape(cycle_count, pair_count, 2)
    pair_index = kind_pairs[:, :, 0] * kinds + kind_pairs[:, :, 1]
    matrices = pairs.reshape(kinds * kinds, 4 * BLK * BLK)[pair_index].reshape(
        cycle_count, pair_count, 2 * BLK, 2 * BLK
    )
    blocked = sky_map.reshape(cycle_count, map_count, pair_count, 2 * BLK)
    noisy_map = weight * jnp.einsum(
        "rbqj,rqij->rbqi", blocked, matrices, preferred_element_type=jnp.float32
    )
    noisy_map = noisy_map.reshape(cycle_count, map_count, RLEN).astype(jnp.bfloat16)
    backward = jnp.einsum("rbk,rcmk->rmcb", noisy_map, tables, preferred_element_type=jnp.float32)
    return backward.reshape(cycle_count, mode_count, columns).astype(jnp.bfloat16)


def noise_kernel(index_ref, length_ref, coeff_ref, table_ref, pair_ref, back_ref, noisy_ref):
    cycle = pl.program_id(0)
    wide = noisy_ref.shape[1]
    pair_width = 2 * BLK
    coeff = coeff_ref[0]
    side = int(round(pair_ref.shape[0] ** 0.5))

    def chunk(start, span, total):
        table = table_ref[0, :, pl.ds(start, span)]
        sky = jnp.dot(coeff, table, preferred_element_type=jnp.float32).astype(jnp.bfloat16)
        for inner in range(span // pair_width):
            block = (start + inner * pair_width) // BLK
            pick = index_ref[cycle, block] * side + index_ref[cycle, block + 1]
            noisy = jnp.dot(
                sky[:, inner * pair_width:(inner + 1) * pair_width],
                pair_ref[pick],
                preferred_element_type=jnp.float32,
            )
            noisy_ref[:, inner * pair_width:(inner + 1) * pair_width] = noisy.astype(jnp.bfloat16)
        return total + lax.dot_general(
            noisy_ref[:, :span], table, (((1,), (1,)), ((), ())), preferred_element_type=jnp.float32
        )

    length = length_ref[cycle]
    mid = wide // 2
    narrow = wide // 4
    full = length // wide
    rest = length - full * wide
    wide_count = full + (rest > mid + narrow).astype(jnp.int32)
    mid_count = ((rest > narrow) & (rest <= mid + narrow)).astype(jnp.int32)
    narrow_count = (((rest > 0) & (rest <= narrow)) | ((rest > mid) & (rest <= mid + narrow))).astype(jnp.int32)
    total = lax.fori_loop(
        0,
        wide_count,
        lambda step, acc: chunk(pl.multiple_of(step * wide, wide), wide, acc),
        jnp.zeros(back_ref.shape[1:], jnp.float32),
    )
    total = lax.fori_loop(
        0,
        mid_count,
        lambda step, acc: chunk(pl.multiple_of(full * wide, wide), mid, acc),
        total,
    )
    total = lax.fori_loop(
        0,
        narrow_count,
        lambda step, acc: chunk(pl.multiple_of(full * wide + mid_count * mid, mid), narrow, acc),
        total,
    )
    back_ref[0] = total.astype(back_ref.dtype)


def cycle_transform(coeffs, lengths, indices, m_values, noise_mats, weight):
    cycle_count, mode_count, columns = coeffs.shape
    map_count = columns // 2
    kinds = noise_mats.shape[0]
    tables = cycle_tables(m_values, lengths, RLEN).reshape(cycle_count, 2 * mode_count, RLEN)
    coeff_t = (
        coeffs.reshape(cycle_count, mode_count, 2, map_count)
        .transpose(0, 3, 2, 1)
        .reshape(cycle_count, map_count, 2 * mode_count)
    )
    pairs_t = jnp.swapaxes(pair_table(noise_mats), 1, 2) * jnp.asarray(weight, jnp.bfloat16)
    grid_spec = pltpu.PrefetchScalarGridSpec(
        num_scalar_prefetch=2,
        grid=(cycle_count,),
        in_specs=[
            pl.BlockSpec((1, map_count, 2 * mode_count), lambda r, idx, n: (r, 0, 0)),
            pl.BlockSpec((1, 2 * mode_count, RLEN), lambda r, idx, n: (r, 0, 0)),
            pl.BlockSpec(memory_space=pltpu.MemorySpace.VMEM),
        ],
        out_specs=pl.BlockSpec((1, map_count, 2 * mode_count), lambda r, idx, n: (r, 0, 0)),
        scratch_shapes=[pltpu.VMEM((map_count, 8192), jnp.bfloat16)],
    )
    back = pl.pallas_call(
        noise_kernel,
        grid_spec=grid_spec,
        out_shape=jax.ShapeDtypeStruct((cycle_count, map_count, 2 * mode_count), jnp.bfloat16),
    )(indices, lengths, coeff_t, tables, pairs_t)
    return (
        back.reshape(cycle_count, map_count, 2, mode_count)
        .transpose(0, 3, 2, 1)
        .reshape(cycle_count, mode_count, columns)
    )


def shards(
    solution,
    residual,
    direction,
    legendre,
    prior_inv,
    noise_mats,
    noise_index,
    cycle_lengths,
    m_values,
    cut_pattern,
):
    band_count = lax.axis_size("band")
    mode_local, cycle_total, l_local = legendre.shape
    map_count = direction.shape[1]
    columns = 2 * map_count
    band_rows = cycle_total // band_count
    weight = L / (cycle_total * RLEN)
    rounded = direction.astype(jnp.bfloat16).reshape(columns, mode_local, l_local)

    def row_mask(first_row, row_count):
        block_flags = lax.dynamic_slice_in_dim(cut_pattern, first_row // RB, row_count // RB, 1)
        return jnp.repeat(block_flags, RB, axis=1).T

    section = legendre
    products = jnp.einsum("mrl,nml->rmn", section, rounded, preferred_element_type=jnp.float32)
    masked_products = products * row_mask(jnp.int32(0), cycle_total).astype(jnp.float32)[:, :, None]
    coeffs = gather_cycles(masked_products.reshape(cycle_total, columns), band_count).astype(jnp.bfloat16)
    cycle_local = coeffs.shape[0]
    mode_total = coeffs.shape[1]
    outputs = cycle_transform(coeffs, cycle_lengths, noise_index, m_values, noise_mats, weight)
    backward = outputs.reshape(cycle_local, mode_total, columns)
    returned = spread_cycles(backward, band_count)
    masked = returned * row_mask(jnp.int32(0), cycle_total).astype(jnp.bfloat16)
    image_data = lax.optimization_barrier(
        jnp.einsum("rl,rn->nl", legendre[0], masked, preferred_element_type=jnp.float32)
    )
    image_data = image_data.reshape(2, map_count, mode_local, l_local)
    image_field = prior_inv[None, None, None, :] * direction + image_data
    norm_now, curvature, cross, image_norm = total_over_mesh(
        jnp.stack(
            [
                jnp.sum(residual * residual, axis=(0, 2, 3)),
                jnp.sum(direction * image_field, axis=(0, 2, 3)),
                jnp.sum(residual * image_field, axis=(0, 2, 3)),
                jnp.sum(image_field * image_field, axis=(0, 2, 3)),
            ]
        )
    )
    step_size = norm_now / curvature
    new_residual = residual - step_size[None, :, None, None] * image_field
    norm_next = norm_now - 2.0 * step_size * cross + step_size * step_size * image_norm
    growth = norm_next / norm_now
    new_solution = solution + step_size[None, :, None, None] * direction
    new_direction = new_residual + growth[None, :, None, None] * direction
    return (new_solution, new_residual, new_direction)


def solution(mesh):
    in_specs = (
        P(None, None, "mgrp", "band"),
        P(None, None, "mgrp", "band"),
        P(None, None, "mgrp", "band"),
        P("mgrp", None, "band"),
        P("band"),
        P(),
        P(("band", "mgrp"), None),
        P(("band", "mgrp")),
        P(),
        P("mgrp", None),
    )
    out_specs = (
        P(None, None, "mgrp", "band"),
        P(None, None, "mgrp", "band"),
        P(None, None, "mgrp", "band"),
    )
    return jax.shard_map(shards, mesh=mesh, in_specs=in_specs, out_specs=out_specs, check_vma=False)
```

```python
import functools
import math

import jax
import jax.numpy as jnp
from jax import lax
from jax.experimental import pallas as pl
from jax.experimental.pallas import tpu as pltpu
from jax.sharding import PartitionSpec as P

L = 8192
RLEN = 16384
BLK = 64
RB = 64


MESH_AXES = ("mgrp", "band")


def total_over_mesh(values):
    count = lax.axis_size(MESH_AXES)
    copies = jnp.broadcast_to(values[None], (count,) + values.shape)
    return jnp.sum(lax.all_to_all(copies, MESH_AXES, 0, 0, tiled=True), axis=0)


def gather_cycles(partials, band_count):
    cycle_total, columns = partials.shape
    group_count = lax.axis_size("mgrp")
    own = cycle_total // (band_count * group_count)
    pieces = partials.reshape(group_count * band_count, own, columns)
    received = lax.all_to_all(pieces, MESH_AXES, 0, 0, tiled=True)
    received = received.reshape(group_count, band_count, own, columns)
    return jnp.sum(received, axis=1).transpose(1, 0, 2)


def forward_kernel(cut_ref, leg_ref, dir_ref, out_ref, *, band_count, group_count):
    cycle_total = leg_ref.shape[0]
    own = cycle_total // (band_count * group_count)
    rounded = dir_ref[...].astype(jnp.bfloat16)
    products = lax.dot_general(
        leg_ref[...], rounded, (((1,), (1,)), ((), ())), preferred_element_type=jnp.float32
    )
    for band in range(band_count):
        for group in range(group_count):
            first = (band * group_count + group) * own
            target = (group * band_count + band) * own
            keep = cut_ref[0, first // RB] != 0
            out_ref[target:target + own, :] = jnp.where(keep, products[first:first + own], 0.0)


def forward_products(cut_pattern, legendre, direction, band_count):
    cycle_total, l_local = legendre.shape[1], legendre.shape[2]
    columns = direction.shape[0] * direction.shape[1]
    return pl.pallas_call(
        functools.partial(
            forward_kernel, band_count=band_count, group_count=lax.axis_size("mgrp")
        ),
        in_specs=[
            pl.BlockSpec(memory_space=pltpu.MemorySpace.SMEM),
            pl.BlockSpec(memory_space=pltpu.MemorySpace.VMEM),
            pl.BlockSpec(memory_space=pltpu.MemorySpace.VMEM),
        ],
        out_specs=pl.BlockSpec(memory_space=pltpu.MemorySpace.VMEM),
        out_shape=jax.ShapeDtypeStruct((cycle_total, columns), jnp.float32),
    )(cut_pattern, legendre[0], direction.reshape(columns, l_local))


def spread_cycles(backward, band_count):
    own, group_count, columns = backward.shape
    pieces = jnp.broadcast_to(
        backward.transpose(1, 0, 2)[:, None], (group_count, band_count, own, columns)
    ).reshape(group_count * band_count, own, columns)
    received = lax.all_to_all(pieces, MESH_AXES, 0, 0, tiled=True)
    received = received.reshape(group_count, band_count, own, columns).transpose(1, 0, 2, 3)
    return received.reshape(band_count * group_count * own, columns)


def cycle_tables(m_values, lengths, pixels):
    high_count = pixels // 128
    coarse = jnp.arange(high_count, dtype=jnp.int32) * 128
    fine = jnp.arange(128, dtype=jnp.int32)
    cycle_size = lengths[:, None, None].astype(jnp.float32)
    phase_high = m_values[None, :, None] * coarse[None, None, :] % lengths[:, None, None]
    phase_low = m_values[None, :, None] * fine[None, None, :] % lengths[:, None, None]
    angle_high = 2.0 * math.pi * phase_high.astype(jnp.float32) / cycle_size
    angle_low = 2.0 * math.pi * phase_low.astype(jnp.float32) / cycle_size
    cos_high = jnp.cos(angle_high)[:, :, :, None]
    sin_high = jnp.sin(angle_high)[:, :, :, None]
    cos_low = jnp.cos(angle_low)[:, :, None, :]
    sin_low = jnp.sin(angle_low)[:, :, None, :]
    cycle_count = lengths.shape[0]
    mode_count = m_values.shape[0]
    cos_full = (cos_high * cos_low - sin_high * sin_low).reshape(cycle_count, mode_count, pixels)
    sin_full = (sin_high * cos_low + cos_high * sin_low).reshape(cycle_count, mode_count, pixels)
    column = jnp.arange(pixels, dtype=jnp.int32)
    factor = jnp.where(m_values == 0, 1.0, 2.0).astype(jnp.float32)[None, :, None]
    inside = (column[None, None, :] < lengths[:, None, None]).astype(jnp.float32)
    cosine = factor * cos_full * inside
    sine_part = -factor * sin_full * inside
    return jnp.stack([cosine, sine_part], axis=1).astype(jnp.bfloat16)


def pair_table(noise_mats):
    kinds = noise_mats.shape[0]
    first = jnp.broadcast_to(noise_mats[:, None], (kinds, kinds, BLK, BLK))
    second = jnp.broadcast_to(noise_mats[None, :], (kinds, kinds, BLK, BLK))
    empty = jnp.zeros((kinds, kinds, BLK, BLK), noise_mats.dtype)
    upper = jnp.concatenate([first, empty], axis=3)
    lower = jnp.concatenate([empty, second], axis=3)
    return jnp.concatenate([upper, lower], axis=2).reshape(kinds * kinds, 2 * BLK, 2 * BLK)


def cycle_segment(coeffs, lengths, indices, m_values, pairs, kinds, weight):
    cycle_count, mode_count, columns = coeffs.shape
    map_count = columns // 2
    tables = cycle_tables(m_values, lengths, RLEN)
    split_coeffs = coeffs.reshape(cycle_count, mode_count, 2, map_count)
    sky_map = jnp.einsum(
        "rmcb,rcmk->rbk", split_coeffs, tables, preferred_element_type=jnp.float32
    ).astype(jnp.bfloat16)
    pair_count = RLEN // (2 * BLK)
    kind_pairs = indices.reshape(cycle_count, pair_count, 2)
    pair_index = kind_pairs[:, :, 0] * kinds + kind_pairs[:, :, 1]
    matrices = pairs.reshape(kinds * kinds, 4 * BLK * BLK)[pair_index].reshape(
        cycle_count, pair_count, 2 * BLK, 2 * BLK
    )
    blocked = sky_map.reshape(cycle_count, map_count, pair_count, 2 * BLK)
    noisy_map = weight * jnp.einsum(
        "rbqj,rqij->rbqi", blocked, matrices, preferred_element_type=jnp.float32
    )
    noisy_map = noisy_map.reshape(cycle_count, map_count, RLEN).astype(jnp.bfloat16)
    backward = jnp.einsum("rbk,rcmk->rmcb", noisy_map, tables, preferred_element_type=jnp.float32)
    return backward.reshape(cycle_count, mode_count, columns).astype(jnp.bfloat16)


def noise_kernel(index_ref, length_ref, coeff_ref, table_ref, pair_ref, back_ref, noisy_ref):
    cycle = pl.program_id(0)
    wide = noisy_ref.shape[1]
    pair_width = 2 * BLK
    coeff = coeff_ref[0]
    side = int(round(pair_ref.shape[0] ** 0.5))

    def chunk(start, span, total):
        table = table_ref[0, :, pl.ds(start, span)]
        sky = jnp.dot(coeff, table, preferred_element_type=jnp.float32).astype(jnp.bfloat16)
        for inner in range(span // pair_width):
            block = (start + inner * pair_width) // BLK
            pick = index_ref[cycle, block] * side + index_ref[cycle, block + 1]
            noisy = jnp.dot(
                sky[:, inner * pair_width:(inner + 1) * pair_width],
                pair_ref[pick],
                preferred_element_type=jnp.float32,
            )
            noisy_ref[:, inner * pair_width:(inner + 1) * pair_width] = noisy.astype(jnp.bfloat16)
        return total + lax.dot_general(
            noisy_ref[:, :span], table, (((1,), (1,)), ((), ())), preferred_element_type=jnp.float32
        )

    length = length_ref[cycle]
    mid = wide // 2
    narrow = wide // 4
    full = length // wide
    rest = length - full * wide
    wide_count = full + (rest > mid + narrow).astype(jnp.int32)
    mid_count = ((rest > narrow) & (rest <= mid + narrow)).astype(jnp.int32)
    narrow_count = (((rest > 0) & (rest <= narrow)) | ((rest > mid) & (rest <= mid + narrow))).astype(jnp.int32)
    total = lax.fori_loop(
        0,
        wide_count,
        lambda step, acc: chunk(pl.multiple_of(step * wide, wide), wide, acc),
        jnp.zeros(back_ref.shape[1:], jnp.float32),
    )
    total = lax.fori_loop(
        0,
        mid_count,
        lambda step, acc: chunk(pl.multiple_of(full * wide, wide), mid, acc),
        total,
    )
    total = lax.fori_loop(
        0,
        narrow_count,
        lambda step, acc: chunk(pl.multiple_of(full * wide + mid_count * mid, mid), narrow, acc),
        total,
    )
    back_ref[0] = total.astype(back_ref.dtype)


def cycle_transform(coeffs, lengths, indices, m_values, noise_mats, weight):
    cycle_count, mode_count, columns = coeffs.shape
    map_count = columns // 2
    kinds = noise_mats.shape[0]
    tables = cycle_tables(m_values, lengths, RLEN).reshape(cycle_count, 2 * mode_count, RLEN)
    coeff_t = (
        coeffs.reshape(cycle_count, mode_count, 2, map_count)
        .transpose(0, 3, 2, 1)
        .reshape(cycle_count, map_count, 2 * mode_count)
    )
    pairs_t = jnp.swapaxes(pair_table(noise_mats), 1, 2) * jnp.asarray(weight, jnp.bfloat16)
    grid_spec = pltpu.PrefetchScalarGridSpec(
        num_scalar_prefetch=2,
        grid=(cycle_count,),
        in_specs=[
            pl.BlockSpec((1, map_count, 2 * mode_count), lambda r, idx, n: (r, 0, 0)),
            pl.BlockSpec((1, 2 * mode_count, RLEN), lambda r, idx, n: (r, 0, 0)),
            pl.BlockSpec(pairs_t.shape, lambda r, idx, n: (0, 0, 0)),
        ],
        out_specs=pl.BlockSpec((1, map_count, 2 * mode_count), lambda r, idx, n: (r, 0, 0)),
        scratch_shapes=[pltpu.VMEM((map_count, 8192), jnp.bfloat16)],
    )
    back = pl.pallas_call(
        noise_kernel,
        grid_spec=grid_spec,
        out_shape=jax.ShapeDtypeStruct((cycle_count, map_count, 2 * mode_count), jnp.bfloat16),
    )(indices, lengths, coeff_t, tables, pairs_t)
    return (
        back.reshape(cycle_count, map_count, 2, mode_count)
        .transpose(0, 3, 2, 1)
        .reshape(cycle_count, mode_count, columns)
    )


def shards(
    solution,
    residual,
    direction,
    legendre,
    prior_inv,
    noise_mats,
    noise_index,
    cycle_lengths,
    m_values,
    cut_pattern,
):
    band_count = lax.axis_size("band")
    mode_local, cycle_total, l_local = legendre.shape
    map_count = direction.shape[1]
    columns = 2 * map_count
    band_rows = cycle_total // band_count
    weight = L / (cycle_total * RLEN)

    def row_mask(first_row, row_count):
        block_flags = lax.dynamic_slice_in_dim(cut_pattern, first_row // RB, row_count // RB, 1)
        return jnp.repeat(block_flags, RB, axis=1).T

    masked_products = forward_products(cut_pattern, legendre, direction, band_count)
    coeffs = gather_cycles(masked_products, band_count).astype(jnp.bfloat16)
    cycle_local = coeffs.shape[0]
    mode_total = coeffs.shape[1]
    outputs = cycle_transform(coeffs, cycle_lengths, noise_index, m_values, noise_mats, weight)
    backward = outputs.reshape(cycle_local, mode_total, columns)
    returned = spread_cycles(backward, band_count)
    masked = returned * row_mask(jnp.int32(0), cycle_total).astype(jnp.bfloat16)
    image_data = lax.optimization_barrier(
        jnp.einsum("rl,rn->nl", legendre[0], masked, preferred_element_type=jnp.float32)
    )
    image_data = image_data.reshape(2, map_count, mode_local, l_local)
    image_field = prior_inv[None, None, None, :] * direction + image_data
    norm_now, curvature, cross, image_norm = total_over_mesh(
        jnp.stack(
            [
                jnp.sum(residual * residual, axis=(0, 2, 3)),
                jnp.sum(direction * image_field, axis=(0, 2, 3)),
                jnp.sum(residual * image_field, axis=(0, 2, 3)),
                jnp.sum(image_field * image_field, axis=(0, 2, 3)),
            ]
        )
    )
    step_size = norm_now / curvature
    new_residual = residual - step_size[None, :, None, None] * image_field
    norm_next = norm_now - 2.0 * step_size * cross + step_size * step_size * image_norm
    growth = norm_next / norm_now
    new_solution = solution + step_size[None, :, None, None] * direction
    new_direction = new_residual + growth[None, :, None, None] * direction
    return (new_solution, new_residual, new_direction)


def solution(mesh):
    in_specs = (
        P(None, None, "mgrp", "band"),
        P(None, None, "mgrp", "band"),
        P(None, None, "mgrp", "band"),
        P("mgrp", None, "band"),
        P("band"),
        P(),
        P(("band", "mgrp"), None),
        P(("band", "mgrp")),
        P(),
        P("mgrp", None),
    )
    out_specs = (
        P(None, None, "mgrp", "band"),
        P(None, None, "mgrp", "band"),
        P(None, None, "mgrp", "band"),
    )
    return jax.shard_map(shards, mesh=mesh, in_specs=in_specs, out_specs=out_specs, check_vma=False)
```

```python
import functools
import math

import jax
import jax.numpy as jnp
from jax import lax
from jax.experimental import pallas as pl
from jax.experimental.pallas import tpu as pltpu
from jax.sharding import PartitionSpec as P

L = 8192
RLEN = 16384
BLK = 64
RB = 64


MESH_AXES = ("mgrp", "band")


def total_over_mesh(values):
    count = lax.axis_size(MESH_AXES)
    copies = jnp.broadcast_to(values[None], (count,) + values.shape)
    return jnp.sum(lax.all_to_all(copies, MESH_AXES, 0, 0, tiled=True), axis=0)


def gather_cycles(partials, band_count):
    cycle_total, columns = partials.shape
    group_count = lax.axis_size("mgrp")
    own = cycle_total // (band_count * group_count)
    pieces = partials.reshape(band_count, group_count, own, columns).transpose(1, 0, 2, 3)
    pieces = pieces.reshape(group_count * band_count, own, columns)
    received = lax.all_to_all(pieces, MESH_AXES, 0, 0, tiled=True)
    received = received.reshape(group_count, band_count, own, columns)
    return jnp.sum(received, axis=1).transpose(1, 0, 2)


def spread_cycles(backward, band_count):
    own, group_count, columns = backward.shape
    pieces = jnp.broadcast_to(
        backward.transpose(1, 0, 2)[:, None], (group_count, band_count, own, columns)
    ).reshape(group_count * band_count, own, columns)
    received = lax.all_to_all(pieces, MESH_AXES, 0, 0, tiled=True)
    received = received.reshape(group_count, band_count, own, columns).transpose(1, 0, 2, 3)
    return received.reshape(band_count * group_count * own, columns)


def cycle_tables(m_values, lengths, pixels):
    high_count = pixels // 128
    coarse = jnp.arange(high_count, dtype=jnp.int32) * 128
    fine = jnp.arange(128, dtype=jnp.int32)
    cycle_size = lengths[:, None, None].astype(jnp.float32)
    phase_high = m_values[None, :, None] * coarse[None, None, :] % lengths[:, None, None]
    phase_low = m_values[None, :, None] * fine[None, None, :] % lengths[:, None, None]
    angle_high = 2.0 * math.pi * phase_high.astype(jnp.float32) / cycle_size
    angle_low = 2.0 * math.pi * phase_low.astype(jnp.float32) / cycle_size
    cos_high = jnp.cos(angle_high)[:, :, :, None]
    sin_high = jnp.sin(angle_high)[:, :, :, None]
    cos_low = jnp.cos(angle_low)[:, :, None, :]
    sin_low = jnp.sin(angle_low)[:, :, None, :]
    cycle_count = lengths.shape[0]
    mode_count = m_values.shape[0]
    cos_full = (cos_high * cos_low - sin_high * sin_low).reshape(cycle_count, mode_count, pixels)
    sin_full = (sin_high * cos_low + cos_high * sin_low).reshape(cycle_count, mode_count, pixels)
    column = jnp.arange(pixels, dtype=jnp.int32)
    factor = jnp.where(m_values == 0, 1.0, 2.0).astype(jnp.float32)[None, :, None]
    inside = (column[None, None, :] < lengths[:, None, None]).astype(jnp.float32)
    cosine = factor * cos_full * inside
    sine_part = -factor * sin_full * inside
    return jnp.stack([cosine, sine_part], axis=1).astype(jnp.bfloat16)


def pair_table(noise_mats):
    kinds = noise_mats.shape[0]
    first = jnp.broadcast_to(noise_mats[:, None], (kinds, kinds, BLK, BLK))
    second = jnp.broadcast_to(noise_mats[None, :], (kinds, kinds, BLK, BLK))
    empty = jnp.zeros((kinds, kinds, BLK, BLK), noise_mats.dtype)
    upper = jnp.concatenate([first, empty], axis=3)
    lower = jnp.concatenate([empty, second], axis=3)
    return jnp.concatenate([upper, lower], axis=2).reshape(kinds * kinds, 2 * BLK, 2 * BLK)


def cycle_segment(coeffs, lengths, indices, m_values, pairs, kinds, weight):
    cycle_count, mode_count, columns = coeffs.shape
    map_count = columns // 2
    tables = cycle_tables(m_values, lengths, RLEN)
    split_coeffs = coeffs.reshape(cycle_count, mode_count, 2, map_count)
    sky_map = jnp.einsum(
        "rmcb,rcmk->rbk", split_coeffs, tables, preferred_element_type=jnp.float32
    ).astype(jnp.bfloat16)
    pair_count = RLEN // (2 * BLK)
    kind_pairs = indices.reshape(cycle_count, pair_count, 2)
    pair_index = kind_pairs[:, :, 0] * kinds + kind_pairs[:, :, 1]
    matrices = pairs.reshape(kinds * kinds, 4 * BLK * BLK)[pair_index].reshape(
        cycle_count, pair_count, 2 * BLK, 2 * BLK
    )
    blocked = sky_map.reshape(cycle_count, map_count, pair_count, 2 * BLK)
    noisy_map = weight * jnp.einsum(
        "rbqj,rqij->rbqi", blocked, matrices, preferred_element_type=jnp.float32
    )
    noisy_map = noisy_map.reshape(cycle_count, map_count, RLEN).astype(jnp.bfloat16)
    backward = jnp.einsum("rbk,rcmk->rmcb", noisy_map, tables, preferred_element_type=jnp.float32)
    return backward.reshape(cycle_count, mode_count, columns).astype(jnp.bfloat16)


def noise_kernel(index_ref, length_ref, coeff_ref, table_ref, pair_ref, back_ref, noisy_ref, quad_ref):
    cycle = pl.program_id(0)
    wide = noisy_ref.shape[1]
    pair_width = 2 * BLK
    coeff = coeff_ref[0]
    side = int(round(pair_ref.shape[0] ** 0.5))

    quad_width = 2 * pair_width
    slots = quad_ref.shape[0]
    zero = jnp.zeros((pair_width, pair_width), quad_ref.dtype)
    for slot in range(slots):
        quad_ref[slot, 0:pair_width, pair_width:quad_width] = zero
        quad_ref[slot, pair_width:quad_width, 0:pair_width] = zero

    def chunk(start, span, total):
        table = table_ref[0, :, pl.ds(start, span)]
        sky = jnp.dot(coeff, table, preferred_element_type=jnp.float32).astype(jnp.bfloat16)
        for inner in range(span // quad_width):
            block = (start + inner * quad_width) // BLK
            first = index_ref[cycle, block] * side + index_ref[cycle, block + 1]
            second = index_ref[cycle, block + 2] * side + index_ref[cycle, block + 3]
            slot = inner % slots
            quad_ref[slot, 0:pair_width, 0:pair_width] = pair_ref[first]
            quad_ref[slot, pair_width:quad_width, pair_width:quad_width] = pair_ref[second]
            noisy = jnp.dot(
                sky[:, inner * quad_width:(inner + 1) * quad_width],
                quad_ref[slot],
                preferred_element_type=jnp.float32,
            )
            noisy_ref[:, inner * quad_width:(inner + 1) * quad_width] = noisy.astype(jnp.bfloat16)
        return total + lax.dot_general(
            noisy_ref[:, :span], table, (((1,), (1,)), ((), ())), preferred_element_type=jnp.float32
        )

    length = length_ref[cycle]
    mid = wide // 2
    narrow = wide // 4
    full = length // wide
    rest = length - full * wide
    wide_count = full + (rest > mid + narrow).astype(jnp.int32)
    mid_count = ((rest > narrow) & (rest <= mid + narrow)).astype(jnp.int32)
    narrow_count = (((rest > 0) & (rest <= narrow)) | ((rest > mid) & (rest <= mid + narrow))).astype(jnp.int32)
    total = lax.fori_loop(
        0,
        wide_count,
        lambda step, acc: chunk(pl.multiple_of(step * wide, wide), wide, acc),
        jnp.zeros(back_ref.shape[1:], jnp.float32),
    )
    total = lax.fori_loop(
        0,
        mid_count,
        lambda step, acc: chunk(pl.multiple_of(full * wide, wide), mid, acc),
        total,
    )
    total = lax.fori_loop(
        0,
        narrow_count,
        lambda step, acc: chunk(pl.multiple_of(full * wide + mid_count * mid, mid), narrow, acc),
        total,
    )
    back_ref[0] = total.astype(back_ref.dtype)


def cycle_transform(coeffs, lengths, indices, m_values, noise_mats, weight):
    cycle_count, mode_count, columns = coeffs.shape
    map_count = columns // 2
    kinds = noise_mats.shape[0]
    tables = cycle_tables(m_values, lengths, RLEN).reshape(cycle_count, 2 * mode_count, RLEN)
    coeff_t = (
        coeffs.reshape(cycle_count, mode_count, 2, map_count)
        .transpose(0, 3, 2, 1)
        .reshape(cycle_count, map_count, 2 * mode_count)
    )
    pairs_t = jnp.swapaxes(pair_table(noise_mats), 1, 2) * jnp.asarray(weight, jnp.bfloat16)
    grid_spec = pltpu.PrefetchScalarGridSpec(
        num_scalar_prefetch=2,
        grid=(cycle_count,),
        in_specs=[
            pl.BlockSpec((1, map_count, 2 * mode_count), lambda r, idx, n: (r, 0, 0)),
            pl.BlockSpec((1, 2 * mode_count, RLEN), lambda r, idx, n: (r, 0, 0)),
            pl.BlockSpec(pairs_t.shape, lambda r, idx, n: (0, 0, 0)),
        ],
        out_specs=pl.BlockSpec((1, map_count, 2 * mode_count), lambda r, idx, n: (r, 0, 0)),
        scratch_shapes=[
            pltpu.VMEM((map_count, 8192), jnp.bfloat16),
            pltpu.VMEM((4, 8 * BLK // 2, 8 * BLK // 2), jnp.bfloat16),
        ],
    )
    back = pl.pallas_call(
        noise_kernel,
        grid_spec=grid_spec,
        out_shape=jax.ShapeDtypeStruct((cycle_count, map_count, 2 * mode_count), jnp.bfloat16),
    )(indices, lengths, coeff_t, tables, pairs_t)
    return (
        back.reshape(cycle_count, map_count, 2, mode_count)
        .transpose(0, 3, 2, 1)
        .reshape(cycle_count, mode_count, columns)
    )


def shards(
    solution,
    residual,
    direction,
    legendre,
    prior_inv,
    noise_mats,
    noise_index,
    cycle_lengths,
    m_values,
    cut_pattern,
):
    band_count = lax.axis_size("band")
    mode_local, cycle_total, l_local = legendre.shape
    map_count = direction.shape[1]
    columns = 2 * map_count
    band_rows = cycle_total // band_count
    weight = L / (cycle_total * RLEN)
    rounded = direction.astype(jnp.bfloat16).reshape(columns, mode_local, l_local)

    def row_mask(first_row, row_count):
        block_flags = lax.dynamic_slice_in_dim(cut_pattern, first_row // RB, row_count // RB, 1)
        return jnp.repeat(block_flags, RB, axis=1).T

    section = legendre
    products = jnp.einsum("mrl,nml->rmn", section, rounded, preferred_element_type=jnp.float32)
    masked_products = products * row_mask(jnp.int32(0), cycle_total).astype(jnp.float32)[:, :, None]
    coeffs = gather_cycles(masked_products.reshape(cycle_total, columns), band_count).astype(jnp.bfloat16)
    cycle_local = coeffs.shape[0]
    mode_total = coeffs.shape[1]
    outputs = cycle_transform(coeffs, cycle_lengths, noise_index, m_values, noise_mats, weight)
    backward = outputs.reshape(cycle_local, mode_total, columns)
    returned = spread_cycles(backward, band_count)
    masked = returned * row_mask(jnp.int32(0), cycle_total).astype(jnp.bfloat16)
    image_data = lax.optimization_barrier(
        jnp.einsum("rl,rn->nl", legendre[0], masked, preferred_element_type=jnp.float32)
    )
    image_data = image_data.reshape(2, map_count, mode_local, l_local)
    image_field = prior_inv[None, None, None, :] * direction + image_data
    norm_now, curvature, cross, image_norm = total_over_mesh(
        jnp.stack(
            [
                jnp.sum(residual * residual, axis=(0, 2, 3)),
                jnp.sum(direction * image_field, axis=(0, 2, 3)),
                jnp.sum(residual * image_field, axis=(0, 2, 3)),
                jnp.sum(image_field * image_field, axis=(0, 2, 3)),
            ]
        )
    )
    step_size = norm_now / curvature
    new_residual = residual - step_size[None, :, None, None] * image_field
    norm_next = norm_now - 2.0 * step_size * cross + step_size * step_size * image_norm
    growth = norm_next / norm_now
    new_solution = solution + step_size[None, :, None, None] * direction
    new_direction = new_residual + growth[None, :, None, None] * direction
    return (new_solution, new_residual, new_direction)


def solution(mesh):
    in_specs = (
        P(None, None, "mgrp", "band"),
        P(None, None, "mgrp", "band"),
        P(None, None, "mgrp", "band"),
        P("mgrp", None, "band"),
        P("band"),
        P(),
        P(("band", "mgrp"), None),
        P(("band", "mgrp")),
        P(),
        P("mgrp", None),
    )
    out_specs = (
        P(None, None, "mgrp", "band"),
        P(None, None, "mgrp", "band"),
        P(None, None, "mgrp", "band"),
    )
    return jax.shard_map(shards, mesh=mesh, in_specs=in_specs, out_specs=out_specs, check_vma=False)
```

```python
import functools
import math

import jax
import jax.numpy as jnp
from jax import lax
from jax.experimental import pallas as pl
from jax.experimental.pallas import tpu as pltpu
from jax.sharding import PartitionSpec as P

L = 8192
RLEN = 16384
BLK = 64
RB = 64


MESH_AXES = ("mgrp", "band")


def total_over_mesh(values):
    count = lax.axis_size(MESH_AXES)
    copies = jnp.broadcast_to(values[None], (count,) + values.shape)
    return jnp.sum(lax.all_to_all(copies, MESH_AXES, 0, 0, tiled=True), axis=0)


def gather_cycles(partials, band_count):
    cycle_total, columns = partials.shape
    group_count = lax.axis_size("mgrp")
    own = cycle_total // (band_count * group_count)
    pieces = partials.reshape(band_count, group_count, own, columns).transpose(1, 0, 2, 3)
    pieces = pieces.reshape(group_count * band_count, own, columns)
    received = lax.all_to_all(pieces, MESH_AXES, 0, 0, tiled=True)
    received = received.reshape(group_count, band_count, own, columns)
    return jnp.sum(received, axis=1).transpose(1, 0, 2)


def spread_cycles(backward, band_count):
    group_count, own, columns = backward.shape
    pieces = jnp.broadcast_to(
        backward[:, None], (group_count, band_count, own, columns)
    ).reshape(group_count * band_count, own, columns)
    received = lax.all_to_all(pieces, MESH_AXES, 0, 0, tiled=True)
    received = received.reshape(group_count, band_count, own, columns).transpose(1, 0, 2, 3)
    return received.reshape(band_count * group_count * own, columns)


def cycle_tables(m_values, lengths, pixels):
    high_count = pixels // 128
    coarse = jnp.arange(high_count, dtype=jnp.int32) * 128
    fine = jnp.arange(128, dtype=jnp.int32)
    cycle_size = lengths[:, None, None].astype(jnp.float32)
    phase_high = m_values[None, :, None] * coarse[None, None, :] % lengths[:, None, None]
    phase_low = m_values[None, :, None] * fine[None, None, :] % lengths[:, None, None]
    angle_high = 2.0 * math.pi * phase_high.astype(jnp.float32) / cycle_size
    angle_low = 2.0 * math.pi * phase_low.astype(jnp.float32) / cycle_size
    cos_high = jnp.cos(angle_high)[:, :, :, None]
    sin_high = jnp.sin(angle_high)[:, :, :, None]
    cos_low = jnp.cos(angle_low)[:, :, None, :]
    sin_low = jnp.sin(angle_low)[:, :, None, :]
    cycle_count = lengths.shape[0]
    mode_count = m_values.shape[0]
    cos_full = (cos_high * cos_low - sin_high * sin_low).reshape(cycle_count, mode_count, pixels)
    sin_full = (sin_high * cos_low + cos_high * sin_low).reshape(cycle_count, mode_count, pixels)
    column = jnp.arange(pixels, dtype=jnp.int32)
    factor = jnp.where(m_values == 0, 1.0, 2.0).astype(jnp.float32)[None, :, None]
    inside = (column[None, None, :] < lengths[:, None, None]).astype(jnp.float32)
    cosine = factor * cos_full * inside
    sine_part = -factor * sin_full * inside
    return jnp.stack([cosine, sine_part], axis=1).astype(jnp.bfloat16)


def pair_table(noise_mats):
    kinds = noise_mats.shape[0]
    first = jnp.broadcast_to(noise_mats[:, None], (kinds, kinds, BLK, BLK))
    second = jnp.broadcast_to(noise_mats[None, :], (kinds, kinds, BLK, BLK))
    empty = jnp.zeros((kinds, kinds, BLK, BLK), noise_mats.dtype)
    upper = jnp.concatenate([first, empty], axis=3)
    lower = jnp.concatenate([empty, second], axis=3)
    return jnp.concatenate([upper, lower], axis=2).reshape(kinds * kinds, 2 * BLK, 2 * BLK)


def cycle_segment(coeffs, lengths, indices, m_values, pairs, kinds, weight):
    cycle_count, mode_count, columns = coeffs.shape
    map_count = columns // 2
    tables = cycle_tables(m_values, lengths, RLEN)
    split_coeffs = coeffs.reshape(cycle_count, mode_count, 2, map_count)
    sky_map = jnp.einsum(
        "rmcb,rcmk->rbk", split_coeffs, tables, preferred_element_type=jnp.float32
    ).astype(jnp.bfloat16)
    pair_count = RLEN // (2 * BLK)
    kind_pairs = indices.reshape(cycle_count, pair_count, 2)
    pair_index = kind_pairs[:, :, 0] * kinds + kind_pairs[:, :, 1]
    matrices = pairs.reshape(kinds * kinds, 4 * BLK * BLK)[pair_index].reshape(
        cycle_count, pair_count, 2 * BLK, 2 * BLK
    )
    blocked = sky_map.reshape(cycle_count, map_count, pair_count, 2 * BLK)
    noisy_map = weight * jnp.einsum(
        "rbqj,rqij->rbqi", blocked, matrices, preferred_element_type=jnp.float32
    )
    noisy_map = noisy_map.reshape(cycle_count, map_count, RLEN).astype(jnp.bfloat16)
    backward = jnp.einsum("rbk,rcmk->rmcb", noisy_map, tables, preferred_element_type=jnp.float32)
    return backward.reshape(cycle_count, mode_count, columns).astype(jnp.bfloat16)


def noise_kernel(index_ref, length_ref, coeff_ref, table_ref, pair_ref, back_ref, noisy_ref):
    cycle = pl.program_id(0)
    wide = noisy_ref.shape[1]
    pair_width = 2 * BLK
    coeff = coeff_ref[0]
    side = int(round(pair_ref.shape[0] ** 0.5))

    def chunk(start, span, total):
        table = table_ref[0, :, pl.ds(start, span)]
        sky = jnp.dot(coeff, table, preferred_element_type=jnp.float32).astype(jnp.bfloat16)
        for inner in range(span // pair_width):
            block = (start + inner * pair_width) // BLK
            pick = index_ref[cycle, block] * side + index_ref[cycle, block + 1]
            noisy = jnp.dot(
                sky[:, inner * pair_width:(inner + 1) * pair_width],
                pair_ref[pick],
                preferred_element_type=jnp.float32,
            )
            noisy_ref[:, inner * pair_width:(inner + 1) * pair_width] = noisy.astype(jnp.bfloat16)
        return total + lax.dot_general(
            table, noisy_ref[:, :span], (((1,), (1,)), ((), ())), preferred_element_type=jnp.float32
        )

    length = length_ref[cycle]
    mid = wide // 2
    narrow = wide // 4
    full = length // wide
    rest = length - full * wide
    wide_count = full + (rest > mid + narrow).astype(jnp.int32)
    mid_count = ((rest > narrow) & (rest <= mid + narrow)).astype(jnp.int32)
    narrow_count = (((rest > 0) & (rest <= narrow)) | ((rest > mid) & (rest <= mid + narrow))).astype(jnp.int32)
    total = lax.fori_loop(
        0,
        wide_count,
        lambda step, acc: chunk(pl.multiple_of(step * wide, wide), wide, acc),
        jnp.zeros((table_ref.shape[1], noisy_ref.shape[0]), jnp.float32),
    )
    total = lax.fori_loop(
        0,
        mid_count,
        lambda step, acc: chunk(pl.multiple_of(full * wide, wide), mid, acc),
        total,
    )
    total = lax.fori_loop(
        0,
        narrow_count,
        lambda step, acc: chunk(pl.multiple_of(full * wide + mid_count * mid, mid), narrow, acc),
        total,
    )
    modes = back_ref.shape[0]
    maps = noisy_ref.shape[0]
    for part in range(table_ref.shape[1] // modes):
        for mode in range(modes):
            row = part * modes + mode
            back_ref[mode, pl.ds(cycle, 1), part * maps:(part + 1) * maps] = total[row:row + 1, :]


def cycle_transform(coeffs, lengths, indices, m_values, noise_mats, weight):
    cycle_count, mode_count, columns = coeffs.shape
    map_count = columns // 2
    kinds = noise_mats.shape[0]
    tables = cycle_tables(m_values, lengths, RLEN).reshape(cycle_count, 2 * mode_count, RLEN)
    coeff_t = (
        coeffs.reshape(cycle_count, mode_count, 2, map_count)
        .transpose(0, 3, 2, 1)
        .reshape(cycle_count, map_count, 2 * mode_count)
    )
    pairs_t = jnp.swapaxes(pair_table(noise_mats), 1, 2) * jnp.asarray(weight, jnp.bfloat16)
    grid_spec = pltpu.PrefetchScalarGridSpec(
        num_scalar_prefetch=2,
        grid=(cycle_count,),
        in_specs=[
            pl.BlockSpec((1, map_count, 2 * mode_count), lambda r, idx, n: (r, 0, 0)),
            pl.BlockSpec((1, 2 * mode_count, RLEN), lambda r, idx, n: (r, 0, 0)),
            pl.BlockSpec(pairs_t.shape, lambda r, idx, n: (0, 0, 0)),
        ],
        out_specs=pl.BlockSpec((mode_count, cycle_count, columns), lambda r, idx, n: (0, 0, 0)),
        scratch_shapes=[pltpu.VMEM((map_count, 8192), jnp.bfloat16)],
    )
    back = pl.pallas_call(
        noise_kernel,
        grid_spec=grid_spec,
        out_shape=jax.ShapeDtypeStruct((mode_count, cycle_count, columns), jnp.float32),
    )(indices, lengths, coeff_t, tables, pairs_t)
    return back.astype(jnp.bfloat16)


def shards(
    solution,
    residual,
    direction,
    legendre,
    prior_inv,
    noise_mats,
    noise_index,
    cycle_lengths,
    m_values,
    cut_pattern,
):
    band_count = lax.axis_size("band")
    mode_local, cycle_total, l_local = legendre.shape
    map_count = direction.shape[1]
    columns = 2 * map_count
    band_rows = cycle_total // band_count
    weight = L / (cycle_total * RLEN)
    rounded = direction.astype(jnp.bfloat16).reshape(columns, mode_local, l_local)

    def row_mask(first_row, row_count):
        block_flags = lax.dynamic_slice_in_dim(cut_pattern, first_row // RB, row_count // RB, 1)
        return jnp.repeat(block_flags, RB, axis=1).T

    section = legendre
    products = jnp.einsum("mrl,nml->rmn", section, rounded, preferred_element_type=jnp.float32)
    masked_products = products * row_mask(jnp.int32(0), cycle_total).astype(jnp.float32)[:, :, None]
    coeffs = gather_cycles(masked_products.reshape(cycle_total, columns), band_count).astype(jnp.bfloat16)
    cycle_local = coeffs.shape[0]
    mode_total = coeffs.shape[1]
    outputs = cycle_transform(coeffs, cycle_lengths, noise_index, m_values, noise_mats, weight)
    returned = spread_cycles(outputs, band_count)
    masked = returned * row_mask(jnp.int32(0), cycle_total).astype(jnp.bfloat16)
    image_data = lax.optimization_barrier(
        jnp.einsum("rl,rn->nl", legendre[0], masked, preferred_element_type=jnp.float32)
    )
    image_data = image_data.reshape(2, map_count, mode_local, l_local)
    image_field = prior_inv[None, None, None, :] * direction + image_data
    norm_now, curvature, cross, image_norm = total_over_mesh(
        jnp.stack(
            [
                jnp.sum(residual * residual, axis=(0, 2, 3)),
                jnp.sum(direction * image_field, axis=(0, 2, 3)),
                jnp.sum(residual * image_field, axis=(0, 2, 3)),
                jnp.sum(image_field * image_field, axis=(0, 2, 3)),
            ]
        )
    )
    step_size = norm_now / curvature
    new_residual = residual - step_size[None, :, None, None] * image_field
    norm_next = norm_now - 2.0 * step_size * cross + step_size * step_size * image_norm
    growth = norm_next / norm_now
    new_solution = solution + step_size[None, :, None, None] * direction
    new_direction = new_residual + growth[None, :, None, None] * direction
    return (new_solution, new_residual, new_direction)


def solution(mesh):
    in_specs = (
        P(None, None, "mgrp", "band"),
        P(None, None, "mgrp", "band"),
        P(None, None, "mgrp", "band"),
        P("mgrp", None, "band"),
        P("band"),
        P(),
        P(("band", "mgrp"), None),
        P(("band", "mgrp")),
        P(),
        P("mgrp", None),
    )
    out_specs = (
        P(None, None, "mgrp", "band"),
        P(None, None, "mgrp", "band"),
        P(None, None, "mgrp", "band"),
    )
    return jax.shard_map(shards, mesh=mesh, in_specs=in_specs, out_specs=out_specs, check_vma=False)
```

```python
import functools
import math

import jax
import jax.numpy as jnp
from jax import lax
from jax.experimental import pallas as pl
from jax.experimental.pallas import tpu as pltpu
from jax.sharding import PartitionSpec as P

L = 8192
RLEN = 16384
BLK = 64
RB = 64


MESH_AXES = ("mgrp", "band")


def total_over_mesh(values):
    count = lax.axis_size(MESH_AXES)
    copies = jnp.broadcast_to(values[None], (count,) + values.shape)
    return jnp.sum(lax.all_to_all(copies, MESH_AXES, 0, 0, tiled=True), axis=0)


def gather_cycles(partials, band_count):
    cycle_total, columns = partials.shape
    group_count = lax.axis_size("mgrp")
    own = cycle_total // (band_count * group_count)
    pieces = partials.reshape(band_count, group_count, own, columns).transpose(1, 0, 2, 3)
    pieces = pieces.reshape(group_count * band_count, own, columns)
    received = lax.all_to_all(pieces, MESH_AXES, 0, 0, tiled=True)
    received = received.reshape(group_count, band_count, own, columns)
    return jnp.sum(received, axis=1).transpose(1, 0, 2)


def spread_cycles(backward, band_count):
    group_count, own, columns = backward.shape
    pieces = jnp.broadcast_to(
        backward[:, None], (group_count, band_count, own, columns)
    ).reshape(group_count * band_count, own, columns)
    received = lax.all_to_all(pieces, MESH_AXES, 0, 0, tiled=True)
    received = received.reshape(group_count, band_count, own, columns).transpose(1, 0, 2, 3)
    return received.reshape(band_count * group_count * own, columns)


def cycle_tables(m_values, lengths, pixels):
    high_count = pixels // 128
    coarse = jnp.arange(high_count, dtype=jnp.int32) * 128
    fine = jnp.arange(128, dtype=jnp.int32)
    cycle_size = lengths[:, None, None].astype(jnp.float32)
    phase_high = m_values[None, :, None] * coarse[None, None, :] % lengths[:, None, None]
    phase_low = m_values[None, :, None] * fine[None, None, :] % lengths[:, None, None]
    angle_high = 2.0 * math.pi * phase_high.astype(jnp.float32) / cycle_size
    angle_low = 2.0 * math.pi * phase_low.astype(jnp.float32) / cycle_size
    cos_high = jnp.cos(angle_high)[:, :, :, None]
    sin_high = jnp.sin(angle_high)[:, :, :, None]
    cos_low = jnp.cos(angle_low)[:, :, None, :]
    sin_low = jnp.sin(angle_low)[:, :, None, :]
    cycle_count = lengths.shape[0]
    mode_count = m_values.shape[0]
    cos_full = (cos_high * cos_low - sin_high * sin_low).reshape(cycle_count, mode_count, pixels)
    sin_full = (sin_high * cos_low + cos_high * sin_low).reshape(cycle_count, mode_count, pixels)
    column = jnp.arange(pixels, dtype=jnp.int32)
    factor = jnp.where(m_values == 0, 1.0, 2.0).astype(jnp.float32)[None, :, None]
    inside = (column[None, None, :] < lengths[:, None, None]).astype(jnp.float32)
    cosine = factor * cos_full * inside
    sine_part = -factor * sin_full * inside
    return jnp.stack([cosine, sine_part], axis=1).astype(jnp.bfloat16)


def pair_table(noise_mats):
    kinds = noise_mats.shape[0]
    first = jnp.broadcast_to(noise_mats[:, None], (kinds, kinds, BLK, BLK))
    second = jnp.broadcast_to(noise_mats[None, :], (kinds, kinds, BLK, BLK))
    empty = jnp.zeros((kinds, kinds, BLK, BLK), noise_mats.dtype)
    upper = jnp.concatenate([first, empty], axis=3)
    lower = jnp.concatenate([empty, second], axis=3)
    return jnp.concatenate([upper, lower], axis=2).reshape(kinds * kinds, 2 * BLK, 2 * BLK)


def cycle_segment(coeffs, lengths, indices, m_values, pairs, kinds, weight):
    cycle_count, mode_count, columns = coeffs.shape
    map_count = columns // 2
    tables = cycle_tables(m_values, lengths, RLEN)
    split_coeffs = coeffs.reshape(cycle_count, mode_count, 2, map_count)
    sky_map = jnp.einsum(
        "rmcb,rcmk->rbk", split_coeffs, tables, preferred_element_type=jnp.float32
    ).astype(jnp.bfloat16)
    pair_count = RLEN // (2 * BLK)
    kind_pairs = indices.reshape(cycle_count, pair_count, 2)
    pair_index = kind_pairs[:, :, 0] * kinds + kind_pairs[:, :, 1]
    matrices = pairs.reshape(kinds * kinds, 4 * BLK * BLK)[pair_index].reshape(
        cycle_count, pair_count, 2 * BLK, 2 * BLK
    )
    blocked = sky_map.reshape(cycle_count, map_count, pair_count, 2 * BLK)
    noisy_map = weight * jnp.einsum(
        "rbqj,rqij->rbqi", blocked, matrices, preferred_element_type=jnp.float32
    )
    noisy_map = noisy_map.reshape(cycle_count, map_count, RLEN).astype(jnp.bfloat16)
    backward = jnp.einsum("rbk,rcmk->rmcb", noisy_map, tables, preferred_element_type=jnp.float32)
    return backward.reshape(cycle_count, mode_count, columns).astype(jnp.bfloat16)


def noise_kernel(index_ref, length_ref, coeff_ref, table_ref, pair_ref, back_ref, noisy_ref):
    cycle = pl.program_id(0)
    wide = noisy_ref.shape[1]
    pair_width = 2 * BLK
    coeff = coeff_ref[0]
    side = int(round(pair_ref.shape[0] ** 0.5))

    def chunk(start, span, total):
        table = table_ref[0, :, pl.ds(start, span)]
        sky = jnp.dot(coeff, table, preferred_element_type=jnp.float32).astype(jnp.bfloat16)
        for inner in range(span // pair_width):
            block = (start + inner * pair_width) // BLK
            pick = index_ref[cycle, block] * side + index_ref[cycle, block + 1]
            noisy = jnp.dot(
                sky[:, inner * pair_width:(inner + 1) * pair_width],
                pair_ref[pick],
                preferred_element_type=jnp.float32,
            )
            noisy_ref[:, inner * pair_width:(inner + 1) * pair_width] = noisy.astype(jnp.bfloat16)
        return total + lax.dot_general(
            table, noisy_ref[:, :span], (((1,), (1,)), ((), ())), preferred_element_type=jnp.float32
        )

    length = length_ref[cycle]
    mid = wide // 2
    narrow = wide // 4
    full = length // wide
    rest = length - full * wide
    wide_count = full + (rest > mid + narrow).astype(jnp.int32)
    mid_count = ((rest > narrow) & (rest <= mid + narrow)).astype(jnp.int32)
    narrow_count = (((rest > 0) & (rest <= narrow)) | ((rest > mid) & (rest <= mid + narrow))).astype(jnp.int32)
    total = lax.fori_loop(
        0,
        wide_count,
        lambda step, acc: chunk(pl.multiple_of(step * wide, wide), wide, acc),
        jnp.zeros((table_ref.shape[1], noisy_ref.shape[0]), jnp.float32),
    )
    total = lax.fori_loop(
        0,
        mid_count,
        lambda step, acc: chunk(pl.multiple_of(full * wide, wide), mid, acc),
        total,
    )
    total = lax.fori_loop(
        0,
        narrow_count,
        lambda step, acc: chunk(pl.multiple_of(full * wide + mid_count * mid, mid), narrow, acc),
        total,
    )
    modes = back_ref.shape[0]
    maps = noisy_ref.shape[0]
    for part in range(table_ref.shape[1] // modes):
        for mode in range(modes):
            row = part * modes + mode
            back_ref[mode, pl.ds(cycle, 1), part * maps:(part + 1) * maps] = total[row:row + 1, :]


def cycle_transform(coeffs, lengths, indices, m_values, noise_mats, weight):
    cycle_count, mode_count, columns = coeffs.shape
    map_count = columns // 2
    kinds = noise_mats.shape[0]
    tables = cycle_tables(m_values, lengths, RLEN).reshape(cycle_count, 2 * mode_count, RLEN)
    coeff_t = (
        coeffs.reshape(cycle_count, mode_count, 2, map_count)
        .transpose(0, 3, 2, 1)
        .reshape(cycle_count, map_count, 2 * mode_count)
    )
    pairs_t = jnp.swapaxes(pair_table(noise_mats), 1, 2) * jnp.asarray(weight, jnp.bfloat16)
    grid_spec = pltpu.PrefetchScalarGridSpec(
        num_scalar_prefetch=2,
        grid=(cycle_count,),
        in_specs=[
            pl.BlockSpec((1, map_count, 2 * mode_count), lambda r, idx, n: (r, 0, 0)),
            pl.BlockSpec((1, 2 * mode_count, RLEN), lambda r, idx, n: (r, 0, 0)),
            pl.BlockSpec(pairs_t.shape, lambda r, idx, n: (0, 0, 0)),
        ],
        out_specs=pl.BlockSpec((mode_count, cycle_count, columns), lambda r, idx, n: (0, 0, 0)),
        scratch_shapes=[pltpu.VMEM((map_count, 8192), jnp.bfloat16)],
    )
    back = pl.pallas_call(
        noise_kernel,
        grid_spec=grid_spec,
        out_shape=jax.ShapeDtypeStruct((mode_count, cycle_count, columns), jnp.float32),
    )(indices, lengths, coeff_t, tables, pairs_t)
    return back.astype(jnp.bfloat16)


def shards(
    solution,
    residual,
    direction,
    legendre,
    prior_inv,
    noise_mats,
    noise_index,
    cycle_lengths,
    m_values,
    cut_pattern,
):
    band_count = lax.axis_size("band")
    mode_local, cycle_total, l_local = legendre.shape
    map_count = direction.shape[1]
    columns = 2 * map_count
    band_rows = cycle_total // band_count
    weight = L / (cycle_total * RLEN)

    def row_mask(first_row, row_count):
        block_flags = lax.dynamic_slice_in_dim(cut_pattern, first_row // RB, row_count // RB, 1)
        return jnp.repeat(block_flags, RB, axis=1).T

    section = legendre
    products = jnp.einsum(
        "mrl,nml->rmn",
        section,
        direction.reshape(columns, mode_local, l_local),
        precision=lax.Precision.DEFAULT,
        preferred_element_type=jnp.float32,
    )
    masked_products = products * row_mask(jnp.int32(0), cycle_total).astype(jnp.float32)[:, :, None]
    coeffs = gather_cycles(masked_products.reshape(cycle_total, columns), band_count).astype(jnp.bfloat16)
    cycle_local = coeffs.shape[0]
    mode_total = coeffs.shape[1]
    outputs = cycle_transform(coeffs, cycle_lengths, noise_index, m_values, noise_mats, weight)
    returned = spread_cycles(outputs, band_count)
    masked = returned * row_mask(jnp.int32(0), cycle_total).astype(jnp.bfloat16)
    image_data = lax.optimization_barrier(
        jnp.einsum("rl,rn->nl", legendre[0], masked, preferred_element_type=jnp.float32)
    )
    image_data = image_data.reshape(2, map_count, mode_local, l_local)
    image_field = prior_inv[None, None, None, :] * direction + image_data
    norm_now, curvature, cross, image_norm = total_over_mesh(
        jnp.stack(
            [
                jnp.sum(residual * residual, axis=(0, 2, 3)),
                jnp.sum(direction * image_field, axis=(0, 2, 3)),
                jnp.sum(residual * image_field, axis=(0, 2, 3)),
                jnp.sum(image_field * image_field, axis=(0, 2, 3)),
            ]
        )
    )
    step_size = norm_now / curvature
    new_residual = residual - step_size[None, :, None, None] * image_field
    norm_next = norm_now - 2.0 * step_size * cross + step_size * step_size * image_norm
    growth = norm_next / norm_now
    new_solution = solution + step_size[None, :, None, None] * direction
    new_direction = new_residual + growth[None, :, None, None] * direction
    return (new_solution, new_residual, new_direction)


def solution(mesh):
    in_specs = (
        P(None, None, "mgrp", "band"),
        P(None, None, "mgrp", "band"),
        P(None, None, "mgrp", "band"),
        P("mgrp", None, "band"),
        P("band"),
        P(),
        P(("band", "mgrp"), None),
        P(("band", "mgrp")),
        P(),
        P("mgrp", None),
    )
    out_specs = (
        P(None, None, "mgrp", "band"),
        P(None, None, "mgrp", "band"),
        P(None, None, "mgrp", "band"),
    )
    return jax.shard_map(shards, mesh=mesh, in_specs=in_specs, out_specs=out_specs, check_vma=False)
```

```python
import functools
import math

import jax
import jax.numpy as jnp
from jax import lax
from jax.experimental import pallas as pl
from jax.experimental.pallas import tpu as pltpu
from jax.sharding import PartitionSpec as P

L = 8192
RLEN = 16384
BLK = 64
RB = 64


MESH_AXES = ("mgrp", "band")


def total_over_mesh(values):
    count = lax.axis_size(MESH_AXES)
    copies = jnp.broadcast_to(values[None], (count,) + values.shape)
    return jnp.sum(lax.all_to_all(copies, MESH_AXES, 0, 0, tiled=True), axis=0)


def gather_cycles(partials, band_count):
    cycle_total, columns = partials.shape
    group_count = lax.axis_size("mgrp")
    own = cycle_total // (band_count * group_count)
    pieces = partials.reshape(band_count, group_count, own, columns).transpose(1, 0, 2, 3)
    pieces = pieces.reshape(group_count * band_count, own, columns)
    received = lax.all_to_all(pieces, MESH_AXES, 0, 0, tiled=True)
    received = received.reshape(group_count, band_count, own, columns)
    return jnp.sum(received, axis=1).transpose(1, 0, 2)


def spread_cycles(backward, band_count):
    group_count, own, columns = backward.shape
    pieces = jnp.broadcast_to(
        backward[:, None], (group_count, band_count, own, columns)
    ).reshape(group_count * band_count, own, columns)
    received = lax.all_to_all(pieces, MESH_AXES, 0, 0, tiled=True)
    received = received.reshape(group_count, band_count, own, columns).transpose(1, 0, 2, 3)
    return received.reshape(band_count * group_count * own, columns)


def cycle_tables(m_values, lengths, pixels):
    high_count = pixels // 128
    coarse = jnp.arange(high_count, dtype=jnp.int32) * 128
    fine = jnp.arange(128, dtype=jnp.int32)
    cycle_size = lengths[:, None, None].astype(jnp.float32)
    phase_high = m_values[None, :, None] * coarse[None, None, :] % lengths[:, None, None]
    phase_low = m_values[None, :, None] * fine[None, None, :] % lengths[:, None, None]
    angle_high = 2.0 * math.pi * phase_high.astype(jnp.float32) / cycle_size
    angle_low = 2.0 * math.pi * phase_low.astype(jnp.float32) / cycle_size
    cos_high = jnp.cos(angle_high)[:, :, :, None]
    sin_high = jnp.sin(angle_high)[:, :, :, None]
    cos_low = jnp.cos(angle_low)[:, :, None, :]
    sin_low = jnp.sin(angle_low)[:, :, None, :]
    cycle_count = lengths.shape[0]
    mode_count = m_values.shape[0]
    cos_full = (cos_high * cos_low - sin_high * sin_low).reshape(cycle_count, mode_count, pixels)
    sin_full = (sin_high * cos_low + cos_high * sin_low).reshape(cycle_count, mode_count, pixels)
    column = jnp.arange(pixels, dtype=jnp.int32)
    factor = jnp.where(m_values == 0, 1.0, 2.0).astype(jnp.float32)[None, :, None]
    inside = (column[None, None, :] < lengths[:, None, None]).astype(jnp.float32)
    cosine = factor * cos_full * inside
    sine_part = -factor * sin_full * inside
    return jnp.stack([cosine, sine_part], axis=1).astype(jnp.bfloat16)


def pair_table(noise_mats):
    kinds = noise_mats.shape[0]
    first = jnp.broadcast_to(noise_mats[:, None], (kinds, kinds, BLK, BLK))
    second = jnp.broadcast_to(noise_mats[None, :], (kinds, kinds, BLK, BLK))
    empty = jnp.zeros((kinds, kinds, BLK, BLK), noise_mats.dtype)
    upper = jnp.concatenate([first, empty], axis=3)
    lower = jnp.concatenate([empty, second], axis=3)
    return jnp.concatenate([upper, lower], axis=2).reshape(kinds * kinds, 2 * BLK, 2 * BLK)


def cycle_segment(coeffs, lengths, indices, m_values, pairs, kinds, weight):
    cycle_count, mode_count, columns = coeffs.shape
    map_count = columns // 2
    tables = cycle_tables(m_values, lengths, RLEN)
    split_coeffs = coeffs.reshape(cycle_count, mode_count, 2, map_count)
    sky_map = jnp.einsum(
        "rmcb,rcmk->rbk", split_coeffs, tables, preferred_element_type=jnp.float32
    ).astype(jnp.bfloat16)
    pair_count = RLEN // (2 * BLK)
    kind_pairs = indices.reshape(cycle_count, pair_count, 2)
    pair_index = kind_pairs[:, :, 0] * kinds + kind_pairs[:, :, 1]
    matrices = pairs.reshape(kinds * kinds, 4 * BLK * BLK)[pair_index].reshape(
        cycle_count, pair_count, 2 * BLK, 2 * BLK
    )
    blocked = sky_map.reshape(cycle_count, map_count, pair_count, 2 * BLK)
    noisy_map = weight * jnp.einsum(
        "rbqj,rqij->rbqi", blocked, matrices, preferred_element_type=jnp.float32
    )
    noisy_map = noisy_map.reshape(cycle_count, map_count, RLEN).astype(jnp.bfloat16)
    backward = jnp.einsum("rbk,rcmk->rmcb", noisy_map, tables, preferred_element_type=jnp.float32)
    return backward.reshape(cycle_count, mode_count, columns).astype(jnp.bfloat16)


def noise_kernel(index_ref, length_ref, coeff_ref, table_ref, pair_ref, back_ref, noisy_ref):
    cycle = pl.program_id(0)
    wide = noisy_ref.shape[1]
    pair_width = 2 * BLK
    coeff = coeff_ref[0]
    side = int(round(pair_ref.shape[0] ** 0.5))

    def chunk(start, span, total):
        table = table_ref[0, :, pl.ds(start, span)]
        sky = jnp.dot(coeff, table, preferred_element_type=jnp.float32).astype(jnp.bfloat16)
        for inner in range(span // pair_width):
            block = (start + inner * pair_width) // BLK
            pick = index_ref[cycle, block] * side + index_ref[cycle, block + 1]
            noisy = jnp.dot(
                sky[:, inner * pair_width:(inner + 1) * pair_width],
                pair_ref[pick],
                preferred_element_type=jnp.float32,
            )
            noisy_ref[:, inner * pair_width:(inner + 1) * pair_width] = noisy.astype(jnp.bfloat16)
        return total + lax.dot_general(
            table, noisy_ref[:, :span], (((1,), (1,)), ((), ())), preferred_element_type=jnp.float32
        )

    length = length_ref[cycle]
    mid = wide // 2
    narrow = wide // 4
    full = length // wide
    rest = length - full * wide
    wide_count = full + (rest > mid + narrow).astype(jnp.int32)
    mid_count = ((rest > narrow) & (rest <= mid + narrow)).astype(jnp.int32)
    narrow_count = (((rest > 0) & (rest <= narrow)) | ((rest > mid) & (rest <= mid + narrow))).astype(jnp.int32)
    total = lax.fori_loop(
        0,
        wide_count,
        lambda step, acc: chunk(pl.multiple_of(step * wide, wide), wide, acc),
        jnp.zeros((table_ref.shape[1], noisy_ref.shape[0]), jnp.float32),
    )
    total = lax.fori_loop(
        0,
        mid_count,
        lambda step, acc: chunk(pl.multiple_of(full * wide, wide), mid, acc),
        total,
    )
    total = lax.fori_loop(
        0,
        narrow_count,
        lambda step, acc: chunk(pl.multiple_of(full * wide + mid_count * mid, mid), narrow, acc),
        total,
    )
    modes = back_ref.shape[0]
    maps = noisy_ref.shape[0]
    for part in range(table_ref.shape[1] // modes):
        for mode in range(modes):
            row = part * modes + mode
            back_ref[mode, pl.ds(cycle, 1), part * maps:(part + 1) * maps] = total[row:row + 1, :]


def cycle_transform(coeffs, lengths, indices, m_values, noise_mats, weight):
    cycle_count, mode_count, columns = coeffs.shape
    map_count = columns // 2
    kinds = noise_mats.shape[0]
    tables = cycle_tables(m_values, lengths, RLEN).reshape(cycle_count, 2 * mode_count, RLEN)
    coeff_t = (
        coeffs.reshape(cycle_count, mode_count, 2, map_count)
        .transpose(0, 3, 2, 1)
        .reshape(cycle_count, map_count, 2 * mode_count)
    )
    pairs_t = jnp.swapaxes(pair_table(noise_mats), 1, 2) * jnp.asarray(weight, jnp.bfloat16)
    grid_spec = pltpu.PrefetchScalarGridSpec(
        num_scalar_prefetch=2,
        grid=(cycle_count,),
        in_specs=[
            pl.BlockSpec((1, map_count, 2 * mode_count), lambda r, idx, n: (r, 0, 0)),
            pl.BlockSpec((1, 2 * mode_count, RLEN), lambda r, idx, n: (r, 0, 0)),
            pl.BlockSpec(pairs_t.shape, lambda r, idx, n: (0, 0, 0)),
        ],
        out_specs=pl.BlockSpec((mode_count, cycle_count, columns), lambda r, idx, n: (0, 0, 0)),
        scratch_shapes=[pltpu.VMEM((map_count, 8192), jnp.bfloat16)],
    )
    back = pl.pallas_call(
        noise_kernel,
        grid_spec=grid_spec,
        out_shape=jax.ShapeDtypeStruct((mode_count, cycle_count, columns), jnp.float32),
    )(indices, lengths, coeff_t, tables, pairs_t)
    return back.astype(jnp.bfloat16)


def shards(
    solution,
    residual,
    direction,
    legendre,
    prior_inv,
    noise_mats,
    noise_index,
    cycle_lengths,
    m_values,
    cut_pattern,
):
    band_count = lax.axis_size("band")
    mode_local, cycle_total, l_local = legendre.shape
    map_count = direction.shape[1]
    columns = 2 * map_count
    band_rows = cycle_total // band_count
    weight = L / (cycle_total * RLEN)

    def row_mask(first_row, row_count):
        block_flags = lax.dynamic_slice_in_dim(cut_pattern, first_row // RB, row_count // RB, 1)
        return jnp.repeat(block_flags, RB, axis=1).T

    section = legendre * row_mask(jnp.int32(0), cycle_total).astype(legendre.dtype)[None]
    products = jnp.einsum(
        "mrl,nml->rmn",
        section,
        direction.reshape(columns, mode_local, l_local),
        precision=lax.Precision.DEFAULT,
        preferred_element_type=jnp.float32,
    )
    masked_products = products
    coeffs = gather_cycles(masked_products.reshape(cycle_total, columns), band_count).astype(jnp.bfloat16)
    cycle_local = coeffs.shape[0]
    mode_total = coeffs.shape[1]
    outputs = cycle_transform(coeffs, cycle_lengths, noise_index, m_values, noise_mats, weight)
    returned = spread_cycles(outputs, band_count)
    masked = returned
    image_data = lax.optimization_barrier(
        jnp.einsum("rl,rn->nl", section[0], masked, preferred_element_type=jnp.float32)
    )
    image_data = image_data.reshape(2, map_count, mode_local, l_local)
    image_field = prior_inv[None, None, None, :] * direction + image_data
    norm_now, curvature, cross, image_norm = total_over_mesh(
        jnp.stack(
            [
                jnp.sum(residual * residual, axis=(0, 2, 3)),
                jnp.sum(direction * image_field, axis=(0, 2, 3)),
                jnp.sum(residual * image_field, axis=(0, 2, 3)),
                jnp.sum(image_field * image_field, axis=(0, 2, 3)),
            ]
        )
    )
    step_size = norm_now / curvature
    new_residual = residual - step_size[None, :, None, None] * image_field
    norm_next = norm_now - 2.0 * step_size * cross + step_size * step_size * image_norm
    growth = norm_next / norm_now
    new_solution = solution + step_size[None, :, None, None] * direction
    new_direction = new_residual + growth[None, :, None, None] * direction
    return (new_solution, new_residual, new_direction)


def solution(mesh):
    in_specs = (
        P(None, None, "mgrp", "band"),
        P(None, None, "mgrp", "band"),
        P(None, None, "mgrp", "band"),
        P("mgrp", None, "band"),
        P("band"),
        P(),
        P(("band", "mgrp"), None),
        P(("band", "mgrp")),
        P(),
        P("mgrp", None),
    )
    out_specs = (
        P(None, None, "mgrp", "band"),
        P(None, None, "mgrp", "band"),
        P(None, None, "mgrp", "band"),
    )
    return jax.shard_map(shards, mesh=mesh, in_specs=in_specs, out_specs=out_specs, check_vma=False)
```

```python
import functools
import math

import jax
import jax.numpy as jnp
from jax import lax
from jax.experimental import pallas as pl
from jax.experimental.pallas import tpu as pltpu
from jax.sharding import PartitionSpec as P

L = 8192
RLEN = 16384
BLK = 64
RB = 64


MESH_AXES = ("mgrp", "band")


def total_over_mesh(values):
    count = lax.axis_size(MESH_AXES)
    flat = values.reshape(-1, 128)
    copies = jnp.broadcast_to(flat[None], (count,) + flat.shape)
    return jnp.sum(lax.all_to_all(copies, MESH_AXES, 0, 0, tiled=True), axis=0).reshape(values.shape)


def gather_cycles(partials, band_count):
    cycle_total, columns = partials.shape
    group_count = lax.axis_size("mgrp")
    own = cycle_total // (band_count * group_count)
    pieces = partials.reshape(band_count, group_count, own, columns).transpose(1, 0, 2, 3)
    pieces = pieces.reshape(group_count * band_count, own, columns)
    received = lax.all_to_all(pieces, MESH_AXES, 0, 0, tiled=True)
    received = received.reshape(group_count, band_count, own, columns)
    return jnp.sum(received, axis=1).transpose(1, 0, 2)


def spread_cycles(backward, band_count):
    group_count, own, columns = backward.shape
    pieces = jnp.broadcast_to(
        backward[:, None], (group_count, band_count, own, columns)
    ).reshape(group_count * band_count, own, columns)
    received = lax.all_to_all(pieces, MESH_AXES, 0, 0, tiled=True)
    received = received.reshape(group_count, band_count, own, columns).transpose(1, 0, 2, 3)
    return received.reshape(band_count * group_count * own, columns)


def cycle_tables(m_values, lengths, pixels):
    high_count = pixels // 128
    coarse = jnp.arange(high_count, dtype=jnp.int32) * 128
    fine = jnp.arange(128, dtype=jnp.int32)
    cycle_size = lengths[:, None, None].astype(jnp.float32)
    phase_high = m_values[None, :, None] * coarse[None, None, :] % lengths[:, None, None]
    phase_low = m_values[None, :, None] * fine[None, None, :] % lengths[:, None, None]
    angle_high = 2.0 * math.pi * phase_high.astype(jnp.float32) / cycle_size
    angle_low = 2.0 * math.pi * phase_low.astype(jnp.float32) / cycle_size
    cos_high = jnp.cos(angle_high)[:, :, :, None]
    sin_high = jnp.sin(angle_high)[:, :, :, None]
    cos_low = jnp.cos(angle_low)[:, :, None, :]
    sin_low = jnp.sin(angle_low)[:, :, None, :]
    cycle_count = lengths.shape[0]
    mode_count = m_values.shape[0]
    cos_full = (cos_high * cos_low - sin_high * sin_low).reshape(cycle_count, mode_count, pixels)
    sin_full = (sin_high * cos_low + cos_high * sin_low).reshape(cycle_count, mode_count, pixels)
    column = jnp.arange(pixels, dtype=jnp.int32)
    factor = jnp.where(m_values == 0, 1.0, 2.0).astype(jnp.float32)[None, :, None]
    inside = (column[None, None, :] < lengths[:, None, None]).astype(jnp.float32)
    cosine = factor * cos_full * inside
    sine_part = -factor * sin_full * inside
    return jnp.stack([cosine, sine_part], axis=1).astype(jnp.bfloat16)


def pair_table(noise_mats):
    kinds = noise_mats.shape[0]
    first = jnp.broadcast_to(noise_mats[:, None], (kinds, kinds, BLK, BLK))
    second = jnp.broadcast_to(noise_mats[None, :], (kinds, kinds, BLK, BLK))
    empty = jnp.zeros((kinds, kinds, BLK, BLK), noise_mats.dtype)
    upper = jnp.concatenate([first, empty], axis=3)
    lower = jnp.concatenate([empty, second], axis=3)
    return jnp.concatenate([upper, lower], axis=2).reshape(kinds * kinds, 2 * BLK, 2 * BLK)


def cycle_segment(coeffs, lengths, indices, m_values, pairs, kinds, weight):
    cycle_count, mode_count, columns = coeffs.shape
    map_count = columns // 2
    tables = cycle_tables(m_values, lengths, RLEN)
    split_coeffs = coeffs.reshape(cycle_count, mode_count, 2, map_count)
    sky_map = jnp.einsum(
        "rmcb,rcmk->rbk", split_coeffs, tables, preferred_element_type=jnp.float32
    ).astype(jnp.bfloat16)
    pair_count = RLEN // (2 * BLK)
    kind_pairs = indices.reshape(cycle_count, pair_count, 2)
    pair_index = kind_pairs[:, :, 0] * kinds + kind_pairs[:, :, 1]
    matrices = pairs.reshape(kinds * kinds, 4 * BLK * BLK)[pair_index].reshape(
        cycle_count, pair_count, 2 * BLK, 2 * BLK
    )
    blocked = sky_map.reshape(cycle_count, map_count, pair_count, 2 * BLK)
    noisy_map = weight * jnp.einsum(
        "rbqj,rqij->rbqi", blocked, matrices, preferred_element_type=jnp.float32
    )
    noisy_map = noisy_map.reshape(cycle_count, map_count, RLEN).astype(jnp.bfloat16)
    backward = jnp.einsum("rbk,rcmk->rmcb", noisy_map, tables, preferred_element_type=jnp.float32)
    return backward.reshape(cycle_count, mode_count, columns).astype(jnp.bfloat16)


def noise_kernel(index_ref, length_ref, coeff_ref, table_ref, pair_ref, back_ref, noisy_ref):
    cycle = pl.program_id(0)
    wide = noisy_ref.shape[1]
    pair_width = 2 * BLK
    coeff = coeff_ref[0]
    side = int(round(pair_ref.shape[0] ** 0.5))

    def chunk(start, span, total):
        table = table_ref[0, :, pl.ds(start, span)]
        sky = jnp.dot(coeff, table, preferred_element_type=jnp.float32).astype(jnp.bfloat16)
        for inner in range(span // pair_width):
            block = (start + inner * pair_width) // BLK
            pick = index_ref[cycle, block] * side + index_ref[cycle, block + 1]
            noisy = jnp.dot(
                sky[:, inner * pair_width:(inner + 1) * pair_width],
                pair_ref[pick],
                preferred_element_type=jnp.float32,
            )
            noisy_ref[:, inner * pair_width:(inner + 1) * pair_width] = noisy.astype(jnp.bfloat16)
        return total + lax.dot_general(
            table, noisy_ref[:, :span], (((1,), (1,)), ((), ())), preferred_element_type=jnp.float32
        )

    length = length_ref[cycle]
    mid = wide // 2
    narrow = wide // 4
    full = length // wide
    rest = length - full * wide
    wide_count = full + (rest > mid + narrow).astype(jnp.int32)
    mid_count = ((rest > narrow) & (rest <= mid + narrow)).astype(jnp.int32)
    narrow_count = (((rest > 0) & (rest <= narrow)) | ((rest > mid) & (rest <= mid + narrow))).astype(jnp.int32)
    total = lax.fori_loop(
        0,
        wide_count,
        lambda step, acc: chunk(pl.multiple_of(step * wide, wide), wide, acc),
        jnp.zeros((table_ref.shape[1], noisy_ref.shape[0]), jnp.float32),
    )
    total = lax.fori_loop(
        0,
        mid_count,
        lambda step, acc: chunk(pl.multiple_of(full * wide, wide), mid, acc),
        total,
    )
    total = lax.fori_loop(
        0,
        narrow_count,
        lambda step, acc: chunk(pl.multiple_of(full * wide + mid_count * mid, mid), narrow, acc),
        total,
    )
    modes = back_ref.shape[0]
    maps = noisy_ref.shape[0]
    for part in range(table_ref.shape[1] // modes):
        for mode in range(modes):
            row = part * modes + mode
            back_ref[mode, pl.ds(cycle, 1), part * maps:(part + 1) * maps] = total[row:row + 1, :]


def cycle_transform(coeffs, lengths, indices, m_values, noise_mats, weight):
    cycle_count, mode_count, columns = coeffs.shape
    map_count = columns // 2
    kinds = noise_mats.shape[0]
    tables = cycle_tables(m_values, lengths, RLEN).reshape(cycle_count, 2 * mode_count, RLEN)
    coeff_t = (
        coeffs.reshape(cycle_count, mode_count, 2, map_count)
        .transpose(0, 3, 2, 1)
        .reshape(cycle_count, map_count, 2 * mode_count)
    )
    pairs_t = jnp.swapaxes(pair_table(noise_mats), 1, 2) * jnp.asarray(weight, jnp.bfloat16)
    grid_spec = pltpu.PrefetchScalarGridSpec(
        num_scalar_prefetch=2,
        grid=(cycle_count,),
        in_specs=[
            pl.BlockSpec((1, map_count, 2 * mode_count), lambda r, idx, n: (r, 0, 0)),
            pl.BlockSpec((1, 2 * mode_count, RLEN), lambda r, idx, n: (r, 0, 0)),
            pl.BlockSpec(pairs_t.shape, lambda r, idx, n: (0, 0, 0)),
        ],
        out_specs=pl.BlockSpec((mode_count, cycle_count, columns), lambda r, idx, n: (0, 0, 0)),
        scratch_shapes=[pltpu.VMEM((map_count, 8192), jnp.bfloat16)],
    )
    back = pl.pallas_call(
        noise_kernel,
        grid_spec=grid_spec,
        out_shape=jax.ShapeDtypeStruct((mode_count, cycle_count, columns), jnp.float32),
    )(indices, lengths, coeff_t, tables, pairs_t)
    return back.astype(jnp.bfloat16)


def shards(
    solution,
    residual,
    direction,
    legendre,
    prior_inv,
    noise_mats,
    noise_index,
    cycle_lengths,
    m_values,
    cut_pattern,
):
    band_count = lax.axis_size("band")
    mode_local, cycle_total, l_local = legendre.shape
    map_count = direction.shape[1]
    columns = 2 * map_count
    band_rows = cycle_total // band_count
    weight = L / (cycle_total * RLEN)

    def row_mask(first_row, row_count):
        block_flags = lax.dynamic_slice_in_dim(cut_pattern, first_row // RB, row_count // RB, 1)
        return jnp.repeat(block_flags, RB, axis=1).T

    section = legendre
    products = jnp.einsum(
        "mrl,nml->rmn",
        section,
        direction.reshape(columns, mode_local, l_local),
        precision=lax.Precision.DEFAULT,
        preferred_element_type=jnp.float32,
    )
    masked_products = products * row_mask(jnp.int32(0), cycle_total).astype(jnp.float32)[:, :, None]
    coeffs = gather_cycles(masked_products.reshape(cycle_total, columns), band_count).astype(jnp.bfloat16)
    cycle_local = coeffs.shape[0]
    mode_total = coeffs.shape[1]
    outputs = cycle_transform(coeffs, cycle_lengths, noise_index, m_values, noise_mats, weight)
    returned = spread_cycles(outputs, band_count)
    masked = returned * row_mask(jnp.int32(0), cycle_total).astype(jnp.bfloat16)
    image_data = lax.optimization_barrier(
        jnp.einsum("rl,rn->nl", legendre[0], masked, preferred_element_type=jnp.float32)
    )
    image_data = image_data.reshape(2, map_count, mode_local, l_local)
    image_field = prior_inv[None, None, None, :] * direction + image_data
    norm_now, curvature, cross, image_norm = total_over_mesh(
        jnp.stack(
            [
                jnp.sum(residual * residual, axis=(0, 2, 3)),
                jnp.sum(direction * image_field, axis=(0, 2, 3)),
                jnp.sum(residual * image_field, axis=(0, 2, 3)),
                jnp.sum(image_field * image_field, axis=(0, 2, 3)),
            ]
        )
    )
    step_size = norm_now / curvature
    new_residual = residual - step_size[None, :, None, None] * image_field
    norm_next = norm_now - 2.0 * step_size * cross + step_size * step_size * image_norm
    growth = norm_next / norm_now
    new_solution = solution + step_size[None, :, None, None] * direction
    new_direction = new_residual + growth[None, :, None, None] * direction
    return (new_solution, new_residual, new_direction)


def solution(mesh):
    in_specs = (
        P(None, None, "mgrp", "band"),
        P(None, None, "mgrp", "band"),
        P(None, None, "mgrp", "band"),
        P("mgrp", None, "band"),
        P("band"),
        P(),
        P(("band", "mgrp"), None),
        P(("band", "mgrp")),
        P(),
        P("mgrp", None),
    )
    out_specs = (
        P(None, None, "mgrp", "band"),
        P(None, None, "mgrp", "band"),
        P(None, None, "mgrp", "band"),
    )
    return jax.shard_map(shards, mesh=mesh, in_specs=in_specs, out_specs=out_specs, check_vma=False)
```

```python
import functools
import math

import jax
import jax.numpy as jnp
from jax import lax
from jax.experimental import pallas as pl
from jax.experimental.pallas import tpu as pltpu
from jax.sharding import PartitionSpec as P

L = 8192
RLEN = 16384
BLK = 64
RB = 64


MESH_AXES = ("mgrp", "band")


def total_over_mesh(values):
    count = lax.axis_size(MESH_AXES)
    flat = values.reshape(-1, 128)
    copies = jnp.broadcast_to(flat[None], (count,) + flat.shape)
    return jnp.sum(lax.all_to_all(copies, MESH_AXES, 0, 0, tiled=True), axis=0).reshape(values.shape)


def gather_cycles(partials, band_count):
    cycle_total, columns = partials.shape
    group_count = lax.axis_size("mgrp")
    own = cycle_total // (band_count * group_count)
    pieces = partials.reshape(band_count, group_count, own, columns).transpose(1, 0, 2, 3)
    pieces = pieces.reshape(group_count * band_count, own, columns)
    received = lax.all_to_all(pieces, MESH_AXES, 0, 0, tiled=True)
    received = received.reshape(group_count, band_count, own, columns)
    return jnp.sum(received, axis=1).transpose(1, 0, 2)


def spread_cycles(backward, band_count):
    group_count, own, columns = backward.shape
    pieces = jnp.broadcast_to(
        backward[:, None], (group_count, band_count, own, columns)
    ).reshape(group_count * band_count, own, columns)
    received = lax.all_to_all(pieces, MESH_AXES, 0, 0, tiled=True)
    received = received.reshape(group_count, band_count, own, columns).transpose(1, 0, 2, 3)
    return received.reshape(band_count * group_count * own, columns)


def cycle_tables(m_values, lengths, pixels):
    high_count = pixels // 128
    coarse = jnp.arange(high_count, dtype=jnp.int32) * 128
    fine = jnp.arange(128, dtype=jnp.int32)
    cycle_size = lengths[:, None, None].astype(jnp.float32)
    phase_high = m_values[None, :, None] * coarse[None, None, :] % lengths[:, None, None]
    phase_low = m_values[None, :, None] * fine[None, None, :] % lengths[:, None, None]
    angle_high = 2.0 * math.pi * phase_high.astype(jnp.float32) / cycle_size
    angle_low = 2.0 * math.pi * phase_low.astype(jnp.float32) / cycle_size
    cos_high = jnp.cos(angle_high)[:, :, :, None]
    sin_high = jnp.sin(angle_high)[:, :, :, None]
    cos_low = jnp.cos(angle_low)[:, :, None, :]
    sin_low = jnp.sin(angle_low)[:, :, None, :]
    cycle_count = lengths.shape[0]
    mode_count = m_values.shape[0]
    cos_full = (cos_high * cos_low - sin_high * sin_low).reshape(cycle_count, mode_count, pixels)
    sin_full = (sin_high * cos_low + cos_high * sin_low).reshape(cycle_count, mode_count, pixels)
    column = jnp.arange(pixels, dtype=jnp.int32)
    factor = jnp.where(m_values == 0, 1.0, 2.0).astype(jnp.float32)[None, :, None]
    inside = (column[None, None, :] < lengths[:, None, None]).astype(jnp.float32)
    cosine = factor * cos_full * inside
    sine_part = -factor * sin_full * inside
    return jnp.stack([cosine, sine_part], axis=1).astype(jnp.bfloat16)


def pair_table(noise_mats):
    kinds = noise_mats.shape[0]
    first = jnp.broadcast_to(noise_mats[:, None], (kinds, kinds, BLK, BLK))
    second = jnp.broadcast_to(noise_mats[None, :], (kinds, kinds, BLK, BLK))
    empty = jnp.zeros((kinds, kinds, BLK, BLK), noise_mats.dtype)
    upper = jnp.concatenate([first, empty], axis=3)
    lower = jnp.concatenate([empty, second], axis=3)
    return jnp.concatenate([upper, lower], axis=2).reshape(kinds * kinds, 2 * BLK, 2 * BLK)


def cycle_segment(coeffs, lengths, indices, m_values, pairs, kinds, weight):
    cycle_count, mode_count, columns = coeffs.shape
    map_count = columns // 2
    tables = cycle_tables(m_values, lengths, RLEN)
    split_coeffs = coeffs.reshape(cycle_count, mode_count, 2, map_count)
    sky_map = jnp.einsum(
        "rmcb,rcmk->rbk", split_coeffs, tables, preferred_element_type=jnp.float32
    ).astype(jnp.bfloat16)
    pair_count = RLEN // (2 * BLK)
    kind_pairs = indices.reshape(cycle_count, pair_count, 2)
    pair_index = kind_pairs[:, :, 0] * kinds + kind_pairs[:, :, 1]
    matrices = pairs.reshape(kinds * kinds, 4 * BLK * BLK)[pair_index].reshape(
        cycle_count, pair_count, 2 * BLK, 2 * BLK
    )
    blocked = sky_map.reshape(cycle_count, map_count, pair_count, 2 * BLK)
    noisy_map = weight * jnp.einsum(
        "rbqj,rqij->rbqi", blocked, matrices, preferred_element_type=jnp.float32
    )
    noisy_map = noisy_map.reshape(cycle_count, map_count, RLEN).astype(jnp.bfloat16)
    backward = jnp.einsum("rbk,rcmk->rmcb", noisy_map, tables, preferred_element_type=jnp.float32)
    return backward.reshape(cycle_count, mode_count, columns).astype(jnp.bfloat16)


def noise_kernel(index_ref, length_ref, coeff_ref, table_ref, pair_ref, back_ref, noisy_ref, sums_ref):
    cycle = pl.program_id(0)
    wide = noisy_ref.shape[1]
    pair_width = 2 * BLK
    coeff = coeff_ref[0]
    side = int(round(pair_ref.shape[0] ** 0.5))

    def chunk(start, span, total):
        table = table_ref[0, :, pl.ds(start, span)]
        sky = jnp.dot(coeff, table, preferred_element_type=jnp.float32).astype(jnp.bfloat16)
        for inner in range(span // pair_width):
            block = (start + inner * pair_width) // BLK
            pick = index_ref[cycle, block] * side + index_ref[cycle, block + 1]
            noisy = jnp.dot(
                sky[:, inner * pair_width:(inner + 1) * pair_width],
                pair_ref[pick],
                preferred_element_type=jnp.float32,
            )
            noisy_ref[:, inner * pair_width:(inner + 1) * pair_width] = noisy.astype(jnp.bfloat16)
        return total + lax.dot_general(
            table, noisy_ref[:, :span], (((1,), (1,)), ((), ())), preferred_element_type=jnp.float32
        )

    length = length_ref[cycle]
    mid = wide // 2
    narrow = wide // 4
    full = length // wide
    rest = length - full * wide
    wide_count = full + (rest > mid + narrow).astype(jnp.int32)
    mid_count = ((rest > narrow) & (rest <= mid + narrow)).astype(jnp.int32)
    narrow_count = (((rest > 0) & (rest <= narrow)) | ((rest > mid) & (rest <= mid + narrow))).astype(jnp.int32)
    total = lax.fori_loop(
        0,
        wide_count,
        lambda step, acc: chunk(pl.multiple_of(step * wide, wide), wide, acc),
        jnp.zeros((table_ref.shape[1], noisy_ref.shape[0]), jnp.float32),
    )
    total = lax.fori_loop(
        0,
        mid_count,
        lambda step, acc: chunk(pl.multiple_of(full * wide, wide), mid, acc),
        total,
    )
    total = lax.fori_loop(
        0,
        narrow_count,
        lambda step, acc: chunk(pl.multiple_of(full * wide + mid_count * mid, mid), narrow, acc),
        total,
    )
    modes = back_ref.shape[0]
    maps = noisy_ref.shape[0]
    for part in range(table_ref.shape[1] // modes):
        for mode in range(modes):
            row = part * modes + mode
            sums_ref[mode, pl.ds(cycle, 1), part * maps:(part + 1) * maps] = total[row:row + 1, :]

    @pl.when(cycle == pl.num_programs(0) - 1)
    def _():
        back_ref[...] = sums_ref[...].astype(back_ref.dtype)


def cycle_transform(coeffs, lengths, indices, m_values, noise_mats, weight):
    cycle_count, mode_count, columns = coeffs.shape
    map_count = columns // 2
    kinds = noise_mats.shape[0]
    tables = cycle_tables(m_values, lengths, RLEN).reshape(cycle_count, 2 * mode_count, RLEN)
    coeff_t = (
        coeffs.reshape(cycle_count, mode_count, 2, map_count)
        .transpose(0, 3, 2, 1)
        .reshape(cycle_count, map_count, 2 * mode_count)
    )
    pairs_t = jnp.swapaxes(pair_table(noise_mats), 1, 2) * jnp.asarray(weight, jnp.bfloat16)
    grid_spec = pltpu.PrefetchScalarGridSpec(
        num_scalar_prefetch=2,
        grid=(cycle_count,),
        in_specs=[
            pl.BlockSpec((1, map_count, 2 * mode_count), lambda r, idx, n: (r, 0, 0)),
            pl.BlockSpec((1, 2 * mode_count, RLEN), lambda r, idx, n: (r, 0, 0)),
            pl.BlockSpec(pairs_t.shape, lambda r, idx, n: (0, 0, 0)),
        ],
        out_specs=pl.BlockSpec((mode_count, cycle_count, columns), lambda r, idx, n: (0, 0, 0)),
        scratch_shapes=[
            pltpu.VMEM((map_count, 8192), jnp.bfloat16),
            pltpu.VMEM((mode_count, cycle_count, columns), jnp.float32),
        ],
    )
    back = pl.pallas_call(
        noise_kernel,
        grid_spec=grid_spec,
        out_shape=jax.ShapeDtypeStruct((mode_count, cycle_count, columns), jnp.bfloat16),
    )(indices, lengths, coeff_t, tables, pairs_t)
    return back


def shards(
    solution,
    residual,
    direction,
    legendre,
    prior_inv,
    noise_mats,
    noise_index,
    cycle_lengths,
    m_values,
    cut_pattern,
):
    band_count = lax.axis_size("band")
    mode_local, cycle_total, l_local = legendre.shape
    map_count = direction.shape[1]
    columns = 2 * map_count
    band_rows = cycle_total // band_count
    weight = L / (cycle_total * RLEN)

    def row_mask(first_row, row_count):
        block_flags = lax.dynamic_slice_in_dim(cut_pattern, first_row // RB, row_count // RB, 1)
        return jnp.repeat(block_flags, RB, axis=1).T

    section = legendre
    products = jnp.einsum(
        "mrl,nml->rmn",
        section,
        direction.reshape(columns, mode_local, l_local),
        precision=lax.Precision.DEFAULT,
        preferred_element_type=jnp.float32,
    )
    masked_products = products * row_mask(jnp.int32(0), cycle_total).astype(jnp.float32)[:, :, None]
    coeffs = gather_cycles(masked_products.reshape(cycle_total, columns), band_count).astype(jnp.bfloat16)
    cycle_local = coeffs.shape[0]
    mode_total = coeffs.shape[1]
    outputs = cycle_transform(coeffs, cycle_lengths, noise_index, m_values, noise_mats, weight)
    returned = spread_cycles(outputs, band_count)
    masked = returned * row_mask(jnp.int32(0), cycle_total).astype(jnp.bfloat16)
    image_data = lax.optimization_barrier(
        jnp.einsum("rl,rn->nl", legendre[0], masked, preferred_element_type=jnp.float32)
    )
    image_data = image_data.reshape(2, map_count, mode_local, l_local)
    image_field = prior_inv[None, None, None, :] * direction + image_data
    norm_now, curvature, cross, image_norm = total_over_mesh(
        jnp.stack(
            [
                jnp.sum(residual * residual, axis=(0, 2, 3)),
                jnp.sum(direction * image_field, axis=(0, 2, 3)),
                jnp.sum(residual * image_field, axis=(0, 2, 3)),
                jnp.sum(image_field * image_field, axis=(0, 2, 3)),
            ]
        )
    )
    step_size = norm_now / curvature
    new_residual = residual - step_size[None, :, None, None] * image_field
    norm_next = norm_now - 2.0 * step_size * cross + step_size * step_size * image_norm
    growth = norm_next / norm_now
    new_solution = solution + step_size[None, :, None, None] * direction
    new_direction = new_residual + growth[None, :, None, None] * direction
    return (new_solution, new_residual, new_direction)


def solution(mesh):
    in_specs = (
        P(None, None, "mgrp", "band"),
        P(None, None, "mgrp", "band"),
        P(None, None, "mgrp", "band"),
        P("mgrp", None, "band"),
        P("band"),
        P(),
        P(("band", "mgrp"), None),
        P(("band", "mgrp")),
        P(),
        P("mgrp", None),
    )
    out_specs = (
        P(None, None, "mgrp", "band"),
        P(None, None, "mgrp", "band"),
        P(None, None, "mgrp", "band"),
    )
    return jax.shard_map(shards, mesh=mesh, in_specs=in_specs, out_specs=out_specs, check_vma=False)
```

```python
import functools
import math

import jax
import jax.numpy as jnp
from jax import lax
from jax.experimental import pallas as pl
from jax.experimental.pallas import tpu as pltpu
from jax.sharding import PartitionSpec as P

L = 8192
RLEN = 16384
BLK = 64
RB = 64


MESH_AXES = ("mgrp", "band")


def total_over_mesh(values):
    count = lax.axis_size(MESH_AXES)
    flat = values.reshape(-1, 128)
    copies = jnp.broadcast_to(flat[None], (count,) + flat.shape)
    return jnp.sum(lax.all_to_all(copies, MESH_AXES, 0, 0, tiled=True), axis=0).reshape(values.shape)


def gather_cycles(partials, band_count):
    cycle_total, columns = partials.shape
    group_count = lax.axis_size("mgrp")
    own = cycle_total // (band_count * group_count)
    pieces = partials.reshape(band_count, group_count, own, columns).transpose(1, 0, 2, 3)
    pieces = pieces.reshape(group_count * band_count, own, columns)
    received = lax.all_to_all(pieces, MESH_AXES, 0, 0, tiled=True)
    received = received.reshape(group_count, band_count, own, columns)
    return jnp.sum(received, axis=1).transpose(1, 0, 2)


def spread_cycles(backward, band_count):
    group_count, own, columns = backward.shape
    pieces = jnp.broadcast_to(
        backward[:, None], (group_count, band_count, own, columns)
    ).reshape(group_count * band_count, own, columns)
    received = lax.all_to_all(pieces, MESH_AXES, 0, 0, tiled=True)
    received = received.reshape(group_count, band_count, own, columns).transpose(1, 0, 2, 3)
    return received.reshape(band_count * group_count * own, columns)


def cycle_tables(m_values, lengths, pixels):
    high_count = pixels // 128
    coarse = jnp.arange(high_count, dtype=jnp.int32) * 128
    fine = jnp.arange(128, dtype=jnp.int32)
    cycle_size = lengths[:, None, None].astype(jnp.float32)
    phase_high = m_values[None, :, None] * coarse[None, None, :] % lengths[:, None, None]
    phase_low = m_values[None, :, None] * fine[None, None, :] % lengths[:, None, None]
    angle_high = 2.0 * math.pi * phase_high.astype(jnp.float32) / cycle_size
    angle_low = 2.0 * math.pi * phase_low.astype(jnp.float32) / cycle_size
    cos_high = jnp.cos(angle_high)[:, :, :, None]
    sin_high = jnp.sin(angle_high)[:, :, :, None]
    cos_low = jnp.cos(angle_low)[:, :, None, :]
    sin_low = jnp.sin(angle_low)[:, :, None, :]
    cycle_count = lengths.shape[0]
    mode_count = m_values.shape[0]
    cos_full = (cos_high * cos_low - sin_high * sin_low).reshape(cycle_count, mode_count, pixels)
    sin_full = (sin_high * cos_low + cos_high * sin_low).reshape(cycle_count, mode_count, pixels)
    column = jnp.arange(pixels, dtype=jnp.int32)
    factor = jnp.where(m_values == 0, 1.0, 2.0).astype(jnp.float32)[None, :, None]
    inside = (column[None, None, :] < lengths[:, None, None]).astype(jnp.float32)
    cosine = factor * cos_full * inside
    sine_part = -factor * sin_full * inside
    return jnp.stack([cosine, sine_part], axis=1).astype(jnp.bfloat16)


def pair_table(noise_mats):
    kinds = noise_mats.shape[0]
    first = jnp.broadcast_to(noise_mats[:, None], (kinds, kinds, BLK, BLK))
    second = jnp.broadcast_to(noise_mats[None, :], (kinds, kinds, BLK, BLK))
    empty = jnp.zeros((kinds, kinds, BLK, BLK), noise_mats.dtype)
    upper = jnp.concatenate([first, empty], axis=3)
    lower = jnp.concatenate([empty, second], axis=3)
    return jnp.concatenate([upper, lower], axis=2).reshape(kinds * kinds, 2 * BLK, 2 * BLK)


def cycle_segment(coeffs, lengths, indices, m_values, pairs, kinds, weight):
    cycle_count, mode_count, columns = coeffs.shape
    map_count = columns // 2
    tables = cycle_tables(m_values, lengths, RLEN)
    split_coeffs = coeffs.reshape(cycle_count, mode_count, 2, map_count)
    sky_map = jnp.einsum(
        "rmcb,rcmk->rbk", split_coeffs, tables, preferred_element_type=jnp.float32
    ).astype(jnp.bfloat16)
    pair_count = RLEN // (2 * BLK)
    kind_pairs = indices.reshape(cycle_count, pair_count, 2)
    pair_index = kind_pairs[:, :, 0] * kinds + kind_pairs[:, :, 1]
    matrices = pairs.reshape(kinds * kinds, 4 * BLK * BLK)[pair_index].reshape(
        cycle_count, pair_count, 2 * BLK, 2 * BLK
    )
    blocked = sky_map.reshape(cycle_count, map_count, pair_count, 2 * BLK)
    noisy_map = weight * jnp.einsum(
        "rbqj,rqij->rbqi", blocked, matrices, preferred_element_type=jnp.float32
    )
    noisy_map = noisy_map.reshape(cycle_count, map_count, RLEN).astype(jnp.bfloat16)
    backward = jnp.einsum("rbk,rcmk->rmcb", noisy_map, tables, preferred_element_type=jnp.float32)
    return backward.reshape(cycle_count, mode_count, columns).astype(jnp.bfloat16)


def noise_kernel(index_ref, length_ref, coeff_ref, table_ref, pair_ref, back_ref, noisy_ref, sums_ref):
    cycle = pl.program_id(0)
    wide = noisy_ref.shape[1]
    pair_width = 2 * BLK
    coeff = coeff_ref[0]
    side = int(round(pair_ref.shape[0] ** 0.5))

    def chunk(start, span, total):
        table = table_ref[0, :, pl.ds(start, span)]
        sky = jnp.dot(coeff, table, preferred_element_type=jnp.float32).astype(jnp.bfloat16)
        for inner in range(span // pair_width):
            block = (start + inner * pair_width) // BLK
            pick = index_ref[cycle, block] * side + index_ref[cycle, block + 1]
            noisy = jnp.dot(
                sky[:, inner * pair_width:(inner + 1) * pair_width],
                pair_ref[pick],
                preferred_element_type=jnp.float32,
            )
            noisy_ref[:, inner * pair_width:(inner + 1) * pair_width] = noisy.astype(jnp.bfloat16)
        return total + lax.dot_general(
            table, noisy_ref[:, :span], (((1,), (1,)), ((), ())), preferred_element_type=jnp.float32
        )

    length = length_ref[cycle]
    mid = wide // 2
    narrow = wide // 4
    full = length // wide
    rest = length - full * wide
    wide_count = full + (rest > mid + narrow).astype(jnp.int32)
    mid_count = ((rest > narrow) & (rest <= mid + narrow)).astype(jnp.int32)
    left = jnp.where(rest > mid + narrow, 0, rest - mid_count * mid)
    narrow_count = (left > narrow // 2).astype(jnp.int32)
    tiny_count = ((left > 0) & (left <= narrow // 2)).astype(jnp.int32)
    total = lax.fori_loop(
        0,
        wide_count,
        lambda step, acc: chunk(pl.multiple_of(step * wide, wide), wide, acc),
        jnp.zeros((table_ref.shape[1], noisy_ref.shape[0]), jnp.float32),
    )
    total = lax.fori_loop(
        0,
        mid_count,
        lambda step, acc: chunk(pl.multiple_of(full * wide, wide), mid, acc),
        total,
    )
    total = lax.fori_loop(
        0,
        narrow_count,
        lambda step, acc: chunk(pl.multiple_of(full * wide + mid_count * mid, mid), narrow, acc),
        total,
    )
    total = lax.fori_loop(
        0,
        tiny_count,
        lambda step, acc: chunk(pl.multiple_of(full * wide + mid_count * mid, mid), narrow // 2, acc),
        total,
    )
    modes = back_ref.shape[0]
    maps = noisy_ref.shape[0]
    for part in range(table_ref.shape[1] // modes):
        for mode in range(modes):
            row = part * modes + mode
            sums_ref[mode, pl.ds(cycle, 1), part * maps:(part + 1) * maps] = total[row:row + 1, :]

    @pl.when(cycle == pl.num_programs(0) - 1)
    def _():
        back_ref[...] = sums_ref[...].astype(back_ref.dtype)


def cycle_transform(coeffs, lengths, indices, m_values, noise_mats, weight):
    cycle_count, mode_count, columns = coeffs.shape
    map_count = columns // 2
    kinds = noise_mats.shape[0]
    tables = cycle_tables(m_values, lengths, RLEN).reshape(cycle_count, 2 * mode_count, RLEN)
    coeff_t = (
        coeffs.reshape(cycle_count, mode_count, 2, map_count)
        .transpose(0, 3, 2, 1)
        .reshape(cycle_count, map_count, 2 * mode_count)
    )
    pairs_t = jnp.swapaxes(pair_table(noise_mats), 1, 2) * jnp.asarray(weight, jnp.bfloat16)
    grid_spec = pltpu.PrefetchScalarGridSpec(
        num_scalar_prefetch=2,
        grid=(cycle_count,),
        in_specs=[
            pl.BlockSpec((1, map_count, 2 * mode_count), lambda r, idx, n: (r, 0, 0)),
            pl.BlockSpec((1, 2 * mode_count, RLEN), lambda r, idx, n: (r, 0, 0)),
            pl.BlockSpec(pairs_t.shape, lambda r, idx, n: (0, 0, 0)),
        ],
        out_specs=pl.BlockSpec((mode_count, cycle_count, columns), lambda r, idx, n: (0, 0, 0)),
        scratch_shapes=[
            pltpu.VMEM((map_count, 8192), jnp.bfloat16),
            pltpu.VMEM((mode_count, cycle_count, columns), jnp.float32),
        ],
    )
    back = pl.pallas_call(
        noise_kernel,
        grid_spec=grid_spec,
        out_shape=jax.ShapeDtypeStruct((mode_count, cycle_count, columns), jnp.bfloat16),
    )(indices, lengths, coeff_t, tables, pairs_t)
    return back


def shards(
    solution,
    residual,
    direction,
    legendre,
    prior_inv,
    noise_mats,
    noise_index,
    cycle_lengths,
    m_values,
    cut_pattern,
):
    band_count = lax.axis_size("band")
    mode_local, cycle_total, l_local = legendre.shape
    map_count = direction.shape[1]
    columns = 2 * map_count
    band_rows = cycle_total // band_count
    weight = L / (cycle_total * RLEN)

    def row_mask(first_row, row_count):
        block_flags = lax.dynamic_slice_in_dim(cut_pattern, first_row // RB, row_count // RB, 1)
        return jnp.repeat(block_flags, RB, axis=1).T

    section = legendre
    products = jnp.einsum(
        "mrl,nml->rmn",
        section,
        direction.reshape(columns, mode_local, l_local),
        precision=lax.Precision.DEFAULT,
        preferred_element_type=jnp.float32,
    )
    masked_products = products * row_mask(jnp.int32(0), cycle_total).astype(jnp.float32)[:, :, None]
    coeffs = gather_cycles(masked_products.reshape(cycle_total, columns), band_count).astype(jnp.bfloat16)
    cycle_local = coeffs.shape[0]
    mode_total = coeffs.shape[1]
    outputs = cycle_transform(coeffs, cycle_lengths, noise_index, m_values, noise_mats, weight)
    returned = spread_cycles(outputs, band_count)
    masked = returned * row_mask(jnp.int32(0), cycle_total).astype(jnp.bfloat16)
    image_data = lax.optimization_barrier(
        jnp.einsum("rl,rn->nl", legendre[0], masked, preferred_element_type=jnp.float32)
    )
    image_data = image_data.reshape(2, map_count, mode_local, l_local)
    image_field = prior_inv[None, None, None, :] * direction + image_data
    norm_now, curvature, cross, image_norm = total_over_mesh(
        jnp.stack(
            [
                jnp.sum(residual * residual, axis=(0, 2, 3)),
                jnp.sum(direction * image_field, axis=(0, 2, 3)),
                jnp.sum(residual * image_field, axis=(0, 2, 3)),
                jnp.sum(image_field * image_field, axis=(0, 2, 3)),
            ]
        )
    )
    step_size = norm_now / curvature
    new_residual = residual - step_size[None, :, None, None] * image_field
    norm_next = norm_now - 2.0 * step_size * cross + step_size * step_size * image_norm
    growth = norm_next / norm_now
    new_solution = solution + step_size[None, :, None, None] * direction
    new_direction = new_residual + growth[None, :, None, None] * direction
    return (new_solution, new_residual, new_direction)


def solution(mesh):
    in_specs = (
        P(None, None, "mgrp", "band"),
        P(None, None, "mgrp", "band"),
        P(None, None, "mgrp", "band"),
        P("mgrp", None, "band"),
        P("band"),
        P(),
        P(("band", "mgrp"), None),
        P(("band", "mgrp")),
        P(),
        P("mgrp", None),
    )
    out_specs = (
        P(None, None, "mgrp", "band"),
        P(None, None, "mgrp", "band"),
        P(None, None, "mgrp", "band"),
    )
    return jax.shard_map(shards, mesh=mesh, in_specs=in_specs, out_specs=out_specs, check_vma=False)
```
